32 devices in a mesh: dp: 4 (over y, x), fsdp: 8 (over z, core).
Axes of the slice: x: 2, y: 2, z: 4, core: 2. Of those that a mesh axis runs over, the one named last changes fastest.
Arguments:
- frames: bfloat16 [256, 1024, 512], P(('dp', 'fsdp')), may hold values from -6 to 6
- counts: int32 [256], P(('dp', 'fsdp')), may hold values from 64 to 1024, as said below
- cotangent: bfloat16 [256, 1024, 512], P(('dp', 'fsdp')), may hold values from -6 to 6
- master: float32 [1581056], P(('dp', 'fsdp'))
- momentum: float32 [1581056], P(('dp', 'fsdp')), may hold values from -48 to 48
- average: float32 [1581056], P(('dp', 'fsdp')), may hold values from -0.75 to 0.75
- disc_grads: float32 [1048576], P(('dp', 'fsdp'))
Outputs:
- block_out: bfloat16 [256, 1024, 512], P(('dp', 'fsdp'))
- input_grad: float32 [256, 1024, 512], P(('dp', 'fsdp'))
- grad_norm: float32 [], replicated
- new_master: float32 [1581056], P(('dp', 'fsdp'))
- new_momentum: float32 [1581056], P(('dp', 'fsdp'))
- new_average: float32 [1581056], P(('dp', 'fsdp'))
- master_copy: bfloat16 [1581056], P(('dp', 'fsdp'))
- average_copy: bfloat16 [1581056], P(('dp', 'fsdp'))
The draws below stay inside these ranges and needn't reach their ends.
Inputs may be any that keep to these rules, and one draw needn't show every extreme that they name: `counts`: clip 0 has 1024 true frames and clip 1 has 64.
All inputs are finite; a program needn't handle non-finite values.
Results may differ from the reference program's by a relative error of at most 0.0014.
The reference program's roundings to bfloat16 on the way count: a program that leaves them out, or rounds other values in their place, can miss the bound.
Values may be sent and summed in bfloat16 or wider, within the bound.
No kernel may reach another device: no remote copies, remote signals or barrier semaphores. Data moves between devices by JAX's collectives and lax.ppermute only.
A program may use at most 320 MiB of HBM per device.

```python
import jax
import jax.numpy as jnp
from jax import lax

D = 512
FF = 1536
KERNEL = 7
CLIP = 1024
MIN_FRAMES = 64
CLIPS_DEV = 8
DISC_DEV = 32768
BATCH = 256
TOTAL = 262144
USED = 1580544
FLAT = 1581056
DISC = 1048576


def draw_counts(key, part):
    values = jax.random.randint(key, (BATCH,), MIN_FRAMES, CLIP + 1).astype(jnp.int32)
    places = jnp.arange(BATCH, dtype=jnp.int32)
    values = jnp.where(places == 1, MIN_FRAMES, values)
    return jnp.where(places == 0, CLIP, values).astype(jnp.int32)


def draw_master(key, part):
    places = jnp.arange(FLAT, dtype=jnp.int32)
    rough = jax.random.normal(key, (FLAT,), jnp.float32)
    even = jax.random.uniform(jax.random.fold_in(key, 11), (FLAT,), jnp.float32)
    end_one = D * FF
    end_two = 2 * D * FF
    end_conv = end_two + KERNEL * D
    end_bias = end_conv + D
    end_gain = end_bias + D
    end_shift = end_gain + D
    end_btwo = end_shift + D
    end_gamma = end_btwo + D
    end_bone = end_gamma + FF
    values = rough * 0.02
    values = jnp.where(places < end_bone, rough * 0.3, values)
    values = jnp.where(places < end_gamma, 0.5 + even, values)
    values = jnp.where(places < end_btwo, rough * 0.3, values)
    values = jnp.where(places < end_shift, rough * 0.3, values)
    values = jnp.where(places < end_gain, 0.7 + 0.6 * even, values)
    values = jnp.where(places < end_bias, rough * 0.3, values)
    values = jnp.where(places < end_conv, rough * (1.0 / KERNEL) ** 0.5, values)
    values = jnp.where(places < end_two, rough * (1.0 / FF) ** 0.5, values)
    values = jnp.where(places < end_one, rough * (1.0 / D) ** 0.5, values)
    return values.astype(jnp.float32)


def draw_disc_grads(key, part):
    places = jnp.arange(DISC, dtype=jnp.int32).astype(jnp.float32) / DISC
    level = 300.0 * (CLIPS_DEV * CLIP / DISC_DEV) ** 0.5
    rough = jax.random.normal(key, (DISC,), jnp.float32)
    rise = 0.6 + 1.2 * places
    return (rough * rise * level).astype(jnp.float32)


def steps_of(rng, shape, shards, smallest, high):
    factor_of = 1.0
    for dim, blocks in shards:
        draws = jax.random.uniform(jax.random.fold_in(jax.random.fold_in(rng, 6), dim), (blocks,), jnp.float32, smallest / len(shards), high / len(shards))
        factor_of = factor_of * jnp.repeat(jnp.exp(draws), shape[dim] // blocks).reshape((-1,) + (1,) * (len(shape) - 1 - dim))
    return factor_of


def centred(own_key, dims, scale, reach, shards=(), kind=jnp.bfloat16):
    loudness = steps_of(own_key, dims, shards, -0.22, 0.18) if shards else 1.0
    array = jax.random.normal(own_key, dims, jnp.float32) * scale * loudness
    return jnp.minimum(jnp.maximum(array, -reach), reach).astype(kind)


def setup_inputs(seed: int = 0) -> dict:
    splits = jax.random.split(jax.random.key(seed), 8)
    frames = centred(splits[0], (BATCH, CLIP, D), 1.0, 6.0, ((0, 32),))
    counts = draw_counts(jax.random.fold_in(splits[7], 71), 0)
    cotangent = centred(splits[2], (BATCH, CLIP, D), 1.0, 6.0, ((0, 32),))
    master = draw_master(jax.random.fold_in(splits[7], 71), 0)
    momentum = centred(splits[4], (FLAT,), (20.0 * (TOTAL / FLAT) ** 0.5), 48.0, ((0, 32),), jnp.float32)
    average = centred(splits[5], (FLAT,), 0.05, 0.75, ((0, 32),), jnp.float32)
    disc_grads = draw_disc_grads(jax.random.fold_in(splits[7], 71), 0)
    return dict(frames=frames, counts=counts, cotangent=cotangent, master=master, momentum=momentum, average=average, disc_grads=disc_grads)


@jax.custom_vjp
def low(v):
    return lax.optimization_barrier(v.astype(jnp.bfloat16)).astype(jnp.float32)

@jax.custom_vjp
def low_back(v):
    return v

def low_keep(v):
    return (low(v), None)

def low_pass(kept, grad):
    return (grad,)

def back_keep(v):
    return (v, None)

def back_low(kept, grad):
    return (low(grad),)
low.defvjp(low_keep, low_pass)
low_back.defvjp(back_keep, back_low)

def unpack(packed):
    shapes = [(D, FF), (FF, D), (KERNEL, D), (D,), (D,), (D,), (D,), (D,), (FF,)]
    pieces = []
    start_at = 0
    for shape in shapes:
        entries = 1
        for extent in shape:
            entries = entries * extent
        pieces.append(packed[start_at:start_at + entries].reshape(shape))
        start_at = start_at + entries
    return tuple(pieces)

def conv_norm(masked, conv_w, conv_b, ln_g, ln_b):
    length = masked.shape[1]
    padded = jnp.pad(masked, ((0, 0), (KERNEL // 2, KERNEL // 2), (0, 0)))
    summed = conv_b + conv_w[0] * padded[:, 0:length, :]
    for offset in range(1, KERNEL):
        summed = summed + conv_w[offset] * padded[:, offset:offset + length, :]
    centre = lax.optimization_barrier(jnp.mean(summed, axis=-1, keepdims=True))
    shifted = summed - centre
    spread = lax.optimization_barrier(jnp.mean(shifted * shifted, axis=-1, keepdims=True))
    return shifted * lax.rsqrt(spread + 1e-06) * ln_g + ln_b

def forward(inputs, params, mask):
    w_one, w_two, conv_w, conv_b, ln_g, ln_b, b_two, gamma, b_one = params
    normed = conv_norm(inputs * mask, conv_w, conv_b, ln_g, ln_b)
    act = low(normed)
    hidden = low_back(jnp.einsum('gtd,df->gtf', act, w_one, precision=lax.Precision.HIGHEST) + b_one)
    gelled = low(jax.nn.gelu(hidden, approximate=False))
    branch = low_back(jnp.einsum('gtf,fd->gtd', gelled, w_two, precision=lax.Precision.HIGHEST) + b_two)
    return mask * (inputs + gamma * branch)

def reference(frames, counts, cotangent, master, momentum, average, disc_grads):
    group_clips = 4
    params = unpack(master.astype(jnp.bfloat16).astype(jnp.float32))
    groups = BATCH // group_clips
    frame_groups = frames.reshape(groups, group_clips, CLIP, D)
    count_groups = counts.reshape(groups, group_clips)
    cot_groups = cotangent.reshape(groups, group_clips, CLIP, D)

    def one_group(carry, inputs):
        frame_block, count_block, cot_block = inputs
        slots = lax.broadcasted_iota(jnp.int32, (group_clips, CLIP), 1)
        mask = (slots < count_block[:, None]).astype(jnp.float32)[:, :, None]
        floats = frame_block.astype(jnp.float32)
        result, pullback = jax.vjp(lambda xin, prm: forward(xin, prm, mask), floats, params)
        d_input, d_params = pullback(cot_block.astype(jnp.float32))
        carry = tuple((acc + part for acc, part in zip(carry, d_params)))
        return (carry, (result.astype(jnp.bfloat16), d_input))
    zeros_init = tuple((jnp.zeros_like(item) for item in params))
    totals, (outs, grads_in) = lax.scan(one_group, zeros_init, (frame_groups, count_groups, cot_groups))
    grad = jnp.concatenate([item.reshape(-1) for item in totals] + [jnp.zeros((FLAT - USED,), jnp.float32)])
    grad_norm = jnp.sqrt(jnp.sum(grad * grad) + jnp.sum(disc_grads * disc_grads))
    total_frames = jnp.float32(TOTAL)
    clipped = grad * jnp.minimum(1.0, 20.0 * jnp.sqrt(total_frames) / (grad_norm + 1e-06))
    new_momentum = 0.9 * momentum + clipped
    new_master = master - (clipped + 0.9 * new_momentum) / jnp.sqrt(total_frames)
    new_average = 0.99 * average + 0.01 * new_master
    return (outs.reshape(BATCH, CLIP, D), grads_in.reshape(BATCH, CLIP, D), grad_norm, new_master, new_momentum, new_average, new_master.astype(jnp.bfloat16), new_average.astype(jnp.bfloat16))
```

```python
import functools
import math

import jax
import jax.numpy as jnp
from jax import lax
from jax.experimental import pallas as pl
from jax.experimental.pallas import tpu as pltpu
from jax.sharding import PartitionSpec as P

F32 = jnp.float32
BF16 = jnp.bfloat16
TAPS = 7
HALF = TAPS // 2
PAD = 8


def tdot(x, y):
    return lax.dot_general(x, y, (((0,), (0,)), ((), ())), preferred_element_type=F32)


def ntdot(x, y):
    return lax.dot_general(x, y, (((1,), (1,)), ((), ())), preferred_element_type=F32)


def block_kernel(length, width, hidden, rows):
    nblk = length // rows
    inv_w = 1.0 / width
    sqrt_half = math.sqrt(0.5)
    inv_sqrt_2pi = 1.0 / math.sqrt(2.0 * math.pi)

    def kernel(counts_ref, fr_ref, cot_ref, w1_ref, w2_ref, cw_ref, vec_ref, b1_ref,
               bo_ref, ig_ref, gw1_hbm, gw2_hbm, gcw_ref, gvec_ref, gb1_ref,
               xpad, xhat_s, rstd_s, a_s, da_s, dpad, gw1_s, gw2_s, sems):
        clip = pl.program_id(0)
        count = counts_ref[clip]

        @pl.when(clip == 0)
        def _init():
            gw1_s[...] = jnp.zeros_like(gw1_s)
            gw2_s[...] = jnp.zeros_like(gw2_s)
            gcw_ref[...] = jnp.zeros_like(gcw_ref)
            gvec_ref[...] = jnp.zeros_like(gvec_ref)
            gb1_ref[...] = jnp.zeros_like(gb1_ref)
            xpad[0:PAD, :] = jnp.zeros((PAD, width), F32)
            xpad[PAD + length:, :] = jnp.zeros((PAD, width), F32)
            dpad[0:PAD, :] = jnp.zeros((PAD, width), F32)
            dpad[PAD + length:, :] = jnp.zeros((PAD, width), F32)

        cw = cw_ref[...]
        conv_b = vec_ref[0:1, :]
        ln_g = vec_ref[1:2, :]
        ln_b = vec_ref[2:3, :]
        b_two = vec_ref[3:4, :]
        gamma = vec_ref[4:5, :]
        b_one = b1_ref[0:1, :]

        all_rows = lax.broadcasted_iota(jnp.int32, (length, 1), 0)
        xpad[PAD:PAD + length, :] = jnp.where(all_rows < count, fr_ref[0].astype(F32), 0.0)

        for b in range(nblk):
            r0 = b * rows

            @pl.when(r0 < count)
            def _fwd_block():
                base = PAD + r0 - HALF
                conv = conv_b + cw[0:1, :] * xpad[base:base + rows, :]
                for k in range(1, TAPS):
                    conv = conv + cw[k:k + 1, :] * xpad[base + k:base + k + rows, :]
                centre = jnp.sum(conv, axis=-1, keepdims=True) * inv_w
                shifted = conv - centre
                spread = jnp.sum(shifted * shifted, axis=-1, keepdims=True) * inv_w
                rstd = lax.rsqrt(spread + 1e-6)
                xhat = shifted * rstd
                xhat_s[r0:r0 + rows, :] = xhat
                rstd_s[r0:r0 + rows, :] = rstd
                a_s[r0:r0 + rows, :] = (xhat * ln_g + ln_b).astype(BF16)

        bo_ref[...] = jnp.zeros_like(bo_ref)

        def chunk(c, carry):
            g_gamma, g_b2, g_b1 = carry
            r0 = pl.multiple_of(c * rows, rows)
            a = a_s[pl.ds(r0, rows), :]
            h1 = jnp.dot(a, w1_ref[...], preferred_element_type=F32) + b_one
            cdf = 0.5 * (1.0 + lax.erf(h1 * sqrt_half))
            hh = (h1 * cdf).astype(BF16)
            z = jnp.dot(hh, w2_ref[...], preferred_element_type=F32) + b_two
            live = (r0 + lax.broadcasted_iota(jnp.int32, (rows, 1), 0)) < count
            xin = fr_ref[0, pl.ds(r0, rows), :].astype(F32)
            bo_ref[0, pl.ds(r0, rows), :] = jnp.where(live, xin + gamma * z, 0.0).astype(BF16)
            dout = jnp.where(live, cot_ref[0, pl.ds(r0, rows), :].astype(F32), 0.0)
            g_gamma = g_gamma + jnp.sum(dout * z, axis=0, keepdims=True)
            dz = (gamma * dout).astype(BF16)
            g_b2 = g_b2 + jnp.sum(dz.astype(F32), axis=0, keepdims=True)
            gw2_s[...] += tdot(hh, dz)
            dhh = ntdot(dz, w2_ref[...])
            slope = cdf + h1 * (jnp.exp(-0.5 * (h1 * h1)) * inv_sqrt_2pi)
            dh1 = (dhh * slope).astype(BF16)
            g_b1 = g_b1 + jnp.sum(dh1.astype(F32), axis=0, keepdims=True)
            gw1_s[...] += tdot(a, dh1)
            da_s[pl.ds(r0, rows), :] = ntdot(dh1, w1_ref[...])
            return g_gamma, g_b2, g_b1

        nact = (count + rows - 1) // rows
        zero_d = jnp.zeros((1, width), F32)
        g_gamma, g_b2, g_b1 = lax.fori_loop(
            0, nact, chunk, (zero_d, zero_d, jnp.zeros((1, hidden), F32)))

        def dxm_block(b):
            r0 = b * rows
            base = PAD + r0 + HALF
            dxm = cw[0:1, :] * dpad[base:base + rows, :]
            for k in range(1, TAPS):
                dxm = dxm + cw[k:k + 1, :] * dpad[base - k:base - k + rows, :]
            live = (r0 + lax.broadcasted_iota(jnp.int32, (rows, 1), 0)) < count
            cot = cot_ref[0, r0:r0 + rows, :].astype(F32)
            ig_ref[0, r0:r0 + rows, :] = jnp.where(live, cot + dxm, 0.0)

        sums = [zero_d] * (3 + TAPS)
        for b in range(nblk):
            r0 = b * rows

            def _bwd_block(r0=r0):
                live = (r0 + lax.broadcasted_iota(jnp.int32, (rows, 1), 0)) < count
                da = jnp.where(live, da_s[r0:r0 + rows, :], 0.0)
                xhat = xhat_s[r0:r0 + rows, :]
                rstd = rstd_s[r0:r0 + rows, :]
                dn = da * ln_g
                m1 = jnp.sum(dn, axis=-1, keepdims=True) * inv_w
                m2 = jnp.sum(dn * xhat, axis=-1, keepdims=True) * inv_w
                dconv = jnp.where(live, rstd * (dn - m1 - xhat * m2), 0.0)
                dpad[PAD + r0:PAD + r0 + rows, :] = dconv
                part = [jnp.sum(dconv, axis=0, keepdims=True),
                        jnp.sum(da * xhat, axis=0, keepdims=True),
                        jnp.sum(da, axis=0, keepdims=True)]
                base = PAD + r0 - HALF
                for k in range(TAPS):
                    part.append(jnp.sum(dconv * xpad[base + k:base + k + rows, :], axis=0, keepdims=True))
                return part

            active = r0 < count
            part = lax.cond(active, _bwd_block, lambda: [zero_d] * (3 + TAPS))

            @pl.when(jnp.logical_not(active))
            def _idle():
                dpad[PAD + r0:PAD + r0 + rows, :] = jnp.zeros((rows, width), F32)
                ig_ref[0, r0:r0 + rows, :] = jnp.zeros((rows, width), F32)

            sums = [s + p for s, p in zip(sums, part)]
            if b >= 1:
                @pl.when((b - 1) * rows < count)
                def _prev(b=b):
                    dxm_block(b - 1)

        @pl.when((nblk - 1) * rows < count)
        def _last():
            dxm_block(nblk - 1)

        gvec_ref[0:1, :] += sums[0]
        gvec_ref[1:2, :] += sums[1]
        gvec_ref[2:3, :] += sums[2]
        gvec_ref[3:4, :] += g_b2
        gvec_ref[4:5, :] += g_gamma
        for k in range(TAPS):
            gcw_ref[k:k + 1, :] += sums[3 + k]
        gb1_ref[0:1, :] += g_b1

        @pl.when(clip == pl.num_programs(0) - 1)
        def _flush():
            c1 = pltpu.make_async_copy(gw1_s, gw1_hbm, sems.at[0])
            c2 = pltpu.make_async_copy(gw2_s, gw2_hbm, sems.at[1])
            c1.start()
            c2.start()
            c1.wait()
            c2.wait()

    return kernel


def fused_block(frames, counts, cotangent, w1, w2, cw8, vec8, b1_8, rows=256):
    clips, length, width = frames.shape
    hidden = w1.shape[1]
    kernel = block_kernel(length, width, hidden, rows)
    clip_spec = pl.BlockSpec((1, length, width), lambda i, c: (i, 0, 0))
    fixed = lambda shape: pl.BlockSpec(shape, lambda i, c: (0, 0))
    grid_spec = pltpu.PrefetchScalarGridSpec(
        num_scalar_prefetch=1,
        grid=(clips,),
        in_specs=[clip_spec, clip_spec, fixed((width, hidden)), fixed((hidden, width)),
                  fixed((8, width)), fixed((8, width)), fixed((8, hidden))],
        out_specs=[clip_spec, clip_spec,
                   pl.BlockSpec(memory_space=pl.ANY), pl.BlockSpec(memory_space=pl.ANY),
                   fixed((8, width)), fixed((8, width)), fixed((8, hidden))],
        scratch_shapes=[
            pltpu.VMEM((length + 2 * PAD, width), F32),
            pltpu.VMEM((length, width), F32),
            pltpu.VMEM((length, 1), F32),
            pltpu.VMEM((length, width), BF16),
            pltpu.VMEM((length, width), F32),
            pltpu.VMEM((length + 2 * PAD, width), F32),
            pltpu.VMEM((width, hidden), F32),
            pltpu.VMEM((hidden, width), F32),
            pltpu.SemaphoreType.DMA((2,)),
        ],
    )
    flops = 12 * clips * length * width * hidden
    cost = pl.CostEstimate(flops=flops, transcendentals=2 * clips * length * hidden,
                           bytes_accessed=clips * length * width * 8 + 4 * width * hidden * 4)
    return pl.pallas_call(
        kernel,
        grid_spec=grid_spec,
        out_shape=[
            jax.ShapeDtypeStruct((clips, length, width), BF16),
            jax.ShapeDtypeStruct((clips, length, width), F32),
            jax.ShapeDtypeStruct((width, hidden), F32),
            jax.ShapeDtypeStruct((hidden, width), F32),
            jax.ShapeDtypeStruct((8, width), F32),
            jax.ShapeDtypeStruct((8, width), F32),
            jax.ShapeDtypeStruct((8, hidden), F32),
        ],
        compiler_params=pltpu.CompilerParams(
            dimension_semantics=("arbitrary",), vmem_limit_bytes=60 * 1024 * 1024),
        cost_estimate=cost,
    )(counts, frames, cotangent, w1, w2, cw8, vec8, b1_8)


def unpack(packed, width, hidden):
    shapes = [(width, hidden), (hidden, width), (TAPS, width), (width,), (width,), (width,), (width,), (width,), (hidden,)]
    pieces = []
    start_at = 0
    for shape in shapes:
        entries = 1
        for extent in shape:
            entries = entries * extent
        pieces.append(packed[start_at : start_at + entries].reshape(shape))
        start_at = start_at + entries
    return (tuple(pieces), start_at)


def body(frames, counts, cotangent, master, momentum, average, disc_grads):
    devices = lax.axis_size(("dp", "fsdp"))
    clips, length, width = frames.shape
    hidden = 3 * width
    rows = clips * length
    flat_size = master.shape[0] * devices
    total_frames = jnp.float32(rows * devices)
    rounded = master.astype(BF16)
    packed = lax.all_gather(rounded, ("dp", "fsdp"), axis=0, tiled=True)
    (w_one, w_two, conv_w, conv_b, ln_g, ln_b, b_two, gamma, b_one), used = unpack(packed, width, hidden)
    cw8 = jnp.zeros((8, width), F32).at[:TAPS].set(conv_w.astype(F32))
    vec8 = jnp.concatenate(
        [jnp.stack([conv_b, ln_g, ln_b, b_two, gamma]).astype(F32), jnp.zeros((3, width), F32)])
    b1_8 = jnp.zeros((8, hidden), F32).at[0].set(b_one.astype(F32))
    block_out, input_grad, g_w1, g_w2, gcw, gvec, gb1 = fused_block(
        frames, counts, cotangent, w_one, w_two, cw8, vec8, b1_8)
    grad_full = jnp.concatenate(
        [
            g_w1.reshape(-1),
            g_w2.reshape(-1),
            gcw[:TAPS].reshape(-1),
            gvec[0],
            gvec[1],
            gvec[2],
            gvec[3],
            gvec[4],
            gb1[0],
            jnp.zeros((flat_size - used,), F32),
        ]
    )
    grad_shard = lax.psum_scatter(grad_full, ("dp", "fsdp"), scatter_dimension=0, tiled=True)
    own_sum, disc_sum = lax.psum(
        (jnp.sum(grad_shard * grad_shard), jnp.sum(disc_grads * disc_grads)), ("dp", "fsdp")
    )
    grad_norm = jnp.sqrt(own_sum + disc_sum)
    clipped = grad_shard * jnp.minimum(1.0, 20.0 * jnp.sqrt(total_frames) / (grad_norm + 1e-06))
    new_momentum = 0.9 * momentum + clipped
    new_master = master - (clipped + 0.9 * new_momentum) / jnp.sqrt(total_frames)
    new_average = 0.99 * average + 0.01 * new_master
    return (
        block_out,
        input_grad,
        grad_norm,
        new_master,
        new_momentum,
        new_average,
        new_master.astype(BF16),
        new_average.astype(BF16),
    )


def solution(mesh):
    clip_spec = P(("dp", "fsdp"), None, None)
    flat_spec = P(("dp", "fsdp"))
    return jax.shard_map(
        body,
        mesh=mesh,
        in_specs=(clip_spec, flat_spec, clip_spec, flat_spec, flat_spec, flat_spec, flat_spec),
        out_specs=(clip_spec, clip_spec, P(), flat_spec, flat_spec, flat_spec, flat_spec, flat_spec),
        check_vma=False,
    )
```

```python
import functools
import math

import jax
import jax.numpy as jnp
from jax import lax
from jax.experimental import pallas as pl
from jax.experimental.pallas import tpu as pltpu
from jax.sharding import PartitionSpec as P

F32 = jnp.float32
BF16 = jnp.bfloat16
TAPS = 7
HALF = TAPS // 2
PAD = 8


def tdot(x, y):
    return lax.dot_general(x, y, (((0,), (0,)), ((), ())), preferred_element_type=F32)


def ntdot(x, y):
    return lax.dot_general(x, y, (((1,), (1,)), ((), ())), preferred_element_type=F32)


def block_kernel(length, width, hidden, rows):
    nblk = length // rows
    inv_w = 1.0 / width
    sqrt_half = math.sqrt(0.5)
    inv_sqrt_2pi = 1.0 / math.sqrt(2.0 * math.pi)

    def kernel(counts_ref, fr_ref, cot_ref, w1_ref, w2_ref, cw_ref, vec_ref, b1_ref,
               bo_ref, ig_ref, gw1_hbm, gw2_hbm, gcw_ref, gvec_ref, gb1_ref,
               xpad, xhat_s, rstd_s, a_s, da_s, dpad, gw1_s, gw2_s, sems):
        clip = pl.program_id(0)
        count = counts_ref[clip]

        @pl.when(clip == 0)
        def _init():
            gw1_s[...] = jnp.zeros_like(gw1_s)
            gw2_s[...] = jnp.zeros_like(gw2_s)
            gcw_ref[...] = jnp.zeros_like(gcw_ref)
            gvec_ref[...] = jnp.zeros_like(gvec_ref)
            gb1_ref[...] = jnp.zeros_like(gb1_ref)
            xpad[0:PAD, :] = jnp.zeros((PAD, width), F32)
            xpad[PAD + length:, :] = jnp.zeros((PAD, width), F32)
            dpad[0:PAD, :] = jnp.zeros((PAD, width), F32)
            dpad[PAD + length:, :] = jnp.zeros((PAD, width), F32)

        cw = cw_ref[...]
        conv_b = vec_ref[0:1, :]
        ln_g = vec_ref[1:2, :]
        ln_b = vec_ref[2:3, :]
        b_two = vec_ref[3:4, :]
        gamma = vec_ref[4:5, :]
        b_one = b1_ref[0:1, :]

        all_rows = lax.broadcasted_iota(jnp.int32, (length, 1), 0)
        xpad[PAD:PAD + length, :] = jnp.where(all_rows < count, fr_ref[0].astype(F32), 0.0)

        for b in range(nblk):
            r0 = b * rows

            @pl.when(r0 < count)
            def _fwd_block():
                base = PAD + r0 - HALF
                conv = conv_b + cw[0:1, :] * xpad[base:base + rows, :]
                for k in range(1, TAPS):
                    conv = conv + cw[k:k + 1, :] * xpad[base + k:base + k + rows, :]
                centre = jnp.sum(conv, axis=-1, keepdims=True) * inv_w
                shifted = conv - centre
                spread = jnp.sum(shifted * shifted, axis=-1, keepdims=True) * inv_w
                rstd = lax.rsqrt(spread + 1e-6)
                xhat = shifted * rstd
                xhat_s[r0:r0 + rows, :] = xhat
                rstd_s[r0:r0 + rows, :] = rstd
                a_s[r0:r0 + rows, :] = (xhat * ln_g + ln_b).astype(BF16)

        bo_ref[...] = jnp.zeros_like(bo_ref)

        def chunk(c, carry):
            g_gamma, g_b2, g_b1 = carry
            r0 = pl.multiple_of(c * rows, rows)
            a = a_s[pl.ds(r0, rows), :]
            h1 = jnp.dot(a, w1_ref[...], preferred_element_type=F32) + b_one
            cdf = 0.5 * (1.0 + lax.erf(h1 * sqrt_half))
            hh = (h1 * cdf).astype(BF16)
            z = jnp.dot(hh, w2_ref[...], preferred_element_type=F32) + b_two
            live = (r0 + lax.broadcasted_iota(jnp.int32, (rows, 1), 0)) < count
            xin = fr_ref[0, pl.ds(r0, rows), :].astype(F32)
            bo_ref[0, pl.ds(r0, rows), :] = jnp.where(live, xin + gamma * z, 0.0).astype(BF16)
            dout = jnp.where(live, cot_ref[0, pl.ds(r0, rows), :].astype(F32), 0.0)
            g_gamma = g_gamma + jnp.sum(dout * z, axis=0, keepdims=True)
            dz = (gamma * dout).astype(BF16)
            g_b2 = g_b2 + jnp.sum(dz.astype(F32), axis=0, keepdims=True)
            gw2_s[...] += tdot(hh, dz)
            dhh = ntdot(dz, w2_ref[...])
            slope = cdf + h1 * (jnp.exp(-0.5 * (h1 * h1)) * inv_sqrt_2pi)
            dh1 = (dhh * slope).astype(BF16)
            g_b1 = g_b1 + jnp.sum(dh1.astype(F32), axis=0, keepdims=True)
            gw1_s[...] += tdot(a, dh1)
            da_s[pl.ds(r0, rows), :] = ntdot(dh1, w1_ref[...])
            return g_gamma, g_b2, g_b1

        nact = (count + rows - 1) // rows
        zero_d = jnp.zeros((1, width), F32)
        g_gamma, g_b2, g_b1 = lax.fori_loop(
            0, nact, chunk, (zero_d, zero_d, jnp.zeros((1, hidden), F32)))

        def dxm_block(b):
            r0 = b * rows
            base = PAD + r0 + HALF
            dxm = cw[0:1, :] * dpad[base:base + rows, :]
            for k in range(1, TAPS):
                dxm = dxm + cw[k:k + 1, :] * dpad[base - k:base - k + rows, :]
            live = (r0 + lax.broadcasted_iota(jnp.int32, (rows, 1), 0)) < count
            cot = cot_ref[0, r0:r0 + rows, :].astype(F32)
            ig_ref[0, r0:r0 + rows, :] = jnp.where(live, cot + dxm, 0.0)

        sums = [zero_d] * (3 + TAPS)
        for b in range(nblk):
            r0 = b * rows

            def _bwd_block(r0=r0):
                live = (r0 + lax.broadcasted_iota(jnp.int32, (rows, 1), 0)) < count
                da = jnp.where(live, da_s[r0:r0 + rows, :], 0.0)
                xhat = xhat_s[r0:r0 + rows, :]
                rstd = rstd_s[r0:r0 + rows, :]
                dn = da * ln_g
                m1 = jnp.sum(dn, axis=-1, keepdims=True) * inv_w
                m2 = jnp.sum(dn * xhat, axis=-1, keepdims=True) * inv_w
                dconv = jnp.where(live, rstd * (dn - m1 - xhat * m2), 0.0)
                dpad[PAD + r0:PAD + r0 + rows, :] = dconv
                part = [jnp.sum(dconv, axis=0, keepdims=True),
                        jnp.sum(da * xhat, axis=0, keepdims=True),
                        jnp.sum(da, axis=0, keepdims=True)]
                base = PAD + r0 - HALF
                for k in range(TAPS):
                    part.append(jnp.sum(dconv * xpad[base + k:base + k + rows, :], axis=0, keepdims=True))
                return part

            active = r0 < count
            part = lax.cond(active, _bwd_block, lambda: [zero_d] * (3 + TAPS))

            @pl.when(jnp.logical_not(active))
            def _idle():
                dpad[PAD + r0:PAD + r0 + rows, :] = jnp.zeros((rows, width), F32)
                ig_ref[0, r0:r0 + rows, :] = jnp.zeros((rows, width), F32)

            sums = [s + p for s, p in zip(sums, part)]
            if b >= 1:
                @pl.when((b - 1) * rows < count)
                def _prev(b=b):
                    dxm_block(b - 1)

        @pl.when((nblk - 1) * rows < count)
        def _last():
            dxm_block(nblk - 1)

        gvec_ref[0:1, :] += sums[0]
        gvec_ref[1:2, :] += sums[1]
        gvec_ref[2:3, :] += sums[2]
        gvec_ref[3:4, :] += g_b2
        gvec_ref[4:5, :] += g_gamma
        for k in range(TAPS):
            gcw_ref[k:k + 1, :] += sums[3 + k]
        gb1_ref[0:1, :] += g_b1

        @pl.when(clip == pl.num_programs(0) - 1)
        def _flush():
            c1 = pltpu.make_async_copy(gw1_s, gw1_hbm, sems.at[0])
            c2 = pltpu.make_async_copy(gw2_s, gw2_hbm, sems.at[1])
            c1.start()
            c2.start()
            c1.wait()
            c2.wait()

    return kernel


def fused_block(frames, counts, cotangent, w1, w2, cw8, vec8, b1_8, rows=256):
    clips, length, width = frames.shape
    hidden = w1.shape[1]
    kernel = block_kernel(length, width, hidden, rows)
    clip_spec = pl.BlockSpec((1, length, width), lambda i, c: (i, 0, 0))
    fixed = lambda shape: pl.BlockSpec(shape, lambda i, c: (0, 0))
    grid_spec = pltpu.PrefetchScalarGridSpec(
        num_scalar_prefetch=1,
        grid=(clips,),
        in_specs=[clip_spec, clip_spec, fixed((width, hidden)), fixed((hidden, width)),
                  fixed((8, width)), fixed((8, width)), fixed((8, hidden))],
        out_specs=[clip_spec, clip_spec,
                   pl.BlockSpec(memory_space=pl.ANY), pl.BlockSpec(memory_space=pl.ANY),
                   fixed((8, width)), fixed((8, width)), fixed((8, hidden))],
        scratch_shapes=[
            pltpu.VMEM((length + 2 * PAD, width), F32),
            pltpu.VMEM((length, width), F32),
            pltpu.VMEM((length, 1), F32),
            pltpu.VMEM((length, width), BF16),
            pltpu.VMEM((length, width), F32),
            pltpu.VMEM((length + 2 * PAD, width), F32),
            pltpu.VMEM((width, hidden), F32),
            pltpu.VMEM((hidden, width), F32),
            pltpu.SemaphoreType.DMA((2,)),
        ],
    )
    flops = 12 * clips * length * width * hidden
    cost = pl.CostEstimate(flops=flops, transcendentals=2 * clips * length * hidden,
                           bytes_accessed=clips * length * width * 8 + 4 * width * hidden * 4)
    return pl.pallas_call(
        kernel,
        grid_spec=grid_spec,
        out_shape=[
            jax.ShapeDtypeStruct((clips, length, width), BF16),
            jax.ShapeDtypeStruct((clips, length, width), F32),
            jax.ShapeDtypeStruct((width, hidden), F32),
            jax.ShapeDtypeStruct((hidden, width), F32),
            jax.ShapeDtypeStruct((8, width), F32),
            jax.ShapeDtypeStruct((8, width), F32),
            jax.ShapeDtypeStruct((8, hidden), F32),
        ],
        compiler_params=pltpu.CompilerParams(
            dimension_semantics=("arbitrary",), vmem_limit_bytes=60 * 1024 * 1024),
        cost_estimate=cost,
    )(counts, frames, cotangent, w1, w2, cw8, vec8, b1_8)


def unpack(packed, width, hidden):
    shapes = [(width, hidden), (hidden, width), (TAPS, width), (width,), (width,), (width,), (width,), (width,), (hidden,)]
    pieces = []
    start_at = 0
    for shape in shapes:
        entries = 1
        for extent in shape:
            entries = entries * extent
        pieces.append(packed[start_at : start_at + entries].reshape(shape))
        start_at = start_at + entries
    return (tuple(pieces), start_at)


AXES = ("dp", "fsdp")
LANES = 128


def bit_order(mesh_sizes):
    dp_size, fsdp_size = mesh_sizes
    fsdp_bits = int(math.log2(fsdp_size))
    dp_bits = int(math.log2(dp_size))
    order = [0] + [fsdp_bits + b for b in range(dp_bits)] + list(range(1, fsdp_bits))
    return order, fsdp_bits + dp_bits


def swap_perm(devices, bit):
    return [(i, i ^ (1 << bit)) for i in range(devices)]


def tree_all_gather(shard, order, nbits):
    me = lax.axis_index(AXES)
    devices = 1 << nbits
    held = shard
    held_bits = []
    for bit in order:
        other = lax.ppermute(held, AXES, swap_perm(devices, bit))
        upper = ((me >> bit) & 1) == 1
        held = jnp.stack([jnp.where(upper, other, held), jnp.where(upper, held, other)])
        held_bits.insert(0, bit)
    axes = [held_bits.index(b) for b in sorted(held_bits, reverse=True)]
    held = jnp.transpose(held, axes + [nbits, nbits + 1])
    return held.reshape(devices * shard.shape[0], LANES)


def tree_reduce_scatter(full, order, nbits):
    me = lax.axis_index(AXES)
    devices = 1 << nbits
    rows = full.shape[0] // devices
    held = full.reshape([2] * nbits + [rows, LANES])
    held_bits = [nbits - 1 - a for a in range(nbits)]
    for bit in order:
        axis = held_bits.index(bit)
        mine = (me >> bit) & 1
        keep = lax.dynamic_index_in_dim(held, mine, axis=axis, keepdims=False)
        send = lax.dynamic_index_in_dim(held, 1 - mine, axis=axis, keepdims=False)
        held = keep + lax.ppermute(send, AXES, swap_perm(devices, bit))
        held_bits.pop(axis)
    return held


def tree_all_sum(value, order, nbits):
    devices = 1 << nbits
    for bit in reversed(order):
        value = value + lax.ppermute(value, AXES, swap_perm(devices, bit))
    return value


def body(frames, counts, cotangent, master, momentum, average, disc_grads, mesh_sizes=None):
    order, nbits = bit_order(mesh_sizes)
    devices = 1 << nbits
    clips, length, width = frames.shape
    hidden = 3 * width
    rows = clips * length
    local = master.shape[0]
    flat_size = local * devices
    total_frames = jnp.float32(rows * devices)
    rounded = master.astype(BF16).reshape(local // LANES, LANES)
    packed = tree_all_gather(rounded, order[::-1], nbits).reshape(-1)
    (w_one, w_two, conv_w, conv_b, ln_g, ln_b, b_two, gamma, b_one), used = unpack(packed, width, hidden)
    cw8 = jnp.zeros((8, width), F32).at[:TAPS].set(conv_w.astype(F32))
    vec8 = jnp.concatenate(
        [jnp.stack([conv_b, ln_g, ln_b, b_two, gamma]).astype(F32), jnp.zeros((3, width), F32)])
    b1_8 = jnp.zeros((8, hidden), F32).at[0].set(b_one.astype(F32))
    block_out, input_grad, g_w1, g_w2, gcw, gvec, gb1 = fused_block(
        frames, counts, cotangent, w_one, w_two, cw8, vec8, b1_8)
    grad_full = jnp.concatenate(
        [
            g_w1.reshape(-1),
            g_w2.reshape(-1),
            gcw[:TAPS].reshape(-1),
            gvec[0],
            gvec[1],
            gvec[2],
            gvec[3],
            gvec[4],
            gb1[0],
            jnp.zeros((flat_size - used,), F32),
        ]
    ).reshape(flat_size // LANES, LANES)
    grad_shard = tree_reduce_scatter(grad_full, order, nbits)
    disc_rows = jnp.sum((disc_grads * disc_grads).reshape(-1, LANES), axis=0, keepdims=True)
    own_rows = jnp.sum(grad_shard * grad_shard, axis=0, keepdims=True)
    squares = jnp.broadcast_to(own_rows + disc_rows, (8, LANES))
    squares = tree_all_sum(squares, order, nbits)
    grad_norm = jnp.sqrt(jnp.sum(squares[0]))
    grad_shard = grad_shard.reshape(-1)
    clipped = grad_shard * jnp.minimum(1.0, 20.0 * jnp.sqrt(total_frames) / (grad_norm + 1e-06))
    new_momentum = 0.9 * momentum + clipped
    new_master = master - (clipped + 0.9 * new_momentum) / jnp.sqrt(total_frames)
    new_average = 0.99 * average + 0.01 * new_master
    return (
        block_out,
        input_grad,
        grad_norm,
        new_master,
        new_momentum,
        new_average,
        new_master.astype(BF16),
        new_average.astype(BF16),
    )


def solution(mesh):
    clip_spec = P(("dp", "fsdp"), None, None)
    flat_spec = P(("dp", "fsdp"))
    mesh_sizes = (mesh.shape["dp"], mesh.shape["fsdp"])
    return jax.shard_map(
        functools.partial(body, mesh_sizes=mesh_sizes),
        mesh=mesh,
        in_specs=(clip_spec, flat_spec, clip_spec, flat_spec, flat_spec, flat_spec, flat_spec),
        out_specs=(clip_spec, clip_spec, P(), flat_spec, flat_spec, flat_spec, flat_spec, flat_spec),
        check_vma=False,
    )
```

```python
import functools
import math

import jax
import jax.numpy as jnp
from jax import lax
from jax.experimental import pallas as pl
from jax.experimental.pallas import tpu as pltpu
from jax.sharding import PartitionSpec as P

F32 = jnp.float32
BF16 = jnp.bfloat16
TAPS = 7
HALF = TAPS // 2
PAD = 8


def tdot(x, y):
    return lax.dot_general(x, y, (((0,), (0,)), ((), ())), preferred_element_type=F32)


def ntdot(x, y):
    return lax.dot_general(x, y, (((1,), (1,)), ((), ())), preferred_element_type=F32)


def block_kernel(length, width, hidden, rows):
    nblk = length // rows
    inv_w = 1.0 / width
    sqrt_half = math.sqrt(0.5)
    inv_sqrt_2pi = 1.0 / math.sqrt(2.0 * math.pi)

    def kernel(counts_ref, fr_ref, cot_ref, w1_ref, w2_ref, cw_ref, vec_ref, b1_ref,
               bo_ref, ig_ref, gw1_hbm, gw2_hbm, gcw_ref, gvec_ref, gb1_ref,
               xpad, xhat_s, rstd_s, a_s, da_s, dpad, gw1_s, gw2_s, sems):
        clip = pl.program_id(0)
        count = counts_ref[clip]

        @pl.when(clip == 0)
        def _init():
            gw1_s[...] = jnp.zeros_like(gw1_s)
            gw2_s[...] = jnp.zeros_like(gw2_s)
            gcw_ref[...] = jnp.zeros_like(gcw_ref)
            gvec_ref[...] = jnp.zeros_like(gvec_ref)
            gb1_ref[...] = jnp.zeros_like(gb1_ref)
            xpad[0:PAD, :] = jnp.zeros((PAD, width), F32)
            xpad[PAD + length:, :] = jnp.zeros((PAD, width), F32)
            dpad[0:PAD, :] = jnp.zeros((PAD, width), F32)
            dpad[PAD + length:, :] = jnp.zeros((PAD, width), F32)

        cw = cw_ref[...]
        conv_b = vec_ref[0:1, :]
        ln_g = vec_ref[1:2, :]
        ln_b = vec_ref[2:3, :]
        b_two = vec_ref[3:4, :]
        gamma = vec_ref[4:5, :]
        b_one = b1_ref[0:1, :]

        all_rows = lax.broadcasted_iota(jnp.int32, (length, 1), 0)
        xpad[PAD:PAD + length, :] = jnp.where(all_rows < count, fr_ref[0].astype(F32), 0.0)

        for b in range(nblk):
            r0 = b * rows

            @pl.when(r0 < count)
            def _fwd_block():
                base = PAD + r0 - HALF
                conv = conv_b + cw[0:1, :] * xpad[base:base + rows, :]
                for k in range(1, TAPS):
                    conv = conv + cw[k:k + 1, :] * xpad[base + k:base + k + rows, :]
                centre = jnp.sum(conv, axis=-1, keepdims=True) * inv_w
                shifted = conv - centre
                spread = jnp.sum(shifted * shifted, axis=-1, keepdims=True) * inv_w
                rstd = lax.rsqrt(spread + 1e-6)
                xhat = shifted * rstd
                xhat_s[r0:r0 + rows, :] = xhat
                rstd_s[r0:r0 + rows, :] = rstd
                a_s[r0:r0 + rows, :] = (xhat * ln_g + ln_b).astype(BF16)

        bo_ref[...] = jnp.zeros_like(bo_ref)

        def chunk(c, carry):
            g_gamma, g_b2, g_b1 = carry
            r0 = pl.multiple_of(c * rows, rows)
            a = a_s[pl.ds(r0, rows), :]
            h1 = jnp.dot(a, w1_ref[...], preferred_element_type=F32) + b_one
            cdf = 0.5 * (1.0 + lax.erf(h1 * sqrt_half))
            hh = (h1 * cdf).astype(BF16)
            z = jnp.dot(hh, w2_ref[...], preferred_element_type=F32) + b_two
            live = (r0 + lax.broadcasted_iota(jnp.int32, (rows, 1), 0)) < count
            xin = fr_ref[0, pl.ds(r0, rows), :].astype(F32)
            bo_ref[0, pl.ds(r0, rows), :] = jnp.where(live, xin + gamma * z, 0.0).astype(BF16)
            dout = jnp.where(live, cot_ref[0, pl.ds(r0, rows), :].astype(F32), 0.0)
            g_gamma = g_gamma + jnp.sum(dout * z, axis=0, keepdims=True)
            dz = (gamma * dout).astype(BF16)
            g_b2 = g_b2 + jnp.sum(dz.astype(F32), axis=0, keepdims=True)
            gw2_s[...] += tdot(hh, dz)
            dhh = ntdot(dz, w2_ref[...])
            slope = cdf + h1 * (jnp.exp(-0.5 * (h1 * h1)) * inv_sqrt_2pi)
            dh1 = (dhh * slope).astype(BF16)
            g_b1 = g_b1 + jnp.sum(dh1.astype(F32), axis=0, keepdims=True)
            gw1_s[...] += tdot(a, dh1)
            da_s[pl.ds(r0, rows), :] = ntdot(dh1, w1_ref[...])
            return g_gamma, g_b2, g_b1

        nact = (count + rows - 1) // rows
        zero_d = jnp.zeros((1, width), F32)
        g_gamma, g_b2, g_b1 = lax.fori_loop(
            0, nact, chunk, (zero_d, zero_d, jnp.zeros((1, hidden), F32)))

        def dxm_block(b):
            r0 = b * rows
            base = PAD + r0 + HALF
            dxm = cw[0:1, :] * dpad[base:base + rows, :]
            for k in range(1, TAPS):
                dxm = dxm + cw[k:k + 1, :] * dpad[base - k:base - k + rows, :]
            live = (r0 + lax.broadcasted_iota(jnp.int32, (rows, 1), 0)) < count
            cot = cot_ref[0, r0:r0 + rows, :].astype(F32)
            ig_ref[0, r0:r0 + rows, :] = jnp.where(live, cot + dxm, 0.0)

        sums = [zero_d] * (3 + TAPS)
        for b in range(nblk):
            r0 = b * rows

            def _bwd_block(r0=r0):
                live = (r0 + lax.broadcasted_iota(jnp.int32, (rows, 1), 0)) < count
                da = jnp.where(live, da_s[r0:r0 + rows, :], 0.0)
                xhat = xhat_s[r0:r0 + rows, :]
                rstd = rstd_s[r0:r0 + rows, :]
                dn = da * ln_g
                m1 = jnp.sum(dn, axis=-1, keepdims=True) * inv_w
                m2 = jnp.sum(dn * xhat, axis=-1, keepdims=True) * inv_w
                dconv = jnp.where(live, rstd * (dn - m1 - xhat * m2), 0.0)
                dpad[PAD + r0:PAD + r0 + rows, :] = dconv
                part = [jnp.sum(dconv, axis=0, keepdims=True),
                        jnp.sum(da * xhat, axis=0, keepdims=True),
                        jnp.sum(da, axis=0, keepdims=True)]
                base = PAD + r0 - HALF
                for k in range(TAPS):
                    part.append(jnp.sum(dconv * xpad[base + k:base + k + rows, :], axis=0, keepdims=True))
                return part

            active = r0 < count
            part = lax.cond(active, _bwd_block, lambda: [zero_d] * (3 + TAPS))

            @pl.when(jnp.logical_not(active))
            def _idle():
                dpad[PAD + r0:PAD + r0 + rows, :] = jnp.zeros((rows, width), F32)
                ig_ref[0, r0:r0 + rows, :] = jnp.zeros((rows, width), F32)

            sums = [s + p for s, p in zip(sums, part)]
            if b >= 1:
                @pl.when((b - 1) * rows < count)
                def _prev(b=b):
                    dxm_block(b - 1)

        @pl.when((nblk - 1) * rows < count)
        def _last():
            dxm_block(nblk - 1)

        gvec_ref[0:1, :] += sums[0]
        gvec_ref[1:2, :] += sums[1]
        gvec_ref[2:3, :] += sums[2]
        gvec_ref[3:4, :] += g_b2
        gvec_ref[4:5, :] += g_gamma
        for k in range(TAPS):
            gcw_ref[k:k + 1, :] += sums[3 + k]
        gb1_ref[0:1, :] += g_b1

        @pl.when(clip == pl.num_programs(0) - 1)
        def _flush():
            c1 = pltpu.make_async_copy(gw1_s, gw1_hbm, sems.at[0])
            c2 = pltpu.make_async_copy(gw2_s, gw2_hbm, sems.at[1])
            c1.start()
            c2.start()
            c1.wait()
            c2.wait()

    return kernel


def fused_block(frames, counts, cotangent, w1, w2, cw8, vec8, b1_8, rows=256):
    clips, length, width = frames.shape
    hidden = w1.shape[1]
    kernel = block_kernel(length, width, hidden, rows)
    clip_spec = pl.BlockSpec((1, length, width), lambda i, c: (i, 0, 0))
    fixed = lambda shape: pl.BlockSpec(shape, lambda i, c: (0, 0))
    grid_spec = pltpu.PrefetchScalarGridSpec(
        num_scalar_prefetch=1,
        grid=(clips,),
        in_specs=[clip_spec, clip_spec, fixed((width, hidden)), fixed((hidden, width)),
                  fixed((8, width)), fixed((8, width)), fixed((8, hidden))],
        out_specs=[clip_spec, clip_spec,
                   pl.BlockSpec(memory_space=pl.ANY), pl.BlockSpec(memory_space=pl.ANY),
                   fixed((8, width)), fixed((8, width)), fixed((8, hidden))],
        scratch_shapes=[
            pltpu.VMEM((length + 2 * PAD, width), F32),
            pltpu.VMEM((length, width), F32),
            pltpu.VMEM((length, 1), F32),
            pltpu.VMEM((length, width), BF16),
            pltpu.VMEM((length, width), F32),
            pltpu.VMEM((length + 2 * PAD, width), F32),
            pltpu.VMEM((width, hidden), F32),
            pltpu.VMEM((hidden, width), F32),
            pltpu.SemaphoreType.DMA((2,)),
        ],
    )
    flops = 12 * clips * length * width * hidden
    cost = pl.CostEstimate(flops=flops, transcendentals=2 * clips * length * hidden,
                           bytes_accessed=clips * length * width * 8 + 4 * width * hidden * 4)
    return pl.pallas_call(
        kernel,
        grid_spec=grid_spec,
        out_shape=[
            jax.ShapeDtypeStruct((clips, length, width), BF16),
            jax.ShapeDtypeStruct((clips, length, width), F32),
            jax.ShapeDtypeStruct((width, hidden), F32),
            jax.ShapeDtypeStruct((hidden, width), F32),
            jax.ShapeDtypeStruct((8, width), F32),
            jax.ShapeDtypeStruct((8, width), F32),
            jax.ShapeDtypeStruct((8, hidden), F32),
        ],
        compiler_params=pltpu.CompilerParams(
            dimension_semantics=("arbitrary",), vmem_limit_bytes=60 * 1024 * 1024),
        cost_estimate=cost,
    )(counts, frames, cotangent, w1, w2, cw8, vec8, b1_8)


def unpack(packed, width, hidden):
    shapes = [(width, hidden), (hidden, width), (TAPS, width), (width,), (width,), (width,), (width,), (width,), (hidden,)]
    pieces = []
    start_at = 0
    for shape in shapes:
        entries = 1
        for extent in shape:
            entries = entries * extent
        pieces.append(packed[start_at : start_at + entries].reshape(shape))
        start_at = start_at + entries
    return (tuple(pieces), start_at)


AXES = ("dp", "fsdp")
LANES = 128


def bit_order(mesh_sizes):
    dp_size, fsdp_size = mesh_sizes
    fsdp_bits = int(math.log2(fsdp_size))
    dp_bits = int(math.log2(dp_size))
    order = [0] + [fsdp_bits + b for b in range(dp_bits)] + list(range(1, fsdp_bits))
    return order, fsdp_bits + dp_bits


def swap_perm(devices, bit):
    return [(i, i ^ (1 << bit)) for i in range(devices)]


def split_orders(order):
    if len(order) < 3:
        return [order]
    other = [order[0], order[2], order[1]] + order[3:]
    return [order, other]


def tree_all_gather(shard, orders, nbits):
    me = lax.axis_index(AXES)
    devices = 1 << nbits
    rows = shard.shape[0]
    cuts = [rows * p // len(orders) for p in range(len(orders) + 1)]
    held = [shard[cuts[p]:cuts[p + 1]] for p in range(len(orders))]
    held_bits = [[] for _ in orders]
    for step in range(nbits):
        for p, order in enumerate(orders):
            bit = order[step]
            other = lax.ppermute(held[p], AXES, swap_perm(devices, bit))
            upper = ((me >> bit) & 1) == 1
            held[p] = jnp.stack([jnp.where(upper, other, held[p]), jnp.where(upper, held[p], other)])
            held_bits[p].insert(0, bit)
    parts = []
    for p in range(len(orders)):
        axes = [held_bits[p].index(b) for b in sorted(held_bits[p], reverse=True)]
        parts.append(jnp.transpose(held[p], axes + [nbits, nbits + 1]).reshape(devices, -1, LANES))
    return jnp.concatenate(parts, axis=1).reshape(devices * rows, LANES)


def tree_reduce_scatter(full, orders, nbits):
    me = lax.axis_index(AXES)
    devices = 1 << nbits
    rows = full.shape[0] // devices
    cuts = [rows * p // len(orders) for p in range(len(orders) + 1)]
    shaped = full.reshape([2] * nbits + [rows, LANES])
    held = [shaped[..., cuts[p]:cuts[p + 1], :] for p in range(len(orders))]
    held_bits = [[nbits - 1 - a for a in range(nbits)] for _ in orders]
    for step in range(nbits):
        for p, order in enumerate(orders):
            bit = order[step]
            axis = held_bits[p].index(bit)
            mine = (me >> bit) & 1
            keep = lax.dynamic_index_in_dim(held[p], mine, axis=axis, keepdims=False)
            send = lax.dynamic_index_in_dim(held[p], 1 - mine, axis=axis, keepdims=False)
            held[p] = keep + lax.ppermute(send, AXES, swap_perm(devices, bit))
            held_bits[p].pop(axis)
    return jnp.concatenate(held, axis=0)


def tree_all_sum(value, order, nbits):
    devices = 1 << nbits
    for bit in reversed(order):
        value = value + lax.ppermute(value, AXES, swap_perm(devices, bit))
    return value


def body(frames, counts, cotangent, master, momentum, average, disc_grads, mesh_sizes=None):
    order, nbits = bit_order(mesh_sizes)
    devices = 1 << nbits
    clips, length, width = frames.shape
    hidden = 3 * width
    rows = clips * length
    local = master.shape[0]
    flat_size = local * devices
    total_frames = jnp.float32(rows * devices)
    rounded = master.astype(BF16).reshape(local // LANES, LANES)
    packed = tree_all_gather(rounded, [o[::-1] for o in split_orders(order)], nbits).reshape(-1)
    (w_one, w_two, conv_w, conv_b, ln_g, ln_b, b_two, gamma, b_one), used = unpack(packed, width, hidden)
    cw8 = jnp.zeros((8, width), F32).at[:TAPS].set(conv_w.astype(F32))
    vec8 = jnp.concatenate(
        [jnp.stack([conv_b, ln_g, ln_b, b_two, gamma]).astype(F32), jnp.zeros((3, width), F32)])
    b1_8 = jnp.zeros((8, hidden), F32).at[0].set(b_one.astype(F32))
    block_out, input_grad, g_w1, g_w2, gcw, gvec, gb1 = fused_block(
        frames, counts, cotangent, w_one, w_two, cw8, vec8, b1_8)
    small = jnp.concatenate(
        [gcw[:TAPS].reshape(-1), gvec[0], gvec[1], gvec[2], gvec[3], gvec[4], gb1[0]]
    )
    grad_full = jnp.concatenate(
        [
            g_w1.reshape(-1, LANES),
            g_w2.reshape(-1, LANES),
            small.reshape(-1, LANES),
            jnp.zeros(((flat_size - used) // LANES, LANES), F32),
        ]
    )
    grad_shard = tree_reduce_scatter(grad_full, split_orders(order), nbits)
    disc_rows = jnp.sum((disc_grads * disc_grads).reshape(-1, LANES), axis=0, keepdims=True)
    own_rows = jnp.sum(grad_shard * grad_shard, axis=0, keepdims=True)
    squares = jnp.broadcast_to(own_rows + disc_rows, (8, LANES))
    squares = tree_all_sum(squares, order, nbits)
    grad_norm = jnp.sqrt(jnp.sum(squares[0]))
    grad_shard = grad_shard.reshape(-1)
    clipped = grad_shard * jnp.minimum(1.0, 20.0 * jnp.sqrt(total_frames) / (grad_norm + 1e-06))
    new_momentum = 0.9 * momentum + clipped
    new_master = master - (clipped + 0.9 * new_momentum) / jnp.sqrt(total_frames)
    new_average = 0.99 * average + 0.01 * new_master
    return (
        block_out,
        input_grad,
        grad_norm,
        new_master,
        new_momentum,
        new_average,
        new_master.astype(BF16),
        new_average.astype(BF16),
    )


def solution(mesh):
    clip_spec = P(("dp", "fsdp"), None, None)
    flat_spec = P(("dp", "fsdp"))
    mesh_sizes = (mesh.shape["dp"], mesh.shape["fsdp"])
    return jax.shard_map(
        functools.partial(body, mesh_sizes=mesh_sizes),
        mesh=mesh,
        in_specs=(clip_spec, flat_spec, clip_spec, flat_spec, flat_spec, flat_spec, flat_spec),
        out_specs=(clip_spec, clip_spec, P(), flat_spec, flat_spec, flat_spec, flat_spec, flat_spec),
        check_vma=False,
    )
```

```python
import functools
import math

import jax
import jax.numpy as jnp
from jax import lax
from jax.experimental import pallas as pl
from jax.experimental.pallas import tpu as pltpu
from jax.sharding import PartitionSpec as P

F32 = jnp.float32
BF16 = jnp.bfloat16
TAPS = 7
HALF = TAPS // 2
PAD = 8
LANE = 128


def tdot(x, y):
    return lax.dot_general(x, y, (((0,), (0,)), ((), ())), preferred_element_type=F32)


def ntdot(x, y):
    return lax.dot_general(x, y, (((1,), (1,)), ((), ())), preferred_element_type=F32)


def block_kernel(length, width, hidden, rows):
    nblk = length // rows
    quads = width // LANE
    inv_w = 1.0 / width
    sqrt_half = math.sqrt(0.5)
    inv_sqrt_2pi = 1.0 / math.sqrt(2.0 * math.pi)

    def kernel(counts_ref, fr_ref, cot_ref, w1_ref, w2_ref, cw_ref, vec_ref, b1_ref,
               bo_ref, ig_ref, gw1_hbm, gw2_hbm, gcw_ref, gvec_ref, gb1_ref,
               xq, xhat_s, rstd_s, a_s, da_s, dq, gw1_s, gw2_s, sems):
        clip = pl.program_id(0)
        count = counts_ref[clip]

        @pl.when(clip == 0)
        def _init():
            gw1_s[...] = jnp.zeros_like(gw1_s)
            gw2_s[...] = jnp.zeros_like(gw2_s)
            gcw_ref[...] = jnp.zeros_like(gcw_ref)
            gvec_ref[...] = jnp.zeros_like(gvec_ref)
            gb1_ref[...] = jnp.zeros_like(gb1_ref)
            xq[0:PAD * quads, :] = jnp.zeros((PAD * quads, LANE), F32)
            xq[(PAD + length) * quads:, :] = jnp.zeros((PAD * quads, LANE), F32)
            dq[0:PAD * quads, :] = jnp.zeros((PAD * quads, LANE), F32)
            dq[(PAD + length) * quads:, :] = jnp.zeros((PAD * quads, LANE), F32)

        cw = cw_ref[...]
        conv_b = vec_ref[0:1, :]
        ln_g = vec_ref[1:2, :]
        ln_b = vec_ref[2:3, :]
        b_two = vec_ref[3:4, :]
        gamma = vec_ref[4:5, :]
        b_one = b1_ref[0:1, :]

        all_rows = lax.broadcasted_iota(jnp.int32, (length, 1), 0)
        xm_all = jnp.where(all_rows < count, fr_ref[0].astype(F32), 0.0)
        for q in range(quads):
            xq[pl.ds(PAD * quads + q, length, stride=quads), :] = xm_all[:, q * LANE:(q + 1) * LANE]

        def taps_of(buf, start):
            return jnp.concatenate(
                [buf[pl.ds(start * quads + q, rows, stride=quads), :] for q in range(quads)], axis=1)

        for b in range(nblk):
            r0 = b * rows

            @pl.when(r0 < count)
            def _fwd_block():
                base = PAD + r0 - HALF
                conv = conv_b + cw[0:1, :] * taps_of(xq, base)
                for k in range(1, TAPS):
                    conv = conv + cw[k:k + 1, :] * taps_of(xq, base + k)
                centre = jnp.sum(conv, axis=-1, keepdims=True) * inv_w
                shifted = conv - centre
                spread = jnp.sum(shifted * shifted, axis=-1, keepdims=True) * inv_w
                rstd = lax.rsqrt(spread + 1e-6)
                xhat = shifted * rstd
                xhat_s[r0:r0 + rows, :] = xhat
                rstd_s[r0:r0 + rows, :] = rstd
                a_s[r0:r0 + rows, :] = (xhat * ln_g + ln_b).astype(BF16)

        bo_ref[...] = jnp.zeros_like(bo_ref)

        def chunk(c, carry):
            g_gamma, g_b2, g_b1 = carry
            r0 = pl.multiple_of(c * rows, rows)
            a = a_s[pl.ds(r0, rows), :]
            h1 = jnp.dot(a, w1_ref[...], preferred_element_type=F32) + b_one
            cdf = 0.5 * (1.0 + lax.erf(h1 * sqrt_half))
            hh = (h1 * cdf).astype(BF16)
            z = jnp.dot(hh, w2_ref[...], preferred_element_type=F32) + b_two
            live = (r0 + lax.broadcasted_iota(jnp.int32, (rows, 1), 0)) < count
            xin = fr_ref[0, pl.ds(r0, rows), :].astype(F32)
            bo_ref[0, pl.ds(r0, rows), :] = jnp.where(live, xin + gamma * z, 0.0).astype(BF16)
            dout = jnp.where(live, cot_ref[0, pl.ds(r0, rows), :].astype(F32), 0.0)
            g_gamma = g_gamma + jnp.sum(dout * z, axis=0, keepdims=True)
            dz = (gamma * dout).astype(BF16)
            g_b2 = g_b2 + jnp.sum(dz.astype(F32), axis=0, keepdims=True)
            gw2_s[...] += tdot(hh, dz)
            dhh = ntdot(dz, w2_ref[...])
            slope = cdf + h1 * (jnp.exp(-0.5 * (h1 * h1)) * inv_sqrt_2pi)
            dh1 = (dhh * slope).astype(BF16)
            g_b1 = g_b1 + jnp.sum(dh1.astype(F32), axis=0, keepdims=True)
            gw1_s[...] += tdot(a, dh1)
            da_s[pl.ds(r0, rows), :] = ntdot(dh1, w1_ref[...])
            return g_gamma, g_b2, g_b1

        nact = (count + rows - 1) // rows
        zero_d = jnp.zeros((1, width), F32)
        g_gamma, g_b2, g_b1 = lax.fori_loop(
            0, nact, chunk, (zero_d, zero_d, jnp.zeros((1, hidden), F32)))

        def dxm_block(b):
            r0 = b * rows
            base = PAD + r0 + HALF
            dxm = cw[0:1, :] * taps_of(dq, base)
            for k in range(1, TAPS):
                dxm = dxm + cw[k:k + 1, :] * taps_of(dq, base - k)
            live = (r0 + lax.broadcasted_iota(jnp.int32, (rows, 1), 0)) < count
            cot = cot_ref[0, r0:r0 + rows, :].astype(F32)
            ig_ref[0, r0:r0 + rows, :] = jnp.where(live, cot + dxm, 0.0)

        sums = [zero_d] * (3 + TAPS)
        for b in range(nblk):
            r0 = b * rows

            def _bwd_block(r0=r0):
                live = (r0 + lax.broadcasted_iota(jnp.int32, (rows, 1), 0)) < count
                da = jnp.where(live, da_s[r0:r0 + rows, :], 0.0)
                xhat = xhat_s[r0:r0 + rows, :]
                rstd = rstd_s[r0:r0 + rows, :]
                dn = da * ln_g
                m1 = jnp.sum(dn, axis=-1, keepdims=True) * inv_w
                m2 = jnp.sum(dn * xhat, axis=-1, keepdims=True) * inv_w
                dconv = jnp.where(live, rstd * (dn - m1 - xhat * m2), 0.0)
                for q in range(quads):
                    dq[pl.ds((PAD + r0) * quads + q, rows, stride=quads), :] = dconv[:, q * LANE:(q + 1) * LANE]
                part = [jnp.sum(dconv, axis=0, keepdims=True),
                        jnp.sum(da * xhat, axis=0, keepdims=True),
                        jnp.sum(da, axis=0, keepdims=True)]
                base = PAD + r0 - HALF
                for k in range(TAPS):
                    part.append(jnp.sum(dconv * taps_of(xq, base + k), axis=0, keepdims=True))
                return part

            active = r0 < count
            part = lax.cond(active, _bwd_block, lambda: [zero_d] * (3 + TAPS))

            @pl.when(jnp.logical_not(active))
            def _idle():
                dq[(PAD + r0) * quads:(PAD + r0 + rows) * quads, :] = jnp.zeros((rows * quads, LANE), F32)
                ig_ref[0, r0:r0 + rows, :] = jnp.zeros((rows, width), F32)

            sums = [s + p for s, p in zip(sums, part)]
            if b >= 1:
                @pl.when((b - 1) * rows < count)
                def _prev(b=b):
                    dxm_block(b - 1)

        @pl.when((nblk - 1) * rows < count)
        def _last():
            dxm_block(nblk - 1)

        gvec_ref[0:1, :] += sums[0]
        gvec_ref[1:2, :] += sums[1]
        gvec_ref[2:3, :] += sums[2]
        gvec_ref[3:4, :] += g_b2
        gvec_ref[4:5, :] += g_gamma
        for k in range(TAPS):
            gcw_ref[k:k + 1, :] += sums[3 + k]
        gb1_ref[0:1, :] += g_b1

        @pl.when(clip == pl.num_programs(0) - 1)
        def _flush():
            c1 = pltpu.make_async_copy(gw1_s, gw1_hbm, sems.at[0])
            c2 = pltpu.make_async_copy(gw2_s, gw2_hbm, sems.at[1])
            c1.start()
            c2.start()
            c1.wait()
            c2.wait()

    return kernel


def fused_block(frames, counts, cotangent, w1, w2, cw8, vec8, b1_8, rows=256):
    clips, length, width = frames.shape
    hidden = w1.shape[1]
    kernel = block_kernel(length, width, hidden, rows)
    clip_spec = pl.BlockSpec((1, length, width), lambda i, c: (i, 0, 0))
    fixed = lambda shape: pl.BlockSpec(shape, lambda i, c: (0, 0))
    grid_spec = pltpu.PrefetchScalarGridSpec(
        num_scalar_prefetch=1,
        grid=(clips,),
        in_specs=[clip_spec, clip_spec, fixed((width, hidden)), fixed((hidden, width)),
                  fixed((8, width)), fixed((8, width)), fixed((8, hidden))],
        out_specs=[clip_spec, clip_spec,
                   pl.BlockSpec(memory_space=pl.ANY), pl.BlockSpec(memory_space=pl.ANY),
                   fixed((8, width)), fixed((8, width)), fixed((8, hidden))],
        scratch_shapes=[
            pltpu.VMEM(((length + 2 * PAD) * (width // LANE), LANE), F32),
            pltpu.VMEM((length, width), F32),
            pltpu.VMEM((length, 1), F32),
            pltpu.VMEM((length, width), BF16),
            pltpu.VMEM((length, width), F32),
            pltpu.VMEM(((length + 2 * PAD) * (width // LANE), LANE), F32),
            pltpu.VMEM((width, hidden), F32),
            pltpu.VMEM((hidden, width), F32),
            pltpu.SemaphoreType.DMA((2,)),
        ],
    )
    flops = 12 * clips * length * width * hidden
    cost = pl.CostEstimate(flops=flops, transcendentals=2 * clips * length * hidden,
                           bytes_accessed=clips * length * width * 8 + 4 * width * hidden * 4)
    return pl.pallas_call(
        kernel,
        grid_spec=grid_spec,
        out_shape=[
            jax.ShapeDtypeStruct((clips, length, width), BF16),
            jax.ShapeDtypeStruct((clips, length, width), F32),
            jax.ShapeDtypeStruct((width, hidden), F32),
            jax.ShapeDtypeStruct((hidden, width), F32),
            jax.ShapeDtypeStruct((8, width), F32),
            jax.ShapeDtypeStruct((8, width), F32),
            jax.ShapeDtypeStruct((8, hidden), F32),
        ],
        compiler_params=pltpu.CompilerParams(
            dimension_semantics=("arbitrary",), vmem_limit_bytes=60 * 1024 * 1024),
        cost_estimate=cost,
    )(counts, frames, cotangent, w1, w2, cw8, vec8, b1_8)


def unpack(packed, width, hidden):
    shapes = [(width, hidden), (hidden, width), (TAPS, width), (width,), (width,), (width,), (width,), (width,), (hidden,)]
    pieces = []
    start_at = 0
    for shape in shapes:
        entries = 1
        for extent in shape:
            entries = entries * extent
        pieces.append(packed[start_at : start_at + entries].reshape(shape))
        start_at = start_at + entries
    return (tuple(pieces), start_at)


AXES = ("dp", "fsdp")
LANES = 128


def bit_order(mesh_sizes):
    dp_size, fsdp_size = mesh_sizes
    fsdp_bits = int(math.log2(fsdp_size))
    dp_bits = int(math.log2(dp_size))
    order = [0] + [fsdp_bits + b for b in range(dp_bits)] + list(range(1, fsdp_bits))
    return order, fsdp_bits + dp_bits


def swap_perm(devices, bit):
    return [(i, i ^ (1 << bit)) for i in range(devices)]


def split_orders(order):
    if len(order) < 3:
        return [order]
    other = [order[0], order[2], order[1]] + order[3:]
    return [order, other]


def tree_all_gather(shard, orders, nbits):
    me = lax.axis_index(AXES)
    devices = 1 << nbits
    rows = shard.shape[0]
    cuts = [rows * p // len(orders) for p in range(len(orders) + 1)]
    held = [shard[cuts[p]:cuts[p + 1]] for p in range(len(orders))]
    held_bits = [[] for _ in orders]
    for step in range(nbits):
        for p, order in enumerate(orders):
            bit = order[step]
            other = lax.ppermute(held[p], AXES, swap_perm(devices, bit))
            upper = ((me >> bit) & 1) == 1
            held[p] = jnp.stack([jnp.where(upper, other, held[p]), jnp.where(upper, held[p], other)])
            held_bits[p].insert(0, bit)
    parts = []
    for p in range(len(orders)):
        axes = [held_bits[p].index(b) for b in sorted(held_bits[p], reverse=True)]
        parts.append(jnp.transpose(held[p], axes + [nbits, nbits + 1]).reshape(devices, -1, LANES))
    return jnp.concatenate(parts, axis=1).reshape(devices * rows, LANES)


def tree_reduce_scatter(full, orders, nbits):
    me = lax.axis_index(AXES)
    devices = 1 << nbits
    rows = full.shape[0] // devices
    cuts = [rows * p // len(orders) for p in range(len(orders) + 1)]
    shaped = full.reshape([2] * nbits + [rows, LANES])
    held = [shaped[..., cuts[p]:cuts[p + 1], :] for p in range(len(orders))]
    held_bits = [[nbits - 1 - a for a in range(nbits)] for _ in orders]
    for step in range(nbits):
        for p, order in enumerate(orders):
            bit = order[step]
            axis = held_bits[p].index(bit)
            mine = (me >> bit) & 1
            keep = lax.dynamic_index_in_dim(held[p], mine, axis=axis, keepdims=False)
            send = lax.dynamic_index_in_dim(held[p], 1 - mine, axis=axis, keepdims=False)
            held[p] = keep + lax.ppermute(send, AXES, swap_perm(devices, bit))
            held_bits[p].pop(axis)
    return jnp.concatenate(held, axis=0)


def tree_all_sum(value, order, nbits):
    devices = 1 << nbits
    for bit in reversed(order):
        value = value + lax.ppermute(value, AXES, swap_perm(devices, bit))
    return value


def body(frames, counts, cotangent, master, momentum, average, disc_grads, mesh_sizes=None):
    order, nbits = bit_order(mesh_sizes)
    devices = 1 << nbits
    clips, length, width = frames.shape
    hidden = 3 * width
    rows = clips * length
    local = master.shape[0]
    flat_size = local * devices
    total_frames = jnp.float32(rows * devices)
    rounded = master.astype(BF16).reshape(local // LANES, LANES)
    packed = tree_all_gather(rounded, [o[::-1] for o in split_orders(order)], nbits).reshape(-1)
    (w_one, w_two, conv_w, conv_b, ln_g, ln_b, b_two, gamma, b_one), used = unpack(packed, width, hidden)
    cw8 = jnp.zeros((8, width), F32).at[:TAPS].set(conv_w.astype(F32))
    vec8 = jnp.concatenate(
        [jnp.stack([conv_b, ln_g, ln_b, b_two, gamma]).astype(F32), jnp.zeros((3, width), F32)])
    b1_8 = jnp.zeros((8, hidden), F32).at[0].set(b_one.astype(F32))
    block_out, input_grad, g_w1, g_w2, gcw, gvec, gb1 = fused_block(
        frames, counts, cotangent, w_one, w_two, cw8, vec8, b1_8)
    small = jnp.concatenate(
        [gcw[:TAPS].reshape(-1), gvec[0], gvec[1], gvec[2], gvec[3], gvec[4], gb1[0]]
    )
    grad_full = jnp.concatenate(
        [
            g_w1.reshape(-1, LANES),
            g_w2.reshape(-1, LANES),
            small.reshape(-1, LANES),
            jnp.zeros(((flat_size - used) // LANES, LANES), F32),
        ]
    )
    grad_shard = tree_reduce_scatter(grad_full, split_orders(order), nbits)
    disc_rows = jnp.sum((disc_grads * disc_grads).reshape(-1, LANES), axis=0, keepdims=True)
    own_rows = jnp.sum(grad_shard * grad_shard, axis=0, keepdims=True)
    squares = jnp.broadcast_to(own_rows + disc_rows, (8, LANES))
    squares = tree_all_sum(squares, order, nbits)
    grad_norm = jnp.sqrt(jnp.sum(squares[0]))
    grad_shard = grad_shard.reshape(-1)
    clipped = grad_shard * jnp.minimum(1.0, 20.0 * jnp.sqrt(total_frames) / (grad_norm + 1e-06))
    new_momentum = 0.9 * momentum + clipped
    new_master = master - (clipped + 0.9 * new_momentum) / jnp.sqrt(total_frames)
    new_average = 0.99 * average + 0.01 * new_master
    return (
        block_out,
        input_grad,
        grad_norm,
        new_master,
        new_momentum,
        new_average,
        new_master.astype(BF16),
        new_average.astype(BF16),
    )


def solution(mesh):
    clip_spec = P(("dp", "fsdp"), None, None)
    flat_spec = P(("dp", "fsdp"))
    mesh_sizes = (mesh.shape["dp"], mesh.shape["fsdp"])
    return jax.shard_map(
        functools.partial(body, mesh_sizes=mesh_sizes),
        mesh=mesh,
        in_specs=(clip_spec, flat_spec, clip_spec, flat_spec, flat_spec, flat_spec, flat_spec),
        out_specs=(clip_spec, clip_spec, P(), flat_spec, flat_spec, flat_spec, flat_spec, flat_spec),
        check_vma=False,
    )
```

```python
import functools
import math

import jax
import jax.numpy as jnp
from jax import lax
from jax.experimental import pallas as pl
from jax.experimental.pallas import tpu as pltpu
from jax.sharding import PartitionSpec as P

F32 = jnp.float32
BF16 = jnp.bfloat16
TAPS = 7
HALF = TAPS // 2
PAD = 8
LANE = 128


def tdot(x, y):
    return lax.dot_general(x, y, (((0,), (0,)), ((), ())), preferred_element_type=F32)


def ntdot(x, y):
    return lax.dot_general(x, y, (((1,), (1,)), ((), ())), preferred_element_type=F32)


def block_kernel(length, width, hidden, rows, flat_rows):
    nblk = length // rows
    quads = width // LANE
    inv_w = 1.0 / width
    sqrt_half = math.sqrt(0.5)
    inv_sqrt_2pi = 1.0 / math.sqrt(2.0 * math.pi)

    def kernel(counts_ref, fr_ref, cot_ref, w1_ref, w2_ref, cw_ref, vec_ref, b1_ref,
               bo_ref, ig_ref, gflat_hbm, gcw_ref, gvec_ref, gb1_ref,
               xq, xhat_s, rstd_s, a_s, da_s, dq, gw1_s, gw2_s, flat_s, sems):
        clip = pl.program_id(0)
        count = counts_ref[clip]

        @pl.when(clip == 0)
        def _init():
            gw1_s[...] = jnp.zeros_like(gw1_s)
            gw2_s[...] = jnp.zeros_like(gw2_s)
            gcw_ref[...] = jnp.zeros_like(gcw_ref)
            gvec_ref[...] = jnp.zeros_like(gvec_ref)
            gb1_ref[...] = jnp.zeros_like(gb1_ref)
            xq[0:PAD * quads, :] = jnp.zeros((PAD * quads, LANE), F32)
            xq[(PAD + length) * quads:, :] = jnp.zeros((PAD * quads, LANE), F32)
            dq[0:PAD * quads, :] = jnp.zeros((PAD * quads, LANE), F32)
            dq[(PAD + length) * quads:, :] = jnp.zeros((PAD * quads, LANE), F32)

        cw = cw_ref[...]
        conv_b = vec_ref[0:1, :]
        ln_g = vec_ref[1:2, :]
        ln_b = vec_ref[2:3, :]
        b_two = vec_ref[3:4, :]
        gamma = vec_ref[4:5, :]
        b_one = b1_ref[0:1, :]

        all_rows = lax.broadcasted_iota(jnp.int32, (length, 1), 0)
        xm_all = jnp.where(all_rows < count, fr_ref[0].astype(F32), 0.0)
        for q in range(quads):
            xq[pl.ds(PAD * quads + q, length, stride=quads), :] = xm_all[:, q * LANE:(q + 1) * LANE]

        def taps_of(buf, start):
            return jnp.concatenate(
                [buf[pl.ds(start * quads + q, rows, stride=quads), :] for q in range(quads)], axis=1)

        for b in range(nblk):
            r0 = b * rows

            @pl.when(r0 < count)
            def _fwd_block():
                base = PAD + r0 - HALF
                conv = conv_b + cw[0:1, :] * taps_of(xq, base)
                for k in range(1, TAPS):
                    conv = conv + cw[k:k + 1, :] * taps_of(xq, base + k)
                centre = jnp.sum(conv, axis=-1, keepdims=True) * inv_w
                shifted = conv - centre
                spread = jnp.sum(shifted * shifted, axis=-1, keepdims=True) * inv_w
                rstd = lax.rsqrt(spread + 1e-6)
                xhat = shifted * rstd
                xhat_s[r0:r0 + rows, :] = xhat
                rstd_s[r0:r0 + rows, :] = rstd
                a_s[r0:r0 + rows, :] = (xhat * ln_g + ln_b).astype(BF16)

        bo_ref[...] = jnp.zeros_like(bo_ref)

        def chunk(c, carry):
            g_gamma, g_b2, g_b1 = carry
            r0 = pl.multiple_of(c * rows, rows)
            a = a_s[pl.ds(r0, rows), :]
            h1 = jnp.dot(a, w1_ref[...], preferred_element_type=F32) + b_one
            cdf = 0.5 * (1.0 + lax.erf(h1 * sqrt_half))
            hh = (h1 * cdf).astype(BF16)
            z = jnp.dot(hh, w2_ref[...], preferred_element_type=F32) + b_two
            live = (r0 + lax.broadcasted_iota(jnp.int32, (rows, 1), 0)) < count
            xin = fr_ref[0, pl.ds(r0, rows), :].astype(F32)
            bo_ref[0, pl.ds(r0, rows), :] = jnp.where(live, xin + gamma * z, 0.0).astype(BF16)
            dout = jnp.where(live, cot_ref[0, pl.ds(r0, rows), :].astype(F32), 0.0)
            g_gamma = g_gamma + jnp.sum(dout * z, axis=0, keepdims=True)
            dz = (gamma * dout).astype(BF16)
            g_b2 = g_b2 + jnp.sum(dz.astype(F32), axis=0, keepdims=True)
            gw2_s[...] += tdot(hh, dz)
            dhh = ntdot(dz, w2_ref[...])
            slope = cdf + h1 * (jnp.exp(-0.5 * (h1 * h1)) * inv_sqrt_2pi)
            dh1 = (dhh * slope).astype(BF16)
            g_b1 = g_b1 + jnp.sum(dh1.astype(F32), axis=0, keepdims=True)
            gw1_s[...] += tdot(a, dh1)
            da_s[pl.ds(r0, rows), :] = ntdot(dh1, w1_ref[...])
            return g_gamma, g_b2, g_b1

        nact = (count + rows - 1) // rows
        zero_d = jnp.zeros((1, width), F32)
        g_gamma, g_b2, g_b1 = lax.fori_loop(
            0, nact, chunk, (zero_d, zero_d, jnp.zeros((1, hidden), F32)))

        def dxm_block(b):
            r0 = b * rows
            base = PAD + r0 + HALF
            dxm = cw[0:1, :] * taps_of(dq, base)
            for k in range(1, TAPS):
                dxm = dxm + cw[k:k + 1, :] * taps_of(dq, base - k)
            live = (r0 + lax.broadcasted_iota(jnp.int32, (rows, 1), 0)) < count
            cot = cot_ref[0, r0:r0 + rows, :].astype(F32)
            ig_ref[0, r0:r0 + rows, :] = jnp.where(live, cot + dxm, 0.0)

        sums = [zero_d] * (3 + TAPS)
        for b in range(nblk):
            r0 = b * rows

            def _bwd_block(r0=r0):
                live = (r0 + lax.broadcasted_iota(jnp.int32, (rows, 1), 0)) < count
                da = jnp.where(live, da_s[r0:r0 + rows, :], 0.0)
                xhat = xhat_s[r0:r0 + rows, :]
                rstd = rstd_s[r0:r0 + rows, :]
                dn = da * ln_g
                m1 = jnp.sum(dn, axis=-1, keepdims=True) * inv_w
                m2 = jnp.sum(dn * xhat, axis=-1, keepdims=True) * inv_w
                dconv = jnp.where(live, rstd * (dn - m1 - xhat * m2), 0.0)
                for q in range(quads):
                    dq[pl.ds((PAD + r0) * quads + q, rows, stride=quads), :] = dconv[:, q * LANE:(q + 1) * LANE]
                part = [jnp.sum(dconv, axis=0, keepdims=True),
                        jnp.sum(da * xhat, axis=0, keepdims=True),
                        jnp.sum(da, axis=0, keepdims=True)]
                base = PAD + r0 - HALF
                for k in range(TAPS):
                    part.append(jnp.sum(dconv * taps_of(xq, base + k), axis=0, keepdims=True))
                return part

            active = r0 < count
            part = lax.cond(active, _bwd_block, lambda: [zero_d] * (3 + TAPS))

            @pl.when(jnp.logical_not(active))
            def _idle():
                dq[(PAD + r0) * quads:(PAD + r0 + rows) * quads, :] = jnp.zeros((rows * quads, LANE), F32)
                ig_ref[0, r0:r0 + rows, :] = jnp.zeros((rows, width), F32)

            sums = [s + p for s, p in zip(sums, part)]
            if b >= 1:
                @pl.when((b - 1) * rows < count)
                def _prev(b=b):
                    dxm_block(b - 1)

        @pl.when((nblk - 1) * rows < count)
        def _last():
            dxm_block(nblk - 1)

        gvec_ref[0:1, :] += sums[0]
        gvec_ref[1:2, :] += sums[1]
        gvec_ref[2:3, :] += sums[2]
        gvec_ref[3:4, :] += g_b2
        gvec_ref[4:5, :] += g_gamma
        for k in range(TAPS):
            gcw_ref[k:k + 1, :] += sums[3 + k]
        gb1_ref[0:1, :] += g_b1

        @pl.when(clip == pl.num_programs(0) - 1)
        def _flush():
            per1 = hidden // LANE
            per2 = width // LANE
            for j in range(per1):
                flat_s[pl.ds(j, width, stride=per1), :] = gw1_s[:, j * LANE:(j + 1) * LANE]
            at = width * hidden // LANE
            for j in range(per2):
                flat_s[pl.ds(at + j, hidden, stride=per2), :] = gw2_s[:, j * LANE:(j + 1) * LANE]
            at = 2 * at
            for q in range(per2):
                flat_s[pl.ds(at + q, TAPS, stride=per2), :] = gcw_ref[0:TAPS, q * LANE:(q + 1) * LANE]
            at = at + TAPS * per2
            for q in range(per2):
                flat_s[pl.ds(at + q, 5, stride=per2), :] = gvec_ref[0:5, q * LANE:(q + 1) * LANE]
            at = at + 5 * per2
            for j in range(per1):
                flat_s[at + j:at + j + 1, :] = gb1_ref[0:1, j * LANE:(j + 1) * LANE]
            at = at + per1
            flat_s[at:, :] = jnp.zeros((flat_rows - at, LANE), F32)
            out = pltpu.make_async_copy(flat_s, gflat_hbm, sems.at[0])
            out.start()
            out.wait()

    return kernel


def fused_block(frames, counts, cotangent, w1, w2, cw8, vec8, b1_8, flat_rows, rows=256):
    clips, length, width = frames.shape
    hidden = w1.shape[1]
    kernel = block_kernel(length, width, hidden, rows, flat_rows)
    clip_spec = pl.BlockSpec((1, length, width), lambda i, c: (i, 0, 0))
    fixed = lambda shape: pl.BlockSpec(shape, lambda i, c: (0, 0))
    grid_spec = pltpu.PrefetchScalarGridSpec(
        num_scalar_prefetch=1,
        grid=(clips,),
        in_specs=[clip_spec, clip_spec, fixed((width, hidden)), fixed((hidden, width)),
                  fixed((8, width)), fixed((8, width)), fixed((8, hidden))],
        out_specs=[clip_spec, clip_spec,
                   pl.BlockSpec(memory_space=pl.ANY),
                   fixed((8, width)), fixed((8, width)), fixed((8, hidden))],
        scratch_shapes=[
            pltpu.VMEM(((length + 2 * PAD) * (width // LANE), LANE), F32),
            pltpu.VMEM((length, width), F32),
            pltpu.VMEM((length, 1), F32),
            pltpu.VMEM((length, width), BF16),
            pltpu.VMEM((length, width), F32),
            pltpu.VMEM(((length + 2 * PAD) * (width // LANE), LANE), F32),
            pltpu.VMEM((width, hidden), F32),
            pltpu.VMEM((hidden, width), F32),
            pltpu.VMEM((flat_rows, LANE), F32),
            pltpu.SemaphoreType.DMA((2,)),
        ],
    )
    flops = 12 * clips * length * width * hidden
    cost = pl.CostEstimate(flops=flops, transcendentals=2 * clips * length * hidden,
                           bytes_accessed=clips * length * width * 8 + 4 * width * hidden * 4)
    return pl.pallas_call(
        kernel,
        grid_spec=grid_spec,
        out_shape=[
            jax.ShapeDtypeStruct((clips, length, width), BF16),
            jax.ShapeDtypeStruct((clips, length, width), F32),
            jax.ShapeDtypeStruct((flat_rows, LANE), F32),
            jax.ShapeDtypeStruct((8, width), F32),
            jax.ShapeDtypeStruct((8, width), F32),
            jax.ShapeDtypeStruct((8, hidden), F32),
        ],
        compiler_params=pltpu.CompilerParams(
            dimension_semantics=("arbitrary",), vmem_limit_bytes=60 * 1024 * 1024),
        cost_estimate=cost,
    )(counts, frames, cotangent, w1, w2, cw8, vec8, b1_8)


def unpack(packed, width, hidden):
    shapes = [(width, hidden), (hidden, width), (TAPS, width), (width,), (width,), (width,), (width,), (width,), (hidden,)]
    pieces = []
    start_at = 0
    for shape in shapes:
        entries = 1
        for extent in shape:
            entries = entries * extent
        pieces.append(packed[start_at : start_at + entries].reshape(shape))
        start_at = start_at + entries
    return (tuple(pieces), start_at)


AXES = ("dp", "fsdp")
LANES = 128


def bit_order(mesh_sizes):
    dp_size, fsdp_size = mesh_sizes
    fsdp_bits = int(math.log2(fsdp_size))
    dp_bits = int(math.log2(dp_size))
    order = [0] + [fsdp_bits + b for b in range(dp_bits)] + list(range(1, fsdp_bits))
    return order, fsdp_bits + dp_bits


def swap_perm(devices, bit):
    return [(i, i ^ (1 << bit)) for i in range(devices)]


def split_orders(order):
    if len(order) < 3:
        return [order]
    other = [order[0], order[2], order[1]] + order[3:]
    return [order, other]


def tree_all_gather(shard, orders, nbits):
    me = lax.axis_index(AXES)
    devices = 1 << nbits
    rows = shard.shape[0]
    cuts = [rows * p // len(orders) for p in range(len(orders) + 1)]
    held = [shard[cuts[p]:cuts[p + 1]] for p in range(len(orders))]
    held_bits = [[] for _ in orders]
    for step in range(nbits):
        for p, order in enumerate(orders):
            bit = order[step]
            other = lax.ppermute(held[p], AXES, swap_perm(devices, bit))
            upper = ((me >> bit) & 1) == 1
            held[p] = jnp.stack([jnp.where(upper, other, held[p]), jnp.where(upper, held[p], other)])
            held_bits[p].insert(0, bit)
    parts = []
    for p in range(len(orders)):
        axes = [held_bits[p].index(b) for b in sorted(held_bits[p], reverse=True)]
        parts.append(jnp.transpose(held[p], axes + [nbits, nbits + 1]).reshape(devices, -1, LANES))
    return jnp.concatenate(parts, axis=1).reshape(devices * rows, LANES)


def tree_reduce_scatter(full, orders, nbits):
    me = lax.axis_index(AXES)
    devices = 1 << nbits
    rows = full.shape[0] // devices
    cuts = [rows * p // len(orders) for p in range(len(orders) + 1)]
    if rows % 8 == 0:
        cuts = [c // 8 * 8 for c in cuts]
    shaped = full.reshape([2] * nbits + [rows, LANES])
    held = [shaped[..., cuts[p]:cuts[p + 1], :] for p in range(len(orders))]
    held_bits = [[nbits - 1 - a for a in range(nbits)] for _ in orders]
    for step in range(nbits):
        for p, order in enumerate(orders):
            bit = order[step]
            axis = held_bits[p].index(bit)
            mine = (me >> bit) & 1
            keep = lax.dynamic_index_in_dim(held[p], mine, axis=axis, keepdims=False)
            send = lax.dynamic_index_in_dim(held[p], 1 - mine, axis=axis, keepdims=False)
            held[p] = keep + lax.ppermute(send, AXES, swap_perm(devices, bit))
            held_bits[p].pop(axis)
    return jnp.concatenate(held, axis=0)


def tree_all_sum(value, order, nbits):
    devices = 1 << nbits
    for bit in reversed(order):
        value = value + lax.ppermute(value, AXES, swap_perm(devices, bit))
    return value


def body(frames, counts, cotangent, master, momentum, average, disc_grads, mesh_sizes=None):
    order, nbits = bit_order(mesh_sizes)
    devices = 1 << nbits
    clips, length, width = frames.shape
    hidden = 3 * width
    rows = clips * length
    local = master.shape[0]
    flat_size = local * devices
    total_frames = jnp.float32(rows * devices)
    rounded = master.astype(BF16).reshape(local // LANES, LANES)
    packed = tree_all_gather(rounded, [o[::-1] for o in split_orders(order)], nbits).reshape(-1)
    (w_one, w_two, conv_w, conv_b, ln_g, ln_b, b_two, gamma, b_one), used = unpack(packed, width, hidden)
    cw8 = jnp.zeros((8, width), F32).at[:TAPS].set(conv_w.astype(F32))
    vec8 = jnp.concatenate(
        [jnp.stack([conv_b, ln_g, ln_b, b_two, gamma]).astype(F32), jnp.zeros((3, width), F32)])
    b1_8 = jnp.zeros((8, hidden), F32).at[0].set(b_one.astype(F32))
    shard_rows = local // LANES
    padded_rows = -(-shard_rows // 8) * 8
    aligned = padded_rows != shard_rows and (padded_rows - shard_rows) * (devices - 1) <= padded_rows
    block = padded_rows if aligned else shard_rows
    block_out, input_grad, grad_full, _, _, _ = fused_block(
        frames, counts, cotangent, w_one, w_two, cw8, vec8, b1_8, devices * block)
    grad_block = tree_reduce_scatter(grad_full, split_orders(order), nbits)
    if aligned:
        me = lax.axis_index(AXES)
        prev = lax.ppermute(grad_block, AXES, [(i, (i + 1) % devices) for i in range(devices)])
        both = jnp.concatenate([prev, grad_block])
        grad_shard = lax.dynamic_slice_in_dim(both, block - (block - shard_rows) * me, shard_rows, axis=0)
    else:
        grad_shard = grad_block
    disc_rows = jnp.sum((disc_grads * disc_grads).reshape(-1, LANES), axis=0, keepdims=True)
    own_rows = jnp.sum(grad_shard * grad_shard, axis=0, keepdims=True)
    squares = jnp.broadcast_to(own_rows + disc_rows, (8, LANES))
    squares = tree_all_sum(squares, order, nbits)
    grad_norm = jnp.sqrt(jnp.sum(squares[0]))
    grad_shard = grad_shard.reshape(-1)
    clipped = grad_shard * jnp.minimum(1.0, 20.0 * jnp.sqrt(total_frames) / (grad_norm + 1e-06))
    new_momentum = 0.9 * momentum + clipped
    new_master = master - (clipped + 0.9 * new_momentum) / jnp.sqrt(total_frames)
    new_average = 0.99 * average + 0.01 * new_master
    return (
        block_out,
        input_grad,
        grad_norm,
        new_master,
        new_momentum,
        new_average,
        new_master.astype(BF16),
        new_average.astype(BF16),
    )


def solution(mesh):
    clip_spec = P(("dp", "fsdp"), None, None)
    flat_spec = P(("dp", "fsdp"))
    mesh_sizes = (mesh.shape["dp"], mesh.shape["fsdp"])
    return jax.shard_map(
        functools.partial(body, mesh_sizes=mesh_sizes),
        mesh=mesh,
        in_specs=(clip_spec, flat_spec, clip_spec, flat_spec, flat_spec, flat_spec, flat_spec),
        out_specs=(clip_spec, clip_spec, P(), flat_spec, flat_spec, flat_spec, flat_spec, flat_spec),
        check_vma=False,
    )
```

```python
import functools
import math

import jax
import jax.numpy as jnp
from jax import lax
from jax.experimental import pallas as pl
from jax.experimental.pallas import tpu as pltpu
from jax.sharding import PartitionSpec as P

F32 = jnp.float32
BF16 = jnp.bfloat16
TAPS = 7
HALF = TAPS // 2
PAD = 8
LANE = 128


def tdot(x, y):
    return lax.dot_general(x, y, (((0,), (0,)), ((), ())), preferred_element_type=F32)


def ntdot(x, y):
    return lax.dot_general(x, y, (((1,), (1,)), ((), ())), preferred_element_type=F32)


def block_kernel(length, width, hidden, rows, flat_rows):
    nblk = length // rows
    quads = width // LANE
    inv_w = 1.0 / width
    sqrt_half = math.sqrt(0.5)
    inv_sqrt_2pi = 1.0 / math.sqrt(2.0 * math.pi)

    def kernel(counts_ref, fr_ref, cot_ref, w1_ref, w2_ref, cw_ref, vec_ref, b1_ref,
               bo_ref, ig_ref, gflat_hbm, gcw_ref, gvec_ref, gb1_ref,
               xq, xhat_s, rstd_s, a_s, da_s, dq, gw1_s, gw2_s, flat_s, sems):
        clip = pl.program_id(0)
        count = counts_ref[clip]

        @pl.when(clip == 0)
        def _init():
            gw1_s[...] = jnp.zeros_like(gw1_s)
            gw2_s[...] = jnp.zeros_like(gw2_s)
            gcw_ref[...] = jnp.zeros_like(gcw_ref)
            gvec_ref[...] = jnp.zeros_like(gvec_ref)
            gb1_ref[...] = jnp.zeros_like(gb1_ref)
            xq[0:PAD * quads, :] = jnp.zeros((PAD * quads, LANE), F32)
            xq[(PAD + length) * quads:, :] = jnp.zeros((PAD * quads, LANE), F32)
            dq[0:PAD * quads, :] = jnp.zeros((PAD * quads, LANE), F32)
            dq[(PAD + length) * quads:, :] = jnp.zeros((PAD * quads, LANE), F32)

        cw = cw_ref[...]
        conv_b = vec_ref[0:1, :]
        ln_g = vec_ref[1:2, :]
        ln_b = vec_ref[2:3, :]
        b_two = vec_ref[3:4, :]
        gamma = vec_ref[4:5, :]
        b_one = b1_ref[0:1, :]

        all_rows = lax.broadcasted_iota(jnp.int32, (length, 1), 0)
        xm_all = jnp.where(all_rows < count, fr_ref[0].astype(F32), 0.0)
        for q in range(quads):
            xq[pl.ds(PAD * quads + q, length, stride=quads), :] = xm_all[:, q * LANE:(q + 1) * LANE]

        def taps_of(buf, start):
            return jnp.concatenate(
                [buf[pl.ds(start * quads + q, rows, stride=quads), :] for q in range(quads)], axis=1)

        for b in range(nblk):
            r0 = b * rows

            @pl.when(r0 < count)
            def _fwd_block():
                base = PAD + r0 - HALF
                conv = conv_b + cw[0:1, :] * taps_of(xq, base)
                for k in range(1, TAPS):
                    conv = conv + cw[k:k + 1, :] * taps_of(xq, base + k)
                centre = jnp.sum(conv, axis=-1, keepdims=True) * inv_w
                shifted = conv - centre
                spread = jnp.sum(shifted * shifted, axis=-1, keepdims=True) * inv_w
                rstd = lax.rsqrt(spread + 1e-6)
                xhat = shifted * rstd
                xhat_s[r0:r0 + rows, :] = xhat
                rstd_s[r0:r0 + rows, :] = rstd
                a_s[r0:r0 + rows, :] = (xhat * ln_g + ln_b).astype(BF16)

        bo_ref[...] = jnp.zeros_like(bo_ref)

        def chunk(c, carry):
            g_gamma, g_b2, g_b1 = carry
            r0 = pl.multiple_of(c * rows, rows)
            a = a_s[pl.ds(r0, rows), :]
            h1 = jnp.dot(a, w1_ref[...], preferred_element_type=F32) + b_one
            cdf = 0.5 * (1.0 + lax.erf(h1 * sqrt_half))
            hh = (h1 * cdf).astype(BF16)
            z = jnp.dot(hh, w2_ref[...], preferred_element_type=F32) + b_two
            live = (r0 + lax.broadcasted_iota(jnp.int32, (rows, 1), 0)) < count
            xin = fr_ref[0, pl.ds(r0, rows), :].astype(F32)
            bo_ref[0, pl.ds(r0, rows), :] = jnp.where(live, xin + gamma * z, 0.0).astype(BF16)
            dout = jnp.where(live, cot_ref[0, pl.ds(r0, rows), :].astype(F32), 0.0)
            g_gamma = g_gamma + jnp.sum(dout * z, axis=0, keepdims=True)
            dz = (gamma * dout).astype(BF16)
            g_b2 = g_b2 + jnp.sum(dz.astype(F32), axis=0, keepdims=True)
            gw2_s[...] += tdot(hh, dz)
            dhh = ntdot(dz, w2_ref[...])
            slope = cdf + h1 * (jnp.exp(-0.5 * (h1 * h1)) * inv_sqrt_2pi)
            dh1 = (dhh * slope).astype(BF16)
            g_b1 = g_b1 + jnp.sum(dh1.astype(F32), axis=0, keepdims=True)
            gw1_s[...] += tdot(a, dh1)
            da_s[pl.ds(r0, rows), :] = ntdot(dh1, w1_ref[...])
            return g_gamma, g_b2, g_b1

        nact = (count + rows - 1) // rows
        zero_d = jnp.zeros((1, width), F32)
        g_gamma, g_b2, g_b1 = lax.fori_loop(
            0, nact, chunk, (zero_d, zero_d, jnp.zeros((1, hidden), F32)))

        def dxm_block(b):
            r0 = b * rows
            base = PAD + r0 + HALF
            dxm = cw[0:1, :] * taps_of(dq, base)
            for k in range(1, TAPS):
                dxm = dxm + cw[k:k + 1, :] * taps_of(dq, base - k)
            live = (r0 + lax.broadcasted_iota(jnp.int32, (rows, 1), 0)) < count
            cot = cot_ref[0, r0:r0 + rows, :].astype(F32)
            ig_ref[0, r0:r0 + rows, :] = jnp.where(live, cot + dxm, 0.0)

        sums = [zero_d] * (3 + TAPS)
        for b in range(nblk):
            r0 = b * rows

            def _bwd_block(r0=r0):
                live = (r0 + lax.broadcasted_iota(jnp.int32, (rows, 1), 0)) < count
                da = jnp.where(live, da_s[r0:r0 + rows, :], 0.0)
                xhat = xhat_s[r0:r0 + rows, :]
                rstd = rstd_s[r0:r0 + rows, :]
                dn = da * ln_g
                m1 = jnp.sum(dn, axis=-1, keepdims=True) * inv_w
                m2 = jnp.sum(dn * xhat, axis=-1, keepdims=True) * inv_w
                dconv = jnp.where(live, rstd * (dn - m1 - xhat * m2), 0.0)
                for q in range(quads):
                    dq[pl.ds((PAD + r0) * quads + q, rows, stride=quads), :] = dconv[:, q * LANE:(q + 1) * LANE]
                part = [jnp.sum(dconv, axis=0, keepdims=True),
                        jnp.sum(da * xhat, axis=0, keepdims=True),
                        jnp.sum(da, axis=0, keepdims=True)]
                base = PAD + r0 - HALF
                for k in range(TAPS):
                    part.append(jnp.sum(dconv * taps_of(xq, base + k), axis=0, keepdims=True))
                return part

            active = r0 < count
            part = lax.cond(active, _bwd_block, lambda: [zero_d] * (3 + TAPS))

            @pl.when(jnp.logical_not(active))
            def _idle():
                dq[(PAD + r0) * quads:(PAD + r0 + rows) * quads, :] = jnp.zeros((rows * quads, LANE), F32)
                ig_ref[0, r0:r0 + rows, :] = jnp.zeros((rows, width), F32)

            sums = [s + p for s, p in zip(sums, part)]
            if b >= 1:
                @pl.when((b - 1) * rows < count)
                def _prev(b=b):
                    dxm_block(b - 1)

        @pl.when((nblk - 1) * rows < count)
        def _last():
            dxm_block(nblk - 1)

        gvec_ref[0:1, :] += sums[0]
        gvec_ref[1:2, :] += sums[1]
        gvec_ref[2:3, :] += sums[2]
        gvec_ref[3:4, :] += g_b2
        gvec_ref[4:5, :] += g_gamma
        for k in range(TAPS):
            gcw_ref[k:k + 1, :] += sums[3 + k]
        gb1_ref[0:1, :] += g_b1

        @pl.when(clip == pl.num_programs(0) - 1)
        def _flush():
            per1 = hidden // LANE
            per2 = width // LANE
            for j in range(per1):
                flat_s[pl.ds(j, width, stride=per1), :] = gw1_s[:, j * LANE:(j + 1) * LANE]
            at = width * hidden // LANE
            for j in range(per2):
                flat_s[pl.ds(at + j, hidden, stride=per2), :] = gw2_s[:, j * LANE:(j + 1) * LANE]
            at = 2 * at
            for q in range(per2):
                flat_s[pl.ds(at + q, TAPS, stride=per2), :] = gcw_ref[0:TAPS, q * LANE:(q + 1) * LANE]
            at = at + TAPS * per2
            for q in range(per2):
                flat_s[pl.ds(at + q, 5, stride=per2), :] = gvec_ref[0:5, q * LANE:(q + 1) * LANE]
            at = at + 5 * per2
            for j in range(per1):
                flat_s[at + j:at + j + 1, :] = gb1_ref[0:1, j * LANE:(j + 1) * LANE]
            at = at + per1
            flat_s[at:, :] = jnp.zeros((flat_rows - at, LANE), F32)
            out = pltpu.make_async_copy(flat_s, gflat_hbm, sems.at[0])
            out.start()
            out.wait()

    return kernel


def fused_block(frames, counts, cotangent, w1, w2, cw8, vec8, b1_8, flat_rows, rows=256):
    clips, length, width = frames.shape
    hidden = w1.shape[1]
    kernel = block_kernel(length, width, hidden, rows, flat_rows)
    clip_spec = pl.BlockSpec((1, length, width), lambda i, c: (i, 0, 0))
    fixed = lambda shape: pl.BlockSpec(shape, lambda i, c: (0, 0))
    grid_spec = pltpu.PrefetchScalarGridSpec(
        num_scalar_prefetch=1,
        grid=(clips,),
        in_specs=[clip_spec, clip_spec, fixed((width, hidden)), fixed((hidden, width)),
                  fixed((8, width)), fixed((8, width)), fixed((8, hidden))],
        out_specs=[clip_spec, clip_spec,
                   pl.BlockSpec(memory_space=pl.ANY),
                   fixed((8, width)), fixed((8, width)), fixed((8, hidden))],
        scratch_shapes=[
            pltpu.VMEM(((length + 2 * PAD) * (width // LANE), LANE), F32),
            pltpu.VMEM((length, width), F32),
            pltpu.VMEM((length, 1), F32),
            pltpu.VMEM((length, width), BF16),
            pltpu.VMEM((length, width), F32),
            pltpu.VMEM(((length + 2 * PAD) * (width // LANE), LANE), F32),
            pltpu.VMEM((width, hidden), F32),
            pltpu.VMEM((hidden, width), F32),
            pltpu.VMEM((flat_rows, LANE), F32),
            pltpu.SemaphoreType.DMA((2,)),
        ],
    )
    flops = 12 * clips * length * width * hidden
    cost = pl.CostEstimate(flops=flops, transcendentals=2 * clips * length * hidden,
                           bytes_accessed=clips * length * width * 8 + 4 * width * hidden * 4)
    return pl.pallas_call(
        kernel,
        grid_spec=grid_spec,
        out_shape=[
            jax.ShapeDtypeStruct((clips, length, width), BF16),
            jax.ShapeDtypeStruct((clips, length, width), F32),
            jax.ShapeDtypeStruct((flat_rows, LANE), F32),
            jax.ShapeDtypeStruct((8, width), F32),
            jax.ShapeDtypeStruct((8, width), F32),
            jax.ShapeDtypeStruct((8, hidden), F32),
        ],
        compiler_params=pltpu.CompilerParams(
            dimension_semantics=("arbitrary",), vmem_limit_bytes=60 * 1024 * 1024),
        cost_estimate=cost,
    )(counts, frames, cotangent, w1, w2, cw8, vec8, b1_8)


def unpack(packed, width, hidden):
    shapes = [(width, hidden), (hidden, width), (TAPS, width), (width,), (width,), (width,), (width,), (width,), (hidden,)]
    pieces = []
    start_at = 0
    for shape in shapes:
        entries = 1
        for extent in shape:
            entries = entries * extent
        pieces.append(packed[start_at : start_at + entries].reshape(shape))
        start_at = start_at + entries
    return (tuple(pieces), start_at)


AXES = ("dp", "fsdp")
LANES = 128


def bit_order(mesh_sizes):
    dp_size, fsdp_size = mesh_sizes
    fsdp_bits = int(math.log2(fsdp_size))
    dp_bits = int(math.log2(dp_size))
    order = [0] + [fsdp_bits + b for b in range(dp_bits)] + list(range(1, fsdp_bits))
    return order, fsdp_bits + dp_bits


def swap_perm(devices, bit):
    return [(i, i ^ (1 << bit)) for i in range(devices)]


def split_orders(order):
    if len(order) < 3:
        return [order]
    other = [order[0], order[2], order[1]] + order[3:]
    return [order, other]


def tree_all_gather(shard, orders, nbits):
    me = lax.axis_index(AXES)
    devices = 1 << nbits
    rows = shard.shape[0]
    cuts = [rows * p // len(orders) for p in range(len(orders) + 1)]
    held = [shard[cuts[p]:cuts[p + 1]] for p in range(len(orders))]
    held_bits = [[] for _ in orders]
    for step in range(nbits):
        for p, order in enumerate(orders):
            bit = order[step]
            other = lax.ppermute(held[p], AXES, swap_perm(devices, bit))
            upper = ((me >> bit) & 1) == 1
            held[p] = jnp.stack([jnp.where(upper, other, held[p]), jnp.where(upper, held[p], other)])
            held_bits[p].insert(0, bit)
    parts = []
    for p in range(len(orders)):
        axes = [held_bits[p].index(b) for b in sorted(held_bits[p], reverse=True)]
        parts.append(jnp.transpose(held[p], axes + [nbits, nbits + 1]).reshape(devices, -1, LANES))
    return jnp.concatenate(parts, axis=1).reshape(devices * rows, LANES)


def tree_reduce_scatter(full, orders, nbits):
    me = lax.axis_index(AXES)
    devices = 1 << nbits
    rows = full.shape[0] // devices
    cuts = [rows * p // len(orders) for p in range(len(orders) + 1)]
    if rows % 8 == 0:
        cuts = [c // 8 * 8 for c in cuts]
    shaped = full.reshape([2] * nbits + [rows, LANES])
    held = [shaped[..., cuts[p]:cuts[p + 1], :] for p in range(len(orders))]
    held_bits = [[nbits - 1 - a for a in range(nbits)] for _ in orders]
    for step in range(nbits):
        for p, order in enumerate(orders):
            bit = order[step]
            axis = held_bits[p].index(bit)
            mine = (me >> bit) & 1
            keep = lax.dynamic_index_in_dim(held[p], mine, axis=axis, keepdims=False)
            send = lax.dynamic_index_in_dim(held[p], 1 - mine, axis=axis, keepdims=False)
            held[p] = keep + lax.ppermute(send, AXES, swap_perm(devices, bit))
            held_bits[p].pop(axis)
    return jnp.concatenate(held, axis=0)


def tree_all_sum(value, order, nbits, group=3):
    me = lax.axis_index(AXES)
    devices = 1 << nbits
    for g0 in range(0, len(order), group):
        bits = order[g0:g0 + group]
        got = []
        for m in range(1 << len(bits)):
            mask = sum(1 << b for i, b in enumerate(bits) if (m >> i) & 1)
            got.append(value if mask == 0 else lax.ppermute(value, AXES, [(i, i ^ mask) for i in range(devices)]))
        got = jnp.stack(got)
        mine = sum(((me >> b) & 1) << i for i, b in enumerate(bits))
        total = None
        for p in range(1 << len(bits)):
            term = lax.dynamic_index_in_dim(got, mine ^ p, axis=0, keepdims=False)
            total = term if total is None else total + term
        value = total
    return value


def body(frames, counts, cotangent, master, momentum, average, disc_grads, mesh_sizes=None):
    order, nbits = bit_order(mesh_sizes)
    devices = 1 << nbits
    clips, length, width = frames.shape
    hidden = 3 * width
    rows = clips * length
    local = master.shape[0]
    flat_size = local * devices
    total_frames = jnp.float32(rows * devices)
    rounded = master.astype(BF16).reshape(local // LANES, LANES)
    packed = tree_all_gather(rounded, [o[::-1] for o in split_orders(order)], nbits).reshape(-1)
    (w_one, w_two, conv_w, conv_b, ln_g, ln_b, b_two, gamma, b_one), used = unpack(packed, width, hidden)
    cw8 = jnp.zeros((8, width), F32).at[:TAPS].set(conv_w.astype(F32))
    vec8 = jnp.concatenate(
        [jnp.stack([conv_b, ln_g, ln_b, b_two, gamma]).astype(F32), jnp.zeros((3, width), F32)])
    b1_8 = jnp.zeros((8, hidden), F32).at[0].set(b_one.astype(F32))
    shard_rows = local // LANES
    padded_rows = -(-shard_rows // 8) * 8
    aligned = padded_rows != shard_rows and (padded_rows - shard_rows) * (devices - 1) <= padded_rows
    block = padded_rows if aligned else shard_rows
    block_out, input_grad, grad_full, _, _, _ = fused_block(
        frames, counts, cotangent, w_one, w_two, cw8, vec8, b1_8, devices * block)
    grad_block = tree_reduce_scatter(grad_full, split_orders(order), nbits)
    if aligned:
        me = lax.axis_index(AXES)
        prev = lax.ppermute(grad_block, AXES, [(i, (i + 1) % devices) for i in range(devices)])
        both = jnp.concatenate([prev, grad_block])
        grad_shard = lax.dynamic_slice_in_dim(both, block - (block - shard_rows) * me, shard_rows, axis=0)
    else:
        grad_shard = grad_block
    disc_rows = jnp.sum((disc_grads * disc_grads).reshape(-1, LANES), axis=0, keepdims=True)
    own_rows = jnp.sum(grad_shard * grad_shard, axis=0, keepdims=True)
    squares = jnp.broadcast_to(own_rows + disc_rows, (8, LANES))
    squares = tree_all_sum(squares, order, nbits)
    grad_norm = jnp.sqrt(jnp.sum(squares[0]))
    grad_shard = grad_shard.reshape(-1)
    clipped = grad_shard * jnp.minimum(1.0, 20.0 * jnp.sqrt(total_frames) / (grad_norm + 1e-06))
    new_momentum = 0.9 * momentum + clipped
    new_master = master - (clipped + 0.9 * new_momentum) / jnp.sqrt(total_frames)
    new_average = 0.99 * average + 0.01 * new_master
    return (
        block_out,
        input_grad,
        grad_norm,
        new_master,
        new_momentum,
        new_average,
        new_master.astype(BF16),
        new_average.astype(BF16),
    )


def solution(mesh):
    clip_spec = P(("dp", "fsdp"), None, None)
    flat_spec = P(("dp", "fsdp"))
    mesh_sizes = (mesh.shape["dp"], mesh.shape["fsdp"])
    return jax.shard_map(
        functools.partial(body, mesh_sizes=mesh_sizes),
        mesh=mesh,
        in_specs=(clip_spec, flat_spec, clip_spec, flat_spec, flat_spec, flat_spec, flat_spec),
        out_specs=(clip_spec, clip_spec, P(), flat_spec, flat_spec, flat_spec, flat_spec, flat_spec),
        check_vma=False,
    )
```

```python
import functools
import math

import jax
import jax.numpy as jnp
from jax import lax
from jax.experimental import pallas as pl
from jax.experimental.pallas import tpu as pltpu
from jax.sharding import PartitionSpec as P

F32 = jnp.float32
BF16 = jnp.bfloat16
TAPS = 7
HALF = TAPS // 2
PAD = 8
LANE = 128


def tdot(x, y):
    return lax.dot_general(x, y, (((0,), (0,)), ((), ())), preferred_element_type=F32)


def ntdot(x, y):
    return lax.dot_general(x, y, (((1,), (1,)), ((), ())), preferred_element_type=F32)


def block_kernel(length, width, hidden, rows, flat_rows):
    nblk = length // rows
    quads = width // LANE
    inv_w = 1.0 / width
    sqrt_half = math.sqrt(0.5)
    inv_sqrt_2pi = 1.0 / math.sqrt(2.0 * math.pi)

    def kernel(counts_ref, fr_ref, cot_ref, wrows_hbm, cw_ref, vec_ref, b1_ref,
               bo_ref, ig_ref, gflat_hbm, gcw_ref, gvec_ref, gb1_ref,
               xq, xhat_s, rstd_s, a_s, da_s, dq, gw1_s, gw2_s, flat_s, wb_s, w1_ref, w2_ref, sems):
        clip = pl.program_id(0)
        count = counts_ref[clip]

        @pl.when(clip == 0)
        def _weights():
            load = pltpu.make_async_copy(wrows_hbm, wb_s, sems.at[1])
            load.start()
            load.wait()
            wide = flat_s.at[0:wb_s.shape[0], :]
            wide[...] = wb_s[...].astype(F32)
            per1 = hidden // LANE
            per2 = width // LANE
            for j in range(per1):
                w1_ref[:, j * LANE:(j + 1) * LANE] = wide[pl.ds(j, width, stride=per1), :].astype(BF16)
            at = width * hidden // LANE
            for j in range(per2):
                w2_ref[:, j * LANE:(j + 1) * LANE] = wide[pl.ds(at + j, hidden, stride=per2), :].astype(BF16)

        @pl.when(clip == 0)
        def _init():
            gw1_s[...] = jnp.zeros_like(gw1_s)
            gw2_s[...] = jnp.zeros_like(gw2_s)
            gcw_ref[...] = jnp.zeros_like(gcw_ref)
            gvec_ref[...] = jnp.zeros_like(gvec_ref)
            gb1_ref[...] = jnp.zeros_like(gb1_ref)
            xq[0:PAD * quads, :] = jnp.zeros((PAD * quads, LANE), F32)
            xq[(PAD + length) * quads:, :] = jnp.zeros((PAD * quads, LANE), F32)
            dq[0:PAD * quads, :] = jnp.zeros((PAD * quads, LANE), F32)
            dq[(PAD + length) * quads:, :] = jnp.zeros((PAD * quads, LANE), F32)

        cw = cw_ref[...]
        conv_b = vec_ref[0:1, :]
        ln_g = vec_ref[1:2, :]
        ln_b = vec_ref[2:3, :]
        b_two = vec_ref[3:4, :]
        gamma = vec_ref[4:5, :]
        b_one = b1_ref[0:1, :]

        all_rows = lax.broadcasted_iota(jnp.int32, (length, 1), 0)
        xm_all = jnp.where(all_rows < count, fr_ref[0].astype(F32), 0.0)
        for q in range(quads):
            xq[pl.ds(PAD * quads + q, length, stride=quads), :] = xm_all[:, q * LANE:(q + 1) * LANE]

        def taps_of(buf, start):
            return jnp.concatenate(
                [buf[pl.ds(start * quads + q, rows, stride=quads), :] for q in range(quads)], axis=1)

        for b in range(nblk):
            r0 = b * rows

            @pl.when(r0 < count)
            def _fwd_block():
                base = PAD + r0 - HALF
                conv = conv_b + cw[0:1, :] * taps_of(xq, base)
                for k in range(1, TAPS):
                    conv = conv + cw[k:k + 1, :] * taps_of(xq, base + k)
                centre = jnp.sum(conv, axis=-1, keepdims=True) * inv_w
                shifted = conv - centre
                spread = jnp.sum(shifted * shifted, axis=-1, keepdims=True) * inv_w
                rstd = lax.rsqrt(spread + 1e-6)
                xhat = shifted * rstd
                xhat_s[r0:r0 + rows, :] = xhat
                rstd_s[r0:r0 + rows, :] = rstd
                a_s[r0:r0 + rows, :] = (xhat * ln_g + ln_b).astype(BF16)

        bo_ref[...] = jnp.zeros_like(bo_ref)

        def chunk(c, carry):
            g_gamma, g_b2, g_b1 = carry
            r0 = pl.multiple_of(c * rows, rows)
            a = a_s[pl.ds(r0, rows), :]
            h1 = jnp.dot(a, w1_ref[...], preferred_element_type=F32) + b_one
            cdf = 0.5 * (1.0 + lax.erf(h1 * sqrt_half))
            hh = (h1 * cdf).astype(BF16)
            z = jnp.dot(hh, w2_ref[...], preferred_element_type=F32) + b_two
            live = (r0 + lax.broadcasted_iota(jnp.int32, (rows, 1), 0)) < count
            xin = fr_ref[0, pl.ds(r0, rows), :].astype(F32)
            bo_ref[0, pl.ds(r0, rows), :] = jnp.where(live, xin + gamma * z, 0.0).astype(BF16)
            dout = jnp.where(live, cot_ref[0, pl.ds(r0, rows), :].astype(F32), 0.0)
            g_gamma = g_gamma + jnp.sum(dout * z, axis=0, keepdims=True)
            dz = (gamma * dout).astype(BF16)
            g_b2 = g_b2 + jnp.sum(dz.astype(F32), axis=0, keepdims=True)
            gw2_s[...] += tdot(hh, dz)
            dhh = ntdot(dz, w2_ref[...])
            slope = cdf + h1 * (jnp.exp(-0.5 * (h1 * h1)) * inv_sqrt_2pi)
            dh1 = (dhh * slope).astype(BF16)
            g_b1 = g_b1 + jnp.sum(dh1.astype(F32), axis=0, keepdims=True)
            gw1_s[...] += tdot(a, dh1)
            da_s[pl.ds(r0, rows), :] = ntdot(dh1, w1_ref[...])
            return g_gamma, g_b2, g_b1

        nact = (count + rows - 1) // rows
        zero_d = jnp.zeros((1, width), F32)
        g_gamma, g_b2, g_b1 = lax.fori_loop(
            0, nact, chunk, (zero_d, zero_d, jnp.zeros((1, hidden), F32)))

        def dxm_block(b):
            r0 = b * rows
            base = PAD + r0 + HALF
            dxm = cw[0:1, :] * taps_of(dq, base)
            for k in range(1, TAPS):
                dxm = dxm + cw[k:k + 1, :] * taps_of(dq, base - k)
            live = (r0 + lax.broadcasted_iota(jnp.int32, (rows, 1), 0)) < count
            cot = cot_ref[0, r0:r0 + rows, :].astype(F32)
            ig_ref[0, r0:r0 + rows, :] = jnp.where(live, cot + dxm, 0.0)

        sums = [zero_d] * (3 + TAPS)
        for b in range(nblk):
            r0 = b * rows

            def _bwd_block(r0=r0):
                live = (r0 + lax.broadcasted_iota(jnp.int32, (rows, 1), 0)) < count
                da = jnp.where(live, da_s[r0:r0 + rows, :], 0.0)
                xhat = xhat_s[r0:r0 + rows, :]
                rstd = rstd_s[r0:r0 + rows, :]
                dn = da * ln_g
                m1 = jnp.sum(dn, axis=-1, keepdims=True) * inv_w
                m2 = jnp.sum(dn * xhat, axis=-1, keepdims=True) * inv_w
                dconv = jnp.where(live, rstd * (dn - m1 - xhat * m2), 0.0)
                for q in range(quads):
                    dq[pl.ds((PAD + r0) * quads + q, rows, stride=quads), :] = dconv[:, q * LANE:(q + 1) * LANE]
                part = [jnp.sum(dconv, axis=0, keepdims=True),
                        jnp.sum(da * xhat, axis=0, keepdims=True),
                        jnp.sum(da, axis=0, keepdims=True)]
                base = PAD + r0 - HALF
                for k in range(TAPS):
                    part.append(jnp.sum(dconv * taps_of(xq, base + k), axis=0, keepdims=True))
                return part

            active = r0 < count
            part = lax.cond(active, _bwd_block, lambda: [zero_d] * (3 + TAPS))

            @pl.when(jnp.logical_not(active))
            def _idle():
                dq[(PAD + r0) * quads:(PAD + r0 + rows) * quads, :] = jnp.zeros((rows * quads, LANE), F32)
                ig_ref[0, r0:r0 + rows, :] = jnp.zeros((rows, width), F32)

            sums = [s + p for s, p in zip(sums, part)]
            if b >= 1:
                @pl.when((b - 1) * rows < count)
                def _prev(b=b):
                    dxm_block(b - 1)

        @pl.when((nblk - 1) * rows < count)
        def _last():
            dxm_block(nblk - 1)

        gvec_ref[0:1, :] += sums[0]
        gvec_ref[1:2, :] += sums[1]
        gvec_ref[2:3, :] += sums[2]
        gvec_ref[3:4, :] += g_b2
        gvec_ref[4:5, :] += g_gamma
        for k in range(TAPS):
            gcw_ref[k:k + 1, :] += sums[3 + k]
        gb1_ref[0:1, :] += g_b1

        @pl.when(clip == pl.num_programs(0) - 1)
        def _flush():
            per1 = hidden // LANE
            per2 = width // LANE
            for j in range(per1):
                flat_s[pl.ds(j, width, stride=per1), :] = gw1_s[:, j * LANE:(j + 1) * LANE]
            at = width * hidden // LANE
            for j in range(per2):
                flat_s[pl.ds(at + j, hidden, stride=per2), :] = gw2_s[:, j * LANE:(j + 1) * LANE]
            at = 2 * at
            for q in range(per2):
                flat_s[pl.ds(at + q, TAPS, stride=per2), :] = gcw_ref[0:TAPS, q * LANE:(q + 1) * LANE]
            at = at + TAPS * per2
            for q in range(per2):
                flat_s[pl.ds(at + q, 5, stride=per2), :] = gvec_ref[0:5, q * LANE:(q + 1) * LANE]
            at = at + 5 * per2
            for j in range(per1):
                flat_s[at + j:at + j + 1, :] = gb1_ref[0:1, j * LANE:(j + 1) * LANE]
            at = at + per1
            flat_s[at:, :] = jnp.zeros((flat_rows - at, LANE), F32)
            out = pltpu.make_async_copy(flat_s, gflat_hbm, sems.at[0])
            out.start()
            out.wait()

    return kernel


def fused_block(frames, counts, cotangent, wrows, cw8, vec8, b1_8, flat_rows, rows=256):
    clips, length, width = frames.shape
    hidden = cw8.shape[1] * 3
    kernel = block_kernel(length, width, hidden, rows, flat_rows)
    clip_spec = pl.BlockSpec((1, length, width), lambda i, c: (i, 0, 0))
    fixed = lambda shape: pl.BlockSpec(shape, lambda i, c: (0, 0))
    grid_spec = pltpu.PrefetchScalarGridSpec(
        num_scalar_prefetch=1,
        grid=(clips,),
        in_specs=[clip_spec, clip_spec, pl.BlockSpec(memory_space=pl.ANY),
                  fixed((8, width)), fixed((8, width)), fixed((8, hidden))],
        out_specs=[clip_spec, clip_spec,
                   pl.BlockSpec(memory_space=pl.ANY),
                   fixed((8, width)), fixed((8, width)), fixed((8, hidden))],
        scratch_shapes=[
            pltpu.VMEM(((length + 2 * PAD) * (width // LANE), LANE), F32),
            pltpu.VMEM((length, width), F32),
            pltpu.VMEM((length, 1), F32),
            pltpu.VMEM((length, width), BF16),
            pltpu.VMEM((length, width), F32),
            pltpu.VMEM(((length + 2 * PAD) * (width // LANE), LANE), F32),
            pltpu.VMEM((width, hidden), F32),
            pltpu.VMEM((hidden, width), F32),
            pltpu.VMEM((flat_rows, LANE), F32),
            pltpu.VMEM(wrows.shape, BF16),
            pltpu.VMEM((width, hidden), BF16),
            pltpu.VMEM((hidden, width), BF16),
            pltpu.SemaphoreType.DMA((2,)),
        ],
    )
    flops = 12 * clips * length * width * hidden
    cost = pl.CostEstimate(flops=flops, transcendentals=2 * clips * length * hidden,
                           bytes_accessed=clips * length * width * 8 + 4 * width * hidden * 4)
    return pl.pallas_call(
        kernel,
        grid_spec=grid_spec,
        out_shape=[
            jax.ShapeDtypeStruct((clips, length, width), BF16),
            jax.ShapeDtypeStruct((clips, length, width), F32),
            jax.ShapeDtypeStruct((flat_rows, LANE), F32),
            jax.ShapeDtypeStruct((8, width), F32),
            jax.ShapeDtypeStruct((8, width), F32),
            jax.ShapeDtypeStruct((8, hidden), F32),
        ],
        compiler_params=pltpu.CompilerParams(
            dimension_semantics=("arbitrary",), vmem_limit_bytes=60 * 1024 * 1024),
        cost_estimate=cost,
    )(counts, frames, cotangent, wrows, cw8, vec8, b1_8)


def unpack(packed, width, hidden):
    shapes = [(width, hidden), (hidden, width), (TAPS, width), (width,), (width,), (width,), (width,), (width,), (hidden,)]
    pieces = []
    start_at = 0
    for shape in shapes:
        entries = 1
        for extent in shape:
            entries = entries * extent
        pieces.append(packed[start_at : start_at + entries].reshape(shape))
        start_at = start_at + entries
    return (tuple(pieces), start_at)


AXES = ("dp", "fsdp")
LANES = 128


def bit_order(mesh_sizes):
    dp_size, fsdp_size = mesh_sizes
    fsdp_bits = int(math.log2(fsdp_size))
    dp_bits = int(math.log2(dp_size))
    order = [0] + [fsdp_bits + b for b in range(dp_bits)] + list(range(1, fsdp_bits))
    return order, fsdp_bits + dp_bits


def swap_perm(devices, bit):
    return [(i, i ^ (1 << bit)) for i in range(devices)]


def split_orders(order):
    if len(order) < 3:
        return [order]
    other = [order[0], order[2], order[1]] + order[3:]
    return [order, other]


def tree_all_gather(shard, orders, nbits):
    me = lax.axis_index(AXES)
    devices = 1 << nbits
    rows = shard.shape[0]
    cuts = [rows * p // len(orders) for p in range(len(orders) + 1)]
    held = [shard[cuts[p]:cuts[p + 1]] for p in range(len(orders))]
    held_bits = [[] for _ in orders]
    for step in range(nbits):
        for p, order in enumerate(orders):
            bit = order[step]
            other = lax.ppermute(held[p], AXES, swap_perm(devices, bit))
            upper = ((me >> bit) & 1) == 1
            held[p] = jnp.stack([jnp.where(upper, other, held[p]), jnp.where(upper, held[p], other)])
            held_bits[p].insert(0, bit)
    parts = []
    for p in range(len(orders)):
        axes = [held_bits[p].index(b) for b in sorted(held_bits[p], reverse=True)]
        parts.append(jnp.transpose(held[p], axes + [nbits, nbits + 1]).reshape(devices, -1, LANES))
    return jnp.concatenate(parts, axis=1).reshape(devices * rows, LANES)


def tree_reduce_scatter(full, orders, nbits):
    me = lax.axis_index(AXES)
    devices = 1 << nbits
    rows = full.shape[0] // devices
    cuts = [rows * p // len(orders) for p in range(len(orders) + 1)]
    if rows % 8 == 0:
        cuts = [c // 8 * 8 for c in cuts]
    shaped = full.reshape([2] * nbits + [rows, LANES])
    held = [shaped[..., cuts[p]:cuts[p + 1], :] for p in range(len(orders))]
    held_bits = [[nbits - 1 - a for a in range(nbits)] for _ in orders]
    for step in range(nbits):
        for p, order in enumerate(orders):
            bit = order[step]
            axis = held_bits[p].index(bit)
            mine = (me >> bit) & 1
            keep = lax.dynamic_index_in_dim(held[p], mine, axis=axis, keepdims=False)
            send = lax.dynamic_index_in_dim(held[p], 1 - mine, axis=axis, keepdims=False)
            held[p] = keep + lax.ppermute(send, AXES, swap_perm(devices, bit))
            held_bits[p].pop(axis)
    return jnp.concatenate(held, axis=0)


def tree_all_sum(value, order, nbits):
    devices = 1 << nbits
    for bit in reversed(order):
        value = value + lax.ppermute(value, AXES, swap_perm(devices, bit))
    return value


def body(frames, counts, cotangent, master, momentum, average, disc_grads, mesh_sizes=None):
    order, nbits = bit_order(mesh_sizes)
    devices = 1 << nbits
    clips, length, width = frames.shape
    hidden = 3 * width
    rows = clips * length
    local = master.shape[0]
    flat_size = local * devices
    total_frames = jnp.float32(rows * devices)
    rounded = master.astype(BF16).reshape(local // LANES, LANES)
    packed_rows = tree_all_gather(rounded, [o[::-1] for o in split_orders(order)], nbits)
    wrows = packed_rows[: 2 * width * hidden // LANES]
    packed = packed_rows.reshape(-1)
    (w_one, w_two, conv_w, conv_b, ln_g, ln_b, b_two, gamma, b_one), used = unpack(packed, width, hidden)
    cw8 = jnp.zeros((8, width), F32).at[:TAPS].set(conv_w.astype(F32))
    vec8 = jnp.concatenate(
        [jnp.stack([conv_b, ln_g, ln_b, b_two, gamma]).astype(F32), jnp.zeros((3, width), F32)])
    b1_8 = jnp.zeros((8, hidden), F32).at[0].set(b_one.astype(F32))
    shard_rows = local // LANES
    padded_rows = -(-shard_rows // 8) * 8
    aligned = padded_rows != shard_rows and (padded_rows - shard_rows) * (devices - 1) <= padded_rows
    block = padded_rows if aligned else shard_rows
    block_out, input_grad, grad_full, _, _, _ = fused_block(
        frames, counts, cotangent, wrows, cw8, vec8, b1_8, devices * block)
    grad_block = tree_reduce_scatter(grad_full, split_orders(order), nbits)
    if aligned:
        me = lax.axis_index(AXES)
        prev = lax.ppermute(grad_block, AXES, [(i, (i + 1) % devices) for i in range(devices)])
        both = jnp.concatenate([prev, grad_block])
        grad_shard = lax.dynamic_slice_in_dim(both, block - (block - shard_rows) * me, shard_rows, axis=0)
    else:
        grad_shard = grad_block
    disc_rows = jnp.sum((disc_grads * disc_grads).reshape(-1, LANES), axis=0, keepdims=True)
    own_rows = jnp.sum(grad_shard * grad_shard, axis=0, keepdims=True)
    squares = jnp.broadcast_to(own_rows + disc_rows, (8, LANES))
    squares = tree_all_sum(squares, order, nbits)
    grad_norm = jnp.sqrt(jnp.sum(squares[0]))
    grad_shard = grad_shard.reshape(-1)
    clipped = grad_shard * jnp.minimum(1.0, 20.0 * jnp.sqrt(total_frames) / (grad_norm + 1e-06))
    new_momentum = 0.9 * momentum + clipped
    new_master = master - (clipped + 0.9 * new_momentum) / jnp.sqrt(total_frames)
    new_average = 0.99 * average + 0.01 * new_master
    return (
        block_out,
        input_grad,
        grad_norm,
        new_master,
        new_momentum,
        new_average,
        new_master.astype(BF16),
        new_average.astype(BF16),
    )


def solution(mesh):
    clip_spec = P(("dp", "fsdp"), None, None)
    flat_spec = P(("dp", "fsdp"))
    mesh_sizes = (mesh.shape["dp"], mesh.shape["fsdp"])
    return jax.shard_map(
        functools.partial(body, mesh_sizes=mesh_sizes),
        mesh=mesh,
        in_specs=(clip_spec, flat_spec, clip_spec, flat_spec, flat_spec, flat_spec, flat_spec),
        out_specs=(clip_spec, clip_spec, P(), flat_spec, flat_spec, flat_spec, flat_spec, flat_spec),
        check_vma=False,
    )
```

```python
import functools
import math

import jax
import jax.numpy as jnp
from jax import lax
from jax.experimental import pallas as pl
from jax.experimental.pallas import tpu as pltpu
from jax.sharding import PartitionSpec as P

F32 = jnp.float32
BF16 = jnp.bfloat16
TAPS = 7
HALF = TAPS // 2
PAD = 8
LANE = 128


def tdot(x, y):
    return lax.dot_general(x, y, (((0,), (0,)), ((), ())), preferred_element_type=F32)


def ntdot(x, y):
    return lax.dot_general(x, y, (((1,), (1,)), ((), ())), preferred_element_type=F32)


def block_kernel(length, width, hidden, rows, flat_rows):
    nblk = length // rows
    quads = width // LANE
    inv_w = 1.0 / width
    sqrt_half = math.sqrt(0.5)
    inv_sqrt_2pi = 1.0 / math.sqrt(2.0 * math.pi)

    def kernel(counts_ref, fr_ref, cot_ref, wrows_hbm, cw_ref, vec_ref, b1_ref,
               bo_ref, ig_ref, gflat_hbm, gcw_ref, gvec_ref, gb1_ref,
               xq, xhat_s, rstd_s, a_s, da_s, dq, gw1_s, gw2_s, flat_s, wb_s, w1_ref, w2_ref, sems):
        clip = pl.program_id(0)
        count = counts_ref[clip]

        @pl.when(clip == 0)
        def _weights():
            load = pltpu.make_async_copy(wrows_hbm.at[0:wb_s.shape[0], :], wb_s, sems.at[1])
            load.start()
            load.wait()
            wide = flat_s.at[0:wb_s.shape[0], :]
            wide[...] = wb_s[...].astype(F32)
            per1 = hidden // LANE
            per2 = width // LANE
            for j in range(per1):
                w1_ref[:, j * LANE:(j + 1) * LANE] = wide[pl.ds(j, width, stride=per1), :].astype(BF16)
            at = width * hidden // LANE
            for j in range(per2):
                w2_ref[:, j * LANE:(j + 1) * LANE] = wide[pl.ds(at + j, hidden, stride=per2), :].astype(BF16)

        @pl.when(clip == 0)
        def _init():
            gw1_s[...] = jnp.zeros_like(gw1_s)
            gw2_s[...] = jnp.zeros_like(gw2_s)
            gcw_ref[...] = jnp.zeros_like(gcw_ref)
            gvec_ref[...] = jnp.zeros_like(gvec_ref)
            gb1_ref[...] = jnp.zeros_like(gb1_ref)
            xq[0:PAD * quads, :] = jnp.zeros((PAD * quads, LANE), F32)
            xq[(PAD + length) * quads:, :] = jnp.zeros((PAD * quads, LANE), F32)
            dq[0:PAD * quads, :] = jnp.zeros((PAD * quads, LANE), F32)
            dq[(PAD + length) * quads:, :] = jnp.zeros((PAD * quads, LANE), F32)

        cw = cw_ref[...]
        conv_b = vec_ref[0:1, :]
        ln_g = vec_ref[1:2, :]
        ln_b = vec_ref[2:3, :]
        b_two = vec_ref[3:4, :]
        gamma = vec_ref[4:5, :]
        b_one = b1_ref[0:1, :]

        all_rows = lax.broadcasted_iota(jnp.int32, (length, 1), 0)
        xm_all = jnp.where(all_rows < count, fr_ref[0].astype(F32), 0.0)
        for q in range(quads):
            xq[pl.ds(PAD * quads + q, length, stride=quads), :] = xm_all[:, q * LANE:(q + 1) * LANE]

        def taps_of(buf, start):
            return jnp.concatenate(
                [buf[pl.ds(start * quads + q, rows, stride=quads), :] for q in range(quads)], axis=1)

        for b in range(nblk):
            r0 = b * rows

            @pl.when(r0 < count)
            def _fwd_block():
                base = PAD + r0 - HALF
                conv = conv_b + cw[0:1, :] * taps_of(xq, base)
                for k in range(1, TAPS):
                    conv = conv + cw[k:k + 1, :] * taps_of(xq, base + k)
                centre = jnp.sum(conv, axis=-1, keepdims=True) * inv_w
                shifted = conv - centre
                spread = jnp.sum(shifted * shifted, axis=-1, keepdims=True) * inv_w
                rstd = lax.rsqrt(spread + 1e-6)
                xhat = shifted * rstd
                xhat_s[r0:r0 + rows, :] = xhat
                rstd_s[r0:r0 + rows, :] = rstd
                a_s[r0:r0 + rows, :] = (xhat * ln_g + ln_b).astype(BF16)

        bo_ref[...] = jnp.zeros_like(bo_ref)

        def chunk(c, carry):
            g_gamma, g_b2, g_b1 = carry
            r0 = pl.multiple_of(c * rows, rows)
            a = a_s[pl.ds(r0, rows), :]
            h1 = jnp.dot(a, w1_ref[...], preferred_element_type=F32) + b_one
            cdf = 0.5 * (1.0 + lax.erf(h1 * sqrt_half))
            hh = (h1 * cdf).astype(BF16)
            z = jnp.dot(hh, w2_ref[...], preferred_element_type=F32) + b_two
            live = (r0 + lax.broadcasted_iota(jnp.int32, (rows, 1), 0)) < count
            xin = fr_ref[0, pl.ds(r0, rows), :].astype(F32)
            bo_ref[0, pl.ds(r0, rows), :] = jnp.where(live, xin + gamma * z, 0.0).astype(BF16)
            dout = jnp.where(live, cot_ref[0, pl.ds(r0, rows), :].astype(F32), 0.0)
            g_gamma = g_gamma + jnp.sum(dout * z, axis=0, keepdims=True)
            dz = (gamma * dout).astype(BF16)
            g_b2 = g_b2 + jnp.sum(dz.astype(F32), axis=0, keepdims=True)
            gw2_s[...] += tdot(hh, dz)
            dhh = ntdot(dz, w2_ref[...])
            slope = cdf + h1 * (jnp.exp(-0.5 * (h1 * h1)) * inv_sqrt_2pi)
            dh1 = (dhh * slope).astype(BF16)
            g_b1 = g_b1 + jnp.sum(dh1.astype(F32), axis=0, keepdims=True)
            gw1_s[...] += tdot(a, dh1)
            da_s[pl.ds(r0, rows), :] = ntdot(dh1, w1_ref[...])
            return g_gamma, g_b2, g_b1

        nact = (count + rows - 1) // rows
        zero_d = jnp.zeros((1, width), F32)
        g_gamma, g_b2, g_b1 = lax.fori_loop(
            0, nact, chunk, (zero_d, zero_d, jnp.zeros((1, hidden), F32)))

        def dxm_block(b):
            r0 = b * rows
            base = PAD + r0 + HALF
            dxm = cw[0:1, :] * taps_of(dq, base)
            for k in range(1, TAPS):
                dxm = dxm + cw[k:k + 1, :] * taps_of(dq, base - k)
            live = (r0 + lax.broadcasted_iota(jnp.int32, (rows, 1), 0)) < count
            cot = cot_ref[0, r0:r0 + rows, :].astype(F32)
            ig_ref[0, r0:r0 + rows, :] = jnp.where(live, cot + dxm, 0.0)

        sums = [zero_d] * (3 + TAPS)
        for b in range(nblk):
            r0 = b * rows

            def _bwd_block(r0=r0):
                live = (r0 + lax.broadcasted_iota(jnp.int32, (rows, 1), 0)) < count
                da = jnp.where(live, da_s[r0:r0 + rows, :], 0.0)
                xhat = xhat_s[r0:r0 + rows, :]
                rstd = rstd_s[r0:r0 + rows, :]
                dn = da * ln_g
                m1 = jnp.sum(dn, axis=-1, keepdims=True) * inv_w
                m2 = jnp.sum(dn * xhat, axis=-1, keepdims=True) * inv_w
                dconv = jnp.where(live, rstd * (dn - m1 - xhat * m2), 0.0)
                for q in range(quads):
                    dq[pl.ds((PAD + r0) * quads + q, rows, stride=quads), :] = dconv[:, q * LANE:(q + 1) * LANE]
                part = [jnp.sum(dconv, axis=0, keepdims=True),
                        jnp.sum(da * xhat, axis=0, keepdims=True),
                        jnp.sum(da, axis=0, keepdims=True)]
                base = PAD + r0 - HALF
                for k in range(TAPS):
                    part.append(jnp.sum(dconv * taps_of(xq, base + k), axis=0, keepdims=True))
                return part

            active = r0 < count
            part = lax.cond(active, _bwd_block, lambda: [zero_d] * (3 + TAPS))

            @pl.when(jnp.logical_not(active))
            def _idle():
                dq[(PAD + r0) * quads:(PAD + r0 + rows) * quads, :] = jnp.zeros((rows * quads, LANE), F32)
                ig_ref[0, r0:r0 + rows, :] = jnp.zeros((rows, width), F32)

            sums = [s + p for s, p in zip(sums, part)]
            if b >= 1:
                @pl.when((b - 1) * rows < count)
                def _prev(b=b):
                    dxm_block(b - 1)

        @pl.when((nblk - 1) * rows < count)
        def _last():
            dxm_block(nblk - 1)

        gvec_ref[0:1, :] += sums[0]
        gvec_ref[1:2, :] += sums[1]
        gvec_ref[2:3, :] += sums[2]
        gvec_ref[3:4, :] += g_b2
        gvec_ref[4:5, :] += g_gamma
        for k in range(TAPS):
            gcw_ref[k:k + 1, :] += sums[3 + k]
        gb1_ref[0:1, :] += g_b1

        @pl.when(clip == pl.num_programs(0) - 1)
        def _flush():
            per1 = hidden // LANE
            per2 = width // LANE
            for j in range(per1):
                flat_s[pl.ds(j, width, stride=per1), :] = gw1_s[:, j * LANE:(j + 1) * LANE]
            at = width * hidden // LANE
            for j in range(per2):
                flat_s[pl.ds(at + j, hidden, stride=per2), :] = gw2_s[:, j * LANE:(j + 1) * LANE]
            at = 2 * at
            for q in range(per2):
                flat_s[pl.ds(at + q, TAPS, stride=per2), :] = gcw_ref[0:TAPS, q * LANE:(q + 1) * LANE]
            at = at + TAPS * per2
            for q in range(per2):
                flat_s[pl.ds(at + q, 5, stride=per2), :] = gvec_ref[0:5, q * LANE:(q + 1) * LANE]
            at = at + 5 * per2
            for j in range(per1):
                flat_s[at + j:at + j + 1, :] = gb1_ref[0:1, j * LANE:(j + 1) * LANE]
            at = at + per1
            flat_s[at:, :] = jnp.zeros((flat_rows - at, LANE), F32)
            out = pltpu.make_async_copy(flat_s, gflat_hbm, sems.at[0])
            out.start()
            out.wait()

    return kernel


def fused_block(frames, counts, cotangent, wrows, cw8, vec8, b1_8, flat_rows, rows=256):
    clips, length, width = frames.shape
    hidden = cw8.shape[1] * 3
    kernel = block_kernel(length, width, hidden, rows, flat_rows)
    clip_spec = pl.BlockSpec((1, length, width), lambda i, c: (i, 0, 0))
    fixed = lambda shape: pl.BlockSpec(shape, lambda i, c: (0, 0))
    grid_spec = pltpu.PrefetchScalarGridSpec(
        num_scalar_prefetch=1,
        grid=(clips,),
        in_specs=[clip_spec, clip_spec, pl.BlockSpec(memory_space=pl.ANY),
                  fixed((8, width)), fixed((8, width)), fixed((8, hidden))],
        out_specs=[clip_spec, clip_spec,
                   pl.BlockSpec(memory_space=pl.ANY),
                   fixed((8, width)), fixed((8, width)), fixed((8, hidden))],
        scratch_shapes=[
            pltpu.VMEM(((length + 2 * PAD) * (width // LANE), LANE), F32),
            pltpu.VMEM((length, width), F32),
            pltpu.VMEM((length, 1), F32),
            pltpu.VMEM((length, width), BF16),
            pltpu.VMEM((length, width), F32),
            pltpu.VMEM(((length + 2 * PAD) * (width // LANE), LANE), F32),
            pltpu.VMEM((width, hidden), F32),
            pltpu.VMEM((hidden, width), F32),
            pltpu.VMEM((flat_rows, LANE), F32),
            pltpu.VMEM((2 * width * hidden // LANE, LANE), BF16),
            pltpu.VMEM((width, hidden), BF16),
            pltpu.VMEM((hidden, width), BF16),
            pltpu.SemaphoreType.DMA((2,)),
        ],
    )
    flops = 12 * clips * length * width * hidden
    cost = pl.CostEstimate(flops=flops, transcendentals=2 * clips * length * hidden,
                           bytes_accessed=clips * length * width * 8 + 4 * width * hidden * 4)
    return pl.pallas_call(
        kernel,
        grid_spec=grid_spec,
        out_shape=[
            jax.ShapeDtypeStruct((clips, length, width), BF16),
            jax.ShapeDtypeStruct((clips, length, width), F32),
            jax.ShapeDtypeStruct((flat_rows, LANE), F32),
            jax.ShapeDtypeStruct((8, width), F32),
            jax.ShapeDtypeStruct((8, width), F32),
            jax.ShapeDtypeStruct((8, hidden), F32),
        ],
        compiler_params=pltpu.CompilerParams(
            dimension_semantics=("arbitrary",), vmem_limit_bytes=60 * 1024 * 1024),
        cost_estimate=cost,
    )(counts, frames, cotangent, wrows, cw8, vec8, b1_8)


def unpack(packed, width, hidden):
    shapes = [(width, hidden), (hidden, width), (TAPS, width), (width,), (width,), (width,), (width,), (width,), (hidden,)]
    pieces = []
    start_at = 0
    for shape in shapes:
        entries = 1
        for extent in shape:
            entries = entries * extent
        pieces.append(packed[start_at : start_at + entries].reshape(shape))
        start_at = start_at + entries
    return (tuple(pieces), start_at)


AXES = ("dp", "fsdp")
LANES = 128


def bit_order(mesh_sizes):
    dp_size, fsdp_size = mesh_sizes
    fsdp_bits = int(math.log2(fsdp_size))
    dp_bits = int(math.log2(dp_size))
    order = [0] + [fsdp_bits + b for b in range(dp_bits)] + list(range(1, fsdp_bits))
    return order, fsdp_bits + dp_bits


def swap_perm(devices, bit):
    return [(i, i ^ (1 << bit)) for i in range(devices)]


def split_orders(order):
    if len(order) < 3:
        return [order]
    other = [order[0], order[2], order[1]] + order[3:]
    return [order, other]


def tree_all_gather(shard, orders, nbits):
    me = lax.axis_index(AXES)
    devices = 1 << nbits
    rows = shard.shape[0]
    cuts = [rows * p // len(orders) for p in range(len(orders) + 1)]
    held = [shard[cuts[p]:cuts[p + 1]] for p in range(len(orders))]
    held_bits = [[] for _ in orders]
    for step in range(nbits):
        for p, order in enumerate(orders):
            bit = order[step]
            other = lax.ppermute(held[p], AXES, swap_perm(devices, bit))
            upper = ((me >> bit) & 1) == 1
            held[p] = jnp.stack([jnp.where(upper, other, held[p]), jnp.where(upper, held[p], other)])
            held_bits[p].insert(0, bit)
    parts = []
    for p in range(len(orders)):
        axes = [held_bits[p].index(b) for b in sorted(held_bits[p], reverse=True)]
        parts.append(jnp.transpose(held[p], axes + [nbits, nbits + 1]).reshape(devices, -1, LANES))
    return jnp.concatenate(parts, axis=1).reshape(devices * rows, LANES)


def tree_reduce_scatter(full, orders, nbits):
    me = lax.axis_index(AXES)
    devices = 1 << nbits
    rows = full.shape[0] // devices
    cuts = [rows * p // len(orders) for p in range(len(orders) + 1)]
    if rows % 8 == 0:
        cuts = [c // 8 * 8 for c in cuts]
    shaped = full.reshape([2] * nbits + [rows, LANES])
    held = [shaped[..., cuts[p]:cuts[p + 1], :] for p in range(len(orders))]
    held_bits = [[nbits - 1 - a for a in range(nbits)] for _ in orders]
    for step in range(nbits):
        for p, order in enumerate(orders):
            bit = order[step]
            axis = held_bits[p].index(bit)
            mine = (me >> bit) & 1
            keep = lax.dynamic_index_in_dim(held[p], mine, axis=axis, keepdims=False)
            send = lax.dynamic_index_in_dim(held[p], 1 - mine, axis=axis, keepdims=False)
            held[p] = keep + lax.ppermute(send, AXES, swap_perm(devices, bit))
            held_bits[p].pop(axis)
    return jnp.concatenate(held, axis=0)


def tree_all_sum(value, order, nbits):
    devices = 1 << nbits
    for bit in reversed(order):
        value = value + lax.ppermute(value, AXES, swap_perm(devices, bit))
    return value


def body(frames, counts, cotangent, master, momentum, average, disc_grads, mesh_sizes=None):
    order, nbits = bit_order(mesh_sizes)
    devices = 1 << nbits
    clips, length, width = frames.shape
    hidden = 3 * width
    rows = clips * length
    local = master.shape[0]
    flat_size = local * devices
    total_frames = jnp.float32(rows * devices)
    rounded = master.astype(BF16).reshape(local // LANES, LANES)
    packed_rows = tree_all_gather(rounded, [o[::-1] for o in split_orders(order)], nbits)
    weight_rows = 2 * width * hidden // LANES
    small_rows = -(-(TAPS * width + 5 * width + hidden) // LANES)
    small = packed_rows[weight_rows:weight_rows + small_rows].reshape(-1)
    conv_w = small[: TAPS * width].reshape(TAPS, width)
    at = TAPS * width
    conv_b, ln_g, ln_b, b_two, gamma = [small[at + i * width: at + (i + 1) * width] for i in range(5)]
    at = at + 5 * width
    b_one = small[at: at + hidden]
    cw8 = jnp.zeros((8, width), F32).at[:TAPS].set(conv_w.astype(F32))
    vec8 = jnp.concatenate(
        [jnp.stack([conv_b, ln_g, ln_b, b_two, gamma]).astype(F32), jnp.zeros((3, width), F32)])
    b1_8 = jnp.zeros((8, hidden), F32).at[0].set(b_one.astype(F32))
    shard_rows = local // LANES
    padded_rows = -(-shard_rows // 8) * 8
    aligned = padded_rows != shard_rows and (padded_rows - shard_rows) * (devices - 1) <= padded_rows
    block = padded_rows if aligned else shard_rows
    block_out, input_grad, grad_full, _, _, _ = fused_block(
        frames, counts, cotangent, packed_rows, cw8, vec8, b1_8, devices * block)
    grad_block = tree_reduce_scatter(grad_full, split_orders(order), nbits)
    if aligned:
        me = lax.axis_index(AXES)
        prev = lax.ppermute(grad_block, AXES, [(i, (i + 1) % devices) for i in range(devices)])
        both = jnp.concatenate([prev, grad_block])
        grad_shard = lax.dynamic_slice_in_dim(both, block - (block - shard_rows) * me, shard_rows, axis=0)
    else:
        grad_shard = grad_block
    disc_rows = jnp.sum((disc_grads * disc_grads).reshape(-1, LANES), axis=0, keepdims=True)
    own_rows = jnp.sum(grad_shard * grad_shard, axis=0, keepdims=True)
    squares = jnp.broadcast_to(own_rows + disc_rows, (8, LANES))
    squares = tree_all_sum(squares, order, nbits)
    grad_norm = jnp.sqrt(jnp.sum(squares[0]))
    grad_shard = grad_shard.reshape(-1)
    clipped = grad_shard * jnp.minimum(1.0, 20.0 * jnp.sqrt(total_frames) / (grad_norm + 1e-06))
    new_momentum = 0.9 * momentum + clipped
    new_master = master - (clipped + 0.9 * new_momentum) / jnp.sqrt(total_frames)
    new_average = 0.99 * average + 0.01 * new_master
    return (
        block_out,
        input_grad,
        grad_norm,
        new_master,
        new_momentum,
        new_average,
        new_master.astype(BF16),
        new_average.astype(BF16),
    )


def solution(mesh):
    clip_spec = P(("dp", "fsdp"), None, None)
    flat_spec = P(("dp", "fsdp"))
    mesh_sizes = (mesh.shape["dp"], mesh.shape["fsdp"])
    return jax.shard_map(
        functools.partial(body, mesh_sizes=mesh_sizes),
        mesh=mesh,
        in_specs=(clip_spec, flat_spec, clip_spec, flat_spec, flat_spec, flat_spec, flat_spec),
        out_specs=(clip_spec, clip_spec, P(), flat_spec, flat_spec, flat_spec, flat_spec, flat_spec),
        check_vma=False,
    )
```

```python
import functools
import math

import jax
import jax.numpy as jnp
from jax import lax
from jax.experimental import pallas as pl
from jax.experimental.pallas import tpu as pltpu
from jax.sharding import PartitionSpec as P

F32 = jnp.float32
BF16 = jnp.bfloat16
TAPS = 7
HALF = TAPS // 2
PAD = 8
LANE = 128


def tdot(x, y):
    return lax.dot_general(x, y, (((0,), (0,)), ((), ())), preferred_element_type=F32)


def ntdot(x, y):
    return lax.dot_general(x, y, (((1,), (1,)), ((), ())), preferred_element_type=F32)


def block_kernel(length, width, hidden, rows, flat_rows):
    nblk = length // rows
    quads = width // LANE
    inv_w = 1.0 / width
    sqrt_half = math.sqrt(0.5)
    inv_sqrt_2pi = 1.0 / math.sqrt(2.0 * math.pi)

    def kernel(counts_ref, fr_ref, cot_ref, wrows_hbm, cw_ref, vec_ref, b1_ref,
               bo_ref, ig_ref, gflat_hbm, gcw_ref, gvec_ref, gb1_ref,
               xq, xhat_s, rstd_s, a_s, da_s, dq, gw1_s, gw2_s, flat_s, wb_s, w1_ref, w2_ref, sems):
        clip = pl.program_id(0)
        count = counts_ref[clip]

        @pl.when(clip == 0)
        def _weights():
            load = pltpu.make_async_copy(wrows_hbm.at[0:wb_s.shape[0], :], wb_s, sems.at[1])
            load.start()
            load.wait()
            wide = flat_s.at[0:wb_s.shape[0], :]
            wide[...] = wb_s[...].astype(F32)
            per1 = hidden // LANE
            per2 = width // LANE
            for j in range(per1):
                w1_ref[:, j * LANE:(j + 1) * LANE] = wide[pl.ds(j, width, stride=per1), :].astype(BF16)
            at = width * hidden // LANE
            for j in range(per2):
                w2_ref[:, j * LANE:(j + 1) * LANE] = wide[pl.ds(at + j, hidden, stride=per2), :].astype(BF16)

        @pl.when(clip == 0)
        def _init():
            gw1_s[...] = jnp.zeros_like(gw1_s)
            gw2_s[...] = jnp.zeros_like(gw2_s)
            gcw_ref[...] = jnp.zeros_like(gcw_ref)
            gvec_ref[...] = jnp.zeros_like(gvec_ref)
            gb1_ref[...] = jnp.zeros_like(gb1_ref)
            xq[0:PAD * quads, :] = jnp.zeros((PAD * quads, LANE), F32)
            xq[(PAD + length) * quads:, :] = jnp.zeros((PAD * quads, LANE), F32)
            dq[0:PAD * quads, :] = jnp.zeros((PAD * quads, LANE), F32)
            dq[(PAD + length) * quads:, :] = jnp.zeros((PAD * quads, LANE), F32)

        cw = cw_ref[...]
        conv_b = vec_ref[0:1, :]
        ln_g = vec_ref[1:2, :]
        ln_b = vec_ref[2:3, :]
        b_two = vec_ref[3:4, :]
        gamma = vec_ref[4:5, :]
        b_one = b1_ref[0:1, :]

        all_rows = lax.broadcasted_iota(jnp.int32, (length, 1), 0)
        xm_all = jnp.where(all_rows < count, fr_ref[0].astype(F32), 0.0)
        for q in range(quads):
            xq[pl.ds(PAD * quads + q, length, stride=quads), :] = xm_all[:, q * LANE:(q + 1) * LANE]

        def taps_of(buf, start):
            return jnp.concatenate(
                [buf[pl.ds(start * quads + q, rows, stride=quads), :] for q in range(quads)], axis=1)

        for b in range(nblk):
            r0 = b * rows

            @pl.when(r0 < count)
            def _fwd_block():
                base = PAD + r0 - HALF
                conv = conv_b + cw[0:1, :] * taps_of(xq, base)
                for k in range(1, TAPS):
                    conv = conv + cw[k:k + 1, :] * taps_of(xq, base + k)
                centre = jnp.sum(conv, axis=-1, keepdims=True) * inv_w
                shifted = conv - centre
                spread = jnp.sum(shifted * shifted, axis=-1, keepdims=True) * inv_w
                rstd = lax.rsqrt(spread + 1e-6)
                xhat = shifted * rstd
                xhat_s[r0:r0 + rows, :] = xhat
                rstd_s[r0:r0 + rows, :] = rstd
                a_s[r0:r0 + rows, :] = (xhat * ln_g + ln_b).astype(BF16)

        bo_ref[...] = jnp.zeros_like(bo_ref)

        def chunk(c, carry):
            g_gamma, g_b2, g_b1 = carry
            r0 = pl.multiple_of(c * rows, rows)
            a = a_s[pl.ds(r0, rows), :]
            h1 = jnp.dot(a, w1_ref[...], preferred_element_type=F32) + b_one
            cdf = 0.5 * (1.0 + lax.erf(h1 * sqrt_half))
            hh = (h1 * cdf).astype(BF16)
            z = jnp.dot(hh, w2_ref[...], preferred_element_type=F32) + b_two
            live = (r0 + lax.broadcasted_iota(jnp.int32, (rows, 1), 0)) < count
            xin = fr_ref[0, pl.ds(r0, rows), :].astype(F32)
            bo_ref[0, pl.ds(r0, rows), :] = jnp.where(live, xin + gamma * z, 0.0).astype(BF16)
            dout = jnp.where(live, cot_ref[0, pl.ds(r0, rows), :].astype(F32), 0.0)
            g_gamma = g_gamma + jnp.sum(dout * z, axis=0, keepdims=True)
            dz = (gamma * dout).astype(BF16)
            g_b2 = g_b2 + jnp.sum(dz.astype(F32), axis=0, keepdims=True)
            gw2_s[...] += tdot(hh, dz)
            dhh = ntdot(dz, w2_ref[...])
            slope = cdf + h1 * (jnp.exp(-0.5 * (h1 * h1)) * inv_sqrt_2pi)
            dh1 = (dhh * slope).astype(BF16)
            g_b1 = g_b1 + jnp.sum(dh1.astype(F32), axis=0, keepdims=True)
            gw1_s[...] += tdot(a, dh1)
            da_s[pl.ds(r0, rows), :] = ntdot(dh1, w1_ref[...])
            return g_gamma, g_b2, g_b1

        nact = (count + rows - 1) // rows
        zero_d = jnp.zeros((1, width), F32)
        g_gamma, g_b2, g_b1 = lax.fori_loop(
            0, nact, chunk, (zero_d, zero_d, jnp.zeros((1, hidden), F32)))

        def dxm_block(b):
            r0 = b * rows
            base = PAD + r0 + HALF
            dxm = cw[0:1, :] * taps_of(dq, base)
            for k in range(1, TAPS):
                dxm = dxm + cw[k:k + 1, :] * taps_of(dq, base - k)
            live = (r0 + lax.broadcasted_iota(jnp.int32, (rows, 1), 0)) < count
            cot = cot_ref[0, r0:r0 + rows, :].astype(F32)
            ig_ref[0, r0:r0 + rows, :] = jnp.where(live, cot + dxm, 0.0)

        sums = [zero_d] * (3 + TAPS)
        for b in range(nblk):
            r0 = b * rows

            def _bwd_block(r0=r0):
                live = (r0 + lax.broadcasted_iota(jnp.int32, (rows, 1), 0)) < count
                da = jnp.where(live, da_s[r0:r0 + rows, :], 0.0)
                xhat = xhat_s[r0:r0 + rows, :]
                rstd = rstd_s[r0:r0 + rows, :]
                dn = da * ln_g
                m1 = jnp.sum(dn, axis=-1, keepdims=True) * inv_w
                m2 = jnp.sum(dn * xhat, axis=-1, keepdims=True) * inv_w
                dconv = jnp.where(live, rstd * (dn - m1 - xhat * m2), 0.0)
                for q in range(quads):
                    dq[pl.ds((PAD + r0) * quads + q, rows, stride=quads), :] = dconv[:, q * LANE:(q + 1) * LANE]
                part = [jnp.sum(dconv, axis=0, keepdims=True),
                        jnp.sum(da * xhat, axis=0, keepdims=True),
                        jnp.sum(da, axis=0, keepdims=True)]
                base = PAD + r0 - HALF
                for k in range(TAPS):
                    part.append(jnp.sum(dconv * taps_of(xq, base + k), axis=0, keepdims=True))
                return part

            active = r0 < count
            part = lax.cond(active, _bwd_block, lambda: [zero_d] * (3 + TAPS))

            @pl.when(jnp.logical_not(active))
            def _idle():
                dq[(PAD + r0) * quads:(PAD + r0 + rows) * quads, :] = jnp.zeros((rows * quads, LANE), F32)
                ig_ref[0, r0:r0 + rows, :] = jnp.zeros((rows, width), F32)

            sums = [s + p for s, p in zip(sums, part)]
            if b >= 1:
                @pl.when((b - 1) * rows < count)
                def _prev(b=b):
                    dxm_block(b - 1)

        @pl.when((nblk - 1) * rows < count)
        def _last():
            dxm_block(nblk - 1)

        gvec_ref[0:1, :] += sums[0]
        gvec_ref[1:2, :] += sums[1]
        gvec_ref[2:3, :] += sums[2]
        gvec_ref[3:4, :] += g_b2
        gvec_ref[4:5, :] += g_gamma
        for k in range(TAPS):
            gcw_ref[k:k + 1, :] += sums[3 + k]
        gb1_ref[0:1, :] += g_b1

        @pl.when(clip == pl.num_programs(0) - 1)
        def _flush():
            per1 = hidden // LANE
            per2 = width // LANE
            for j in range(per1):
                flat_s[pl.ds(j, width, stride=per1), :] = gw1_s[:, j * LANE:(j + 1) * LANE]
            at = width * hidden // LANE
            for j in range(per2):
                flat_s[pl.ds(at + j, hidden, stride=per2), :] = gw2_s[:, j * LANE:(j + 1) * LANE]
            at = 2 * at
            for q in range(per2):
                flat_s[pl.ds(at + q, TAPS, stride=per2), :] = gcw_ref[0:TAPS, q * LANE:(q + 1) * LANE]
            at = at + TAPS * per2
            for q in range(per2):
                flat_s[pl.ds(at + q, 5, stride=per2), :] = gvec_ref[0:5, q * LANE:(q + 1) * LANE]
            at = at + 5 * per2
            for j in range(per1):
                flat_s[at + j:at + j + 1, :] = gb1_ref[0:1, j * LANE:(j + 1) * LANE]
            at = at + per1
            flat_s[at:, :] = jnp.zeros((flat_rows - at, LANE), F32)
            out = pltpu.make_async_copy(flat_s, gflat_hbm, sems.at[0])
            out.start()
            out.wait()

    return kernel


def fused_block(frames, counts, cotangent, wrows, cw8, vec8, b1_8, flat_rows, rows=256):
    clips, length, width = frames.shape
    hidden = cw8.shape[1] * 3
    kernel = block_kernel(length, width, hidden, rows, flat_rows)
    clip_spec = pl.BlockSpec((1, length, width), lambda i, c: (i, 0, 0))
    fixed = lambda shape: pl.BlockSpec(shape, lambda i, c: (0, 0))
    grid_spec = pltpu.PrefetchScalarGridSpec(
        num_scalar_prefetch=1,
        grid=(clips,),
        in_specs=[clip_spec, clip_spec, pl.BlockSpec(memory_space=pl.ANY),
                  fixed((8, width)), fixed((8, width)), fixed((8, hidden))],
        out_specs=[clip_spec, clip_spec,
                   pl.BlockSpec(memory_space=pl.ANY),
                   fixed((8, width)), fixed((8, width)), fixed((8, hidden))],
        scratch_shapes=[
            pltpu.VMEM(((length + 2 * PAD) * (width // LANE), LANE), F32),
            pltpu.VMEM((length, width), F32),
            pltpu.VMEM((length, 1), F32),
            pltpu.VMEM((length, width), BF16),
            pltpu.VMEM((length, width), F32),
            pltpu.VMEM(((length + 2 * PAD) * (width // LANE), LANE), F32),
            pltpu.VMEM((width, hidden), F32),
            pltpu.VMEM((hidden, width), F32),
            pltpu.VMEM((flat_rows, LANE), F32),
            pltpu.VMEM((2 * width * hidden // LANE, LANE), BF16),
            pltpu.VMEM((width, hidden), BF16),
            pltpu.VMEM((hidden, width), BF16),
            pltpu.SemaphoreType.DMA((2,)),
        ],
    )
    flops = 12 * clips * length * width * hidden
    cost = pl.CostEstimate(flops=flops, transcendentals=2 * clips * length * hidden,
                           bytes_accessed=clips * length * width * 8 + 4 * width * hidden * 4)
    return pl.pallas_call(
        kernel,
        grid_spec=grid_spec,
        out_shape=[
            jax.ShapeDtypeStruct((clips, length, width), BF16),
            jax.ShapeDtypeStruct((clips, length, width), F32),
            jax.ShapeDtypeStruct((flat_rows, LANE), F32),
            jax.ShapeDtypeStruct((8, width), F32),
            jax.ShapeDtypeStruct((8, width), F32),
            jax.ShapeDtypeStruct((8, hidden), F32),
        ],
        compiler_params=pltpu.CompilerParams(
            dimension_semantics=("arbitrary",), vmem_limit_bytes=60 * 1024 * 1024),
        cost_estimate=cost,
    )(counts, frames, cotangent, wrows, cw8, vec8, b1_8)


def unpack(packed, width, hidden):
    shapes = [(width, hidden), (hidden, width), (TAPS, width), (width,), (width,), (width,), (width,), (width,), (hidden,)]
    pieces = []
    start_at = 0
    for shape in shapes:
        entries = 1
        for extent in shape:
            entries = entries * extent
        pieces.append(packed[start_at : start_at + entries].reshape(shape))
        start_at = start_at + entries
    return (tuple(pieces), start_at)


AXES = ("dp", "fsdp")
LANES = 128


def bit_order(mesh_sizes):
    dp_size, fsdp_size = mesh_sizes
    fsdp_bits = int(math.log2(fsdp_size))
    dp_bits = int(math.log2(dp_size))
    order = [0] + [fsdp_bits + b for b in range(dp_bits)] + list(range(1, fsdp_bits))
    return order, fsdp_bits + dp_bits


def swap_perm(devices, bit):
    return [(i, i ^ (1 << bit)) for i in range(devices)]


def split_orders(order):
    if len(order) < 3:
        return [order]
    other = [order[0], order[2], order[1]] + order[3:]
    return [order, other]


def tree_all_gather(shard, orders, nbits):
    me = lax.axis_index(AXES)
    devices = 1 << nbits
    rows = shard.shape[0]
    cuts = [rows * p // len(orders) for p in range(len(orders) + 1)]
    held = [shard[cuts[p]:cuts[p + 1]].reshape([1] * nbits + [-1, LANES]) for p in range(len(orders))]
    for step in range(nbits):
        for p, order in enumerate(orders):
            bit = order[step]
            other = lax.ppermute(held[p], AXES, swap_perm(devices, bit))
            upper = ((me >> bit) & 1) == 1
            held[p] = jnp.concatenate(
                [jnp.where(upper, other, held[p]), jnp.where(upper, held[p], other)], axis=nbits - 1 - bit)
    parts = [h.reshape(devices, -1, LANES) for h in held]
    return jnp.concatenate(parts, axis=1).reshape(devices * rows, LANES)


def tree_reduce_scatter(full, orders, nbits):
    me = lax.axis_index(AXES)
    devices = 1 << nbits
    rows = full.shape[0] // devices
    cuts = [rows * p // len(orders) for p in range(len(orders) + 1)]
    if rows % 8 == 0:
        cuts = [c // 8 * 8 for c in cuts]
    shaped = full.reshape([2] * nbits + [rows, LANES])
    held = [shaped[..., cuts[p]:cuts[p + 1], :] for p in range(len(orders))]
    held_bits = [[nbits - 1 - a for a in range(nbits)] for _ in orders]
    for step in range(nbits):
        for p, order in enumerate(orders):
            bit = order[step]
            axis = held_bits[p].index(bit)
            mine = (me >> bit) & 1
            keep = lax.dynamic_index_in_dim(held[p], mine, axis=axis, keepdims=False)
            send = lax.dynamic_index_in_dim(held[p], 1 - mine, axis=axis, keepdims=False)
            held[p] = keep + lax.ppermute(send, AXES, swap_perm(devices, bit))
            held_bits[p].pop(axis)
    return jnp.concatenate(held, axis=0)


def tree_all_sum(value, order, nbits):
    devices = 1 << nbits
    for bit in reversed(order):
        value = value + lax.ppermute(value, AXES, swap_perm(devices, bit))
    return value


def body(frames, counts, cotangent, master, momentum, average, disc_grads, mesh_sizes=None):
    order, nbits = bit_order(mesh_sizes)
    devices = 1 << nbits
    clips, length, width = frames.shape
    hidden = 3 * width
    rows = clips * length
    local = master.shape[0]
    flat_size = local * devices
    total_frames = jnp.float32(rows * devices)
    rounded = master.astype(BF16).reshape(local // LANES, LANES)
    packed_rows = tree_all_gather(rounded, [o[::-1] for o in split_orders(order)], nbits)
    weight_rows = 2 * width * hidden // LANES
    small_rows = -(-(TAPS * width + 5 * width + hidden) // LANES)
    small = packed_rows[weight_rows:weight_rows + small_rows].reshape(-1)
    conv_w = small[: TAPS * width].reshape(TAPS, width)
    at = TAPS * width
    conv_b, ln_g, ln_b, b_two, gamma = [small[at + i * width: at + (i + 1) * width] for i in range(5)]
    at = at + 5 * width
    b_one = small[at: at + hidden]
    cw8 = jnp.zeros((8, width), F32).at[:TAPS].set(conv_w.astype(F32))
    vec8 = jnp.concatenate(
        [jnp.stack([conv_b, ln_g, ln_b, b_two, gamma]).astype(F32), jnp.zeros((3, width), F32)])
    b1_8 = jnp.zeros((8, hidden), F32).at[0].set(b_one.astype(F32))
    shard_rows = local // LANES
    padded_rows = -(-shard_rows // 8) * 8
    aligned = padded_rows != shard_rows and (padded_rows - shard_rows) * (devices - 1) <= padded_rows
    block = padded_rows if aligned else shard_rows
    block_out, input_grad, grad_full, _, _, _ = fused_block(
        frames, counts, cotangent, packed_rows, cw8, vec8, b1_8, devices * block)
    grad_block = tree_reduce_scatter(grad_full, split_orders(order), nbits)
    if aligned:
        me = lax.axis_index(AXES)
        prev = lax.ppermute(grad_block, AXES, [(i, (i + 1) % devices) for i in range(devices)])
        both = jnp.concatenate([prev, grad_block])
        grad_shard = lax.dynamic_slice_in_dim(both, block - (block - shard_rows) * me, shard_rows, axis=0)
    else:
        grad_shard = grad_block
    disc_rows = jnp.sum((disc_grads * disc_grads).reshape(-1, LANES), axis=0, keepdims=True)
    own_rows = jnp.sum(grad_block * grad_block, axis=0, keepdims=True)
    squares = jnp.broadcast_to(own_rows + disc_rows, (8, LANES))
    squares = tree_all_sum(squares, order, nbits)
    grad_norm = jnp.sqrt(jnp.sum(squares[0]))
    grad_shard = grad_shard.reshape(-1)
    clipped = grad_shard * jnp.minimum(1.0, 20.0 * jnp.sqrt(total_frames) / (grad_norm + 1e-06))
    new_momentum = 0.9 * momentum + clipped
    new_master = master - (clipped + 0.9 * new_momentum) / jnp.sqrt(total_frames)
    new_average = 0.99 * average + 0.01 * new_master
    return (
        block_out,
        input_grad,
        grad_norm,
        new_master,
        new_momentum,
        new_average,
        new_master.astype(BF16),
        new_average.astype(BF16),
    )


def solution(mesh):
    clip_spec = P(("dp", "fsdp"), None, None)
    flat_spec = P(("dp", "fsdp"))
    mesh_sizes = (mesh.shape["dp"], mesh.shape["fsdp"])
    return jax.shard_map(
        functools.partial(body, mesh_sizes=mesh_sizes),
        mesh=mesh,
        in_specs=(clip_spec, flat_spec, clip_spec, flat_spec, flat_spec, flat_spec, flat_spec),
        out_specs=(clip_spec, clip_spec, P(), flat_spec, flat_spec, flat_spec, flat_spec, flat_spec),
        check_vma=False,
    )
```

```python
import functools
import math

import jax
import jax.numpy as jnp
from jax import lax
from jax.experimental import pallas as pl
from jax.experimental.pallas import tpu as pltpu
from jax.sharding import PartitionSpec as P

F32 = jnp.float32
BF16 = jnp.bfloat16
TAPS = 7
HALF = TAPS // 2
PAD = 8
LANE = 128


def tdot(x, y):
    return lax.dot_general(x, y, (((0,), (0,)), ((), ())), preferred_element_type=F32)


def ntdot(x, y):
    return lax.dot_general(x, y, (((1,), (1,)), ((), ())), preferred_element_type=F32)


def block_kernel(length, width, hidden, rows, flat_rows):
    nblk = length // rows
    quads = width // LANE
    inv_w = 1.0 / width
    sqrt_half = math.sqrt(0.5)
    inv_sqrt_2pi = 1.0 / math.sqrt(2.0 * math.pi)

    def kernel(counts_ref, fr_ref, cot_ref, wrows_hbm, cw_ref, vec_ref, b1_ref,
               bo_ref, ig_ref, gflat_hbm, gcw_ref, gvec_ref, gb1_ref,
               xq, xhat_s, rstd_s, a_s, da_s, dq, gw1_s, gw2_s, flat_s, wb_s, w1_ref, w2_ref, sems):
        clip = pl.program_id(0)
        count = counts_ref[clip]

        @pl.when(clip == 0)
        def _weights():
            load = pltpu.make_async_copy(wrows_hbm.at[0:wb_s.shape[0], :], wb_s, sems.at[1])
            load.start()
            load.wait()
            wide = flat_s.at[0:wb_s.shape[0], :]
            wide[...] = wb_s[...].astype(F32)
            per1 = hidden // LANE
            per2 = width // LANE
            for j in range(per1):
                w1_ref[:, j * LANE:(j + 1) * LANE] = wide[pl.ds(j, width, stride=per1), :].astype(BF16)
            at = width * hidden // LANE
            for j in range(per2):
                w2_ref[:, j * LANE:(j + 1) * LANE] = wide[pl.ds(at + j, hidden, stride=per2), :].astype(BF16)

        @pl.when(clip == 0)
        def _init():
            gw1_s[...] = jnp.zeros_like(gw1_s)
            gw2_s[...] = jnp.zeros_like(gw2_s)
            gcw_ref[...] = jnp.zeros_like(gcw_ref)
            gvec_ref[...] = jnp.zeros_like(gvec_ref)
            gb1_ref[...] = jnp.zeros_like(gb1_ref)
            xq[0:PAD * quads, :] = jnp.zeros((PAD * quads, LANE), F32)
            xq[(PAD + length) * quads:, :] = jnp.zeros((PAD * quads, LANE), F32)
            dq[0:PAD * quads, :] = jnp.zeros((PAD * quads, LANE), F32)
            dq[(PAD + length) * quads:, :] = jnp.zeros((PAD * quads, LANE), F32)

        cw = cw_ref[...]
        conv_b = vec_ref[0:1, :]
        ln_g = vec_ref[1:2, :]
        ln_b = vec_ref[2:3, :]
        b_two = vec_ref[3:4, :]
        gamma = vec_ref[4:5, :]
        b_one = b1_ref[0:1, :]

        all_rows = lax.broadcasted_iota(jnp.int32, (length, 1), 0)
        xm_all = jnp.where(all_rows < count, fr_ref[0].astype(F32), 0.0)
        for q in range(quads):
            xq[pl.ds(PAD * quads + q, length, stride=quads), :] = xm_all[:, q * LANE:(q + 1) * LANE]

        def taps_of(buf, start):
            return jnp.concatenate(
                [buf[pl.ds(start * quads + q, rows, stride=quads), :] for q in range(quads)], axis=1)

        def fwd_block(b):
            r0 = pl.multiple_of(b * rows, rows)
            start = (PAD - HALF) * quads + r0 * quads
            conv = conv_b
            for k in range(TAPS):
                tap = jnp.concatenate(
                    [xq[pl.ds(start + k * quads + q, rows, stride=quads), :] for q in range(quads)], axis=1)
                conv = conv + cw[k:k + 1, :] * tap
            centre = jnp.sum(conv, axis=-1, keepdims=True) * inv_w
            shifted = conv - centre
            spread = jnp.sum(shifted * shifted, axis=-1, keepdims=True) * inv_w
            rstd = lax.rsqrt(spread + 1e-6)
            xhat = shifted * rstd
            xhat_s[pl.ds(r0, rows), :] = xhat
            rstd_s[pl.ds(r0, rows), :] = rstd
            a_s[pl.ds(r0, rows), :] = (xhat * ln_g + ln_b).astype(BF16)

        @pl.when(count > 0)
        def _first_block():
            fwd_block(0)

        bo_ref[...] = jnp.zeros_like(bo_ref)

        def chunk(c, carry):
            g_gamma, g_b2, g_b1 = carry
            r0 = pl.multiple_of(c * rows, rows)
            a = a_s[pl.ds(r0, rows), :]
            fwd_block(jnp.minimum(c + 1, nblk - 1))
            h1 = jnp.dot(a, w1_ref[...], preferred_element_type=F32) + b_one
            cdf = 0.5 * (1.0 + lax.erf(h1 * sqrt_half))
            hh = (h1 * cdf).astype(BF16)
            z = jnp.dot(hh, w2_ref[...], preferred_element_type=F32) + b_two
            live = (r0 + lax.broadcasted_iota(jnp.int32, (rows, 1), 0)) < count
            xin = fr_ref[0, pl.ds(r0, rows), :].astype(F32)
            bo_ref[0, pl.ds(r0, rows), :] = jnp.where(live, xin + gamma * z, 0.0).astype(BF16)
            dout = jnp.where(live, cot_ref[0, pl.ds(r0, rows), :].astype(F32), 0.0)
            g_gamma = g_gamma + jnp.sum(dout * z, axis=0, keepdims=True)
            dz = (gamma * dout).astype(BF16)
            g_b2 = g_b2 + jnp.sum(dz.astype(F32), axis=0, keepdims=True)
            gw2_s[...] += tdot(hh, dz)
            dhh = ntdot(dz, w2_ref[...])
            slope = cdf + h1 * (jnp.exp(-0.5 * (h1 * h1)) * inv_sqrt_2pi)
            dh1 = (dhh * slope).astype(BF16)
            g_b1 = g_b1 + jnp.sum(dh1.astype(F32), axis=0, keepdims=True)
            gw1_s[...] += tdot(a, dh1)
            da_s[pl.ds(r0, rows), :] = ntdot(dh1, w1_ref[...])
            return g_gamma, g_b2, g_b1

        nact = (count + rows - 1) // rows
        zero_d = jnp.zeros((1, width), F32)
        g_gamma, g_b2, g_b1 = lax.fori_loop(
            0, nact, chunk, (zero_d, zero_d, jnp.zeros((1, hidden), F32)))

        def dxm_block(b):
            r0 = b * rows
            base = PAD + r0 + HALF
            dxm = cw[0:1, :] * taps_of(dq, base)
            for k in range(1, TAPS):
                dxm = dxm + cw[k:k + 1, :] * taps_of(dq, base - k)
            live = (r0 + lax.broadcasted_iota(jnp.int32, (rows, 1), 0)) < count
            cot = cot_ref[0, r0:r0 + rows, :].astype(F32)
            ig_ref[0, r0:r0 + rows, :] = jnp.where(live, cot + dxm, 0.0)

        sums = [zero_d] * (3 + TAPS)
        for b in range(nblk):
            r0 = b * rows

            def _bwd_block(r0=r0):
                live = (r0 + lax.broadcasted_iota(jnp.int32, (rows, 1), 0)) < count
                da = jnp.where(live, da_s[r0:r0 + rows, :], 0.0)
                xhat = xhat_s[r0:r0 + rows, :]
                rstd = rstd_s[r0:r0 + rows, :]
                dn = da * ln_g
                m1 = jnp.sum(dn, axis=-1, keepdims=True) * inv_w
                m2 = jnp.sum(dn * xhat, axis=-1, keepdims=True) * inv_w
                dconv = jnp.where(live, rstd * (dn - m1 - xhat * m2), 0.0)
                for q in range(quads):
                    dq[pl.ds((PAD + r0) * quads + q, rows, stride=quads), :] = dconv[:, q * LANE:(q + 1) * LANE]
                part = [jnp.sum(dconv, axis=0, keepdims=True),
                        jnp.sum(da * xhat, axis=0, keepdims=True),
                        jnp.sum(da, axis=0, keepdims=True)]
                base = PAD + r0 - HALF
                for k in range(TAPS):
                    part.append(jnp.sum(dconv * taps_of(xq, base + k), axis=0, keepdims=True))
                return part

            active = r0 < count
            part = lax.cond(active, _bwd_block, lambda: [zero_d] * (3 + TAPS))

            @pl.when(jnp.logical_not(active))
            def _idle():
                dq[(PAD + r0) * quads:(PAD + r0 + rows) * quads, :] = jnp.zeros((rows * quads, LANE), F32)
                ig_ref[0, r0:r0 + rows, :] = jnp.zeros((rows, width), F32)

            sums = [s + p for s, p in zip(sums, part)]
            if b >= 1:
                @pl.when((b - 1) * rows < count)
                def _prev(b=b):
                    dxm_block(b - 1)

        @pl.when((nblk - 1) * rows < count)
        def _last():
            dxm_block(nblk - 1)

        gvec_ref[0:1, :] += sums[0]
        gvec_ref[1:2, :] += sums[1]
        gvec_ref[2:3, :] += sums[2]
        gvec_ref[3:4, :] += g_b2
        gvec_ref[4:5, :] += g_gamma
        for k in range(TAPS):
            gcw_ref[k:k + 1, :] += sums[3 + k]
        gb1_ref[0:1, :] += g_b1

        @pl.when(clip == pl.num_programs(0) - 1)
        def _flush():
            per1 = hidden // LANE
            per2 = width // LANE
            for j in range(per1):
                flat_s[pl.ds(j, width, stride=per1), :] = gw1_s[:, j * LANE:(j + 1) * LANE]
            at = width * hidden // LANE
            for j in range(per2):
                flat_s[pl.ds(at + j, hidden, stride=per2), :] = gw2_s[:, j * LANE:(j + 1) * LANE]
            at = 2 * at
            for q in range(per2):
                flat_s[pl.ds(at + q, TAPS, stride=per2), :] = gcw_ref[0:TAPS, q * LANE:(q + 1) * LANE]
            at = at + TAPS * per2
            for q in range(per2):
                flat_s[pl.ds(at + q, 5, stride=per2), :] = gvec_ref[0:5, q * LANE:(q + 1) * LANE]
            at = at + 5 * per2
            for j in range(per1):
                flat_s[at + j:at + j + 1, :] = gb1_ref[0:1, j * LANE:(j + 1) * LANE]
            at = at + per1
            flat_s[at:, :] = jnp.zeros((flat_rows - at, LANE), F32)
            out = pltpu.make_async_copy(flat_s, gflat_hbm, sems.at[0])
            out.start()
            out.wait()

    return kernel


def fused_block(frames, counts, cotangent, wrows, cw8, vec8, b1_8, flat_rows, rows=256):
    clips, length, width = frames.shape
    hidden = cw8.shape[1] * 3
    kernel = block_kernel(length, width, hidden, rows, flat_rows)
    clip_spec = pl.BlockSpec((1, length, width), lambda i, c: (i, 0, 0))
    fixed = lambda shape: pl.BlockSpec(shape, lambda i, c: (0, 0))
    grid_spec = pltpu.PrefetchScalarGridSpec(
        num_scalar_prefetch=1,
        grid=(clips,),
        in_specs=[clip_spec, clip_spec, pl.BlockSpec(memory_space=pl.ANY),
                  fixed((8, width)), fixed((8, width)), fixed((8, hidden))],
        out_specs=[clip_spec, clip_spec,
                   pl.BlockSpec(memory_space=pl.ANY),
                   fixed((8, width)), fixed((8, width)), fixed((8, hidden))],
        scratch_shapes=[
            pltpu.VMEM(((length + 2 * PAD) * (width // LANE), LANE), F32),
            pltpu.VMEM((length, width), F32),
            pltpu.VMEM((length, 1), F32),
            pltpu.VMEM((length, width), BF16),
            pltpu.VMEM((length, width), F32),
            pltpu.VMEM(((length + 2 * PAD) * (width // LANE), LANE), F32),
            pltpu.VMEM((width, hidden), F32),
            pltpu.VMEM((hidden, width), F32),
            pltpu.VMEM((flat_rows, LANE), F32),
            pltpu.VMEM((2 * width * hidden // LANE, LANE), BF16),
            pltpu.VMEM((width, hidden), BF16),
            pltpu.VMEM((hidden, width), BF16),
            pltpu.SemaphoreType.DMA((2,)),
        ],
    )
    flops = 12 * clips * length * width * hidden
    cost = pl.CostEstimate(flops=flops, transcendentals=2 * clips * length * hidden,
                           bytes_accessed=clips * length * width * 8 + 4 * width * hidden * 4)
    return pl.pallas_call(
        kernel,
        grid_spec=grid_spec,
        out_shape=[
            jax.ShapeDtypeStruct((clips, length, width), BF16),
            jax.ShapeDtypeStruct((clips, length, width), F32),
            jax.ShapeDtypeStruct((flat_rows, LANE), F32),
            jax.ShapeDtypeStruct((8, width), F32),
            jax.ShapeDtypeStruct((8, width), F32),
            jax.ShapeDtypeStruct((8, hidden), F32),
        ],
        compiler_params=pltpu.CompilerParams(
            dimension_semantics=("arbitrary",), vmem_limit_bytes=60 * 1024 * 1024),
        cost_estimate=cost,
    )(counts, frames, cotangent, wrows, cw8, vec8, b1_8)


def unpack(packed, width, hidden):
    shapes = [(width, hidden), (hidden, width), (TAPS, width), (width,), (width,), (width,), (width,), (width,), (hidden,)]
    pieces = []
    start_at = 0
    for shape in shapes:
        entries = 1
        for extent in shape:
            entries = entries * extent
        pieces.append(packed[start_at : start_at + entries].reshape(shape))
        start_at = start_at + entries
    return (tuple(pieces), start_at)


AXES = ("dp", "fsdp")
LANES = 128


def bit_order(mesh_sizes):
    dp_size, fsdp_size = mesh_sizes
    fsdp_bits = int(math.log2(fsdp_size))
    dp_bits = int(math.log2(dp_size))
    order = [0] + [fsdp_bits + b for b in range(dp_bits)] + list(range(1, fsdp_bits))
    return order, fsdp_bits + dp_bits


def swap_perm(devices, bit):
    return [(i, i ^ (1 << bit)) for i in range(devices)]


def split_orders(order):
    if len(order) < 3:
        return [order]
    other = [order[0], order[2], order[1]] + order[3:]
    return [order, other]


def tree_all_gather(shard, orders, nbits):
    me = lax.axis_index(AXES)
    devices = 1 << nbits
    rows = shard.shape[0]
    cuts = [rows * p // len(orders) for p in range(len(orders) + 1)]
    held = [shard[cuts[p]:cuts[p + 1]].reshape([1] * nbits + [-1, LANES]) for p in range(len(orders))]
    for step in range(nbits):
        for p, order in enumerate(orders):
            bit = order[step]
            other = lax.ppermute(held[p], AXES, swap_perm(devices, bit))
            upper = ((me >> bit) & 1) == 1
            held[p] = jnp.concatenate(
                [jnp.where(upper, other, held[p]), jnp.where(upper, held[p], other)], axis=nbits - 1 - bit)
    parts = [h.reshape(devices, -1, LANES) for h in held]
    return jnp.concatenate(parts, axis=1).reshape(devices * rows, LANES)


def tree_reduce_scatter(full, orders, nbits):
    me = lax.axis_index(AXES)
    devices = 1 << nbits
    rows = full.shape[0] // devices
    cuts = [rows * p // len(orders) for p in range(len(orders) + 1)]
    if rows % 8 == 0:
        cuts = [c // 8 * 8 for c in cuts]
    shaped = full.reshape([2] * nbits + [rows, LANES])
    held = [shaped[..., cuts[p]:cuts[p + 1], :] for p in range(len(orders))]
    held_bits = [[nbits - 1 - a for a in range(nbits)] for _ in orders]
    for step in range(nbits):
        for p, order in enumerate(orders):
            bit = order[step]
            axis = held_bits[p].index(bit)
            mine = (me >> bit) & 1
            keep = lax.dynamic_index_in_dim(held[p], mine, axis=axis, keepdims=False)
            send = lax.dynamic_index_in_dim(held[p], 1 - mine, axis=axis, keepdims=False)
            held[p] = keep + lax.ppermute(send, AXES, swap_perm(devices, bit))
            held_bits[p].pop(axis)
    return jnp.concatenate(held, axis=0)


def tree_all_sum(value, order, nbits):
    devices = 1 << nbits
    for bit in reversed(order):
        value = value + lax.ppermute(value, AXES, swap_perm(devices, bit))
    return value


def body(frames, counts, cotangent, master, momentum, average, disc_grads, mesh_sizes=None):
    order, nbits = bit_order(mesh_sizes)
    devices = 1 << nbits
    clips, length, width = frames.shape
    hidden = 3 * width
    rows = clips * length
    local = master.shape[0]
    flat_size = local * devices
    total_frames = jnp.float32(rows * devices)
    rounded = master.astype(BF16).reshape(local // LANES, LANES)
    packed_rows = tree_all_gather(rounded, [o[::-1] for o in split_orders(order)], nbits)
    weight_rows = 2 * width * hidden // LANES
    small_rows = -(-(TAPS * width + 5 * width + hidden) // LANES)
    small = packed_rows[weight_rows:weight_rows + small_rows].reshape(-1)
    conv_w = small[: TAPS * width].reshape(TAPS, width)
    at = TAPS * width
    conv_b, ln_g, ln_b, b_two, gamma = [small[at + i * width: at + (i + 1) * width] for i in range(5)]
    at = at + 5 * width
    b_one = small[at: at + hidden]
    cw8 = jnp.zeros((8, width), F32).at[:TAPS].set(conv_w.astype(F32))
    vec8 = jnp.concatenate(
        [jnp.stack([conv_b, ln_g, ln_b, b_two, gamma]).astype(F32), jnp.zeros((3, width), F32)])
    b1_8 = jnp.zeros((8, hidden), F32).at[0].set(b_one.astype(F32))
    shard_rows = local // LANES
    padded_rows = -(-shard_rows // 8) * 8
    aligned = padded_rows != shard_rows and (padded_rows - shard_rows) * (devices - 1) <= padded_rows
    block = padded_rows if aligned else shard_rows
    block_out, input_grad, grad_full, _, _, _ = fused_block(
        frames, counts, cotangent, packed_rows, cw8, vec8, b1_8, devices * block)
    grad_block = tree_reduce_scatter(grad_full, split_orders(order), nbits)
    if aligned:
        me = lax.axis_index(AXES)
        prev = lax.ppermute(grad_block, AXES, [(i, (i + 1) % devices) for i in range(devices)])
        both = jnp.concatenate([prev, grad_block])
        grad_shard = lax.dynamic_slice_in_dim(both, block - (block - shard_rows) * me, shard_rows, axis=0)
    else:
        grad_shard = grad_block
    disc_rows = jnp.sum((disc_grads * disc_grads).reshape(-1, LANES), axis=0, keepdims=True)
    own_rows = jnp.sum(grad_block * grad_block, axis=0, keepdims=True)
    squares = jnp.broadcast_to(own_rows + disc_rows, (8, LANES))
    squares = tree_all_sum(squares, order, nbits)
    grad_norm = jnp.sqrt(jnp.sum(squares[0]))
    grad_shard = grad_shard.reshape(-1)
    clipped = grad_shard * jnp.minimum(1.0, 20.0 * jnp.sqrt(total_frames) / (grad_norm + 1e-06))
    new_momentum = 0.9 * momentum + clipped
    new_master = master - (clipped + 0.9 * new_momentum) / jnp.sqrt(total_frames)
    new_average = 0.99 * average + 0.01 * new_master
    return (
        block_out,
        input_grad,
        grad_norm,
        new_master,
        new_momentum,
        new_average,
        new_master.astype(BF16),
        new_average.astype(BF16),
    )


def solution(mesh):
    clip_spec = P(("dp", "fsdp"), None, None)
    flat_spec = P(("dp", "fsdp"))
    mesh_sizes = (mesh.shape["dp"], mesh.shape["fsdp"])
    return jax.shard_map(
        functools.partial(body, mesh_sizes=mesh_sizes),
        mesh=mesh,
        in_specs=(clip_spec, flat_spec, clip_spec, flat_spec, flat_spec, flat_spec, flat_spec),
        out_specs=(clip_spec, clip_spec, P(), flat_spec, flat_spec, flat_spec, flat_spec, flat_spec),
        check_vma=False,
    )
```

```python
import functools
import math

import jax
import jax.numpy as jnp
from jax import lax
from jax.experimental import pallas as pl
from jax.experimental.pallas import tpu as pltpu
from jax.sharding import PartitionSpec as P

F32 = jnp.float32
BF16 = jnp.bfloat16
TAPS = 7
HALF = TAPS // 2
PAD = 8
LANE = 128


def tdot(x, y):
    return lax.dot_general(x, y, (((0,), (0,)), ((), ())), preferred_element_type=F32)


def ntdot(x, y):
    return lax.dot_general(x, y, (((1,), (1,)), ((), ())), preferred_element_type=F32)


def block_kernel(length, width, hidden, rows, flat_rows):
    nblk = length // rows
    quads = width // LANE
    inv_w = 1.0 / width
    sqrt_half = math.sqrt(0.5)
    inv_sqrt_2pi = 1.0 / math.sqrt(2.0 * math.pi)

    def kernel(counts_ref, fr_ref, cot_ref, wrows_hbm, cw_ref, vec_ref, b1_ref,
               bo_ref, ig_ref, gflat_hbm, gcw_ref, gvec_ref, gb1_ref,
               xq, xhat_s, rstd_s, a_s, da_s, dq, gw1_s, gw2_s, flat_s, wb_s, w1_ref, w2_ref, sems):
        clip = pl.program_id(0)
        count = counts_ref[clip]

        @pl.when(clip == 0)
        def _weights():
            load = pltpu.make_async_copy(wrows_hbm.at[0:wb_s.shape[0], :], wb_s, sems.at[1])
            load.start()
            load.wait()
            wide = flat_s.at[0:wb_s.shape[0], :]
            wide[...] = wb_s[...].astype(F32)
            per1 = hidden // LANE
            per2 = width // LANE
            for j in range(per1):
                w1_ref[:, j * LANE:(j + 1) * LANE] = wide[pl.ds(j, width, stride=per1), :].astype(BF16)
            at = width * hidden // LANE
            for j in range(per2):
                w2_ref[:, j * LANE:(j + 1) * LANE] = wide[pl.ds(at + j, hidden, stride=per2), :].astype(BF16)

        @pl.when(clip == 0)
        def _init():
            gw1_s[...] = jnp.zeros_like(gw1_s)
            gw2_s[...] = jnp.zeros_like(gw2_s)
            gcw_ref[...] = jnp.zeros_like(gcw_ref)
            gvec_ref[...] = jnp.zeros_like(gvec_ref)
            gb1_ref[...] = jnp.zeros_like(gb1_ref)
            xq[0:PAD * quads, :] = jnp.zeros((PAD * quads, LANE), F32)
            xq[(PAD + length) * quads:, :] = jnp.zeros((PAD * quads, LANE), F32)
            dq[0:PAD * quads, :] = jnp.zeros((PAD * quads, LANE), F32)
            dq[(PAD + length) * quads:, :] = jnp.zeros((PAD * quads, LANE), F32)

        cw = cw_ref[...]
        conv_b = vec_ref[0:1, :]
        ln_g = vec_ref[1:2, :]
        ln_b = vec_ref[2:3, :]
        b_two = vec_ref[3:4, :]
        gamma = vec_ref[4:5, :]
        b_one = b1_ref[0:1, :]

        all_rows = lax.broadcasted_iota(jnp.int32, (length, 1), 0)
        xm_all = jnp.where(all_rows < count, fr_ref[0].astype(F32), 0.0)
        for q in range(quads):
            xq[pl.ds(PAD * quads + q, length, stride=quads), :] = xm_all[:, q * LANE:(q + 1) * LANE]

        def taps_of(buf, start):
            return jnp.concatenate(
                [buf[pl.ds(start * quads + q, rows, stride=quads), :] for q in range(quads)], axis=1)

        def fwd_block(b):
            r0 = pl.multiple_of(b * rows, rows)
            start = (PAD - HALF) * quads + r0 * quads
            conv = conv_b
            for k in range(TAPS):
                tap = jnp.concatenate(
                    [xq[pl.ds(start + k * quads + q, rows, stride=quads), :] for q in range(quads)], axis=1)
                conv = conv + cw[k:k + 1, :] * tap
            centre = jnp.sum(conv, axis=-1, keepdims=True) * inv_w
            shifted = conv - centre
            spread = jnp.sum(shifted * shifted, axis=-1, keepdims=True) * inv_w
            rstd = lax.rsqrt(spread + 1e-6)
            xhat = shifted * rstd
            xhat_s[pl.ds(r0, rows), :] = xhat
            rstd_s[pl.ds(r0, rows), :] = rstd
            a_s[pl.ds(r0, rows), :] = (xhat * ln_g + ln_b).astype(BF16)

        @pl.when(count > 0)
        def _first_block():
            fwd_block(0)

        bo_ref[...] = jnp.zeros_like(bo_ref)

        def chunk(c, carry):
            g_gamma, g_b2, g_b1 = carry
            r0 = pl.multiple_of(c * rows, rows)
            a = a_s[pl.ds(r0, rows), :]
            fwd_block(jnp.minimum(c + 1, nblk - 1))
            h1 = jnp.dot(a, w1_ref[...], preferred_element_type=F32) + b_one
            cdf = 0.5 * (1.0 + lax.erf(h1 * sqrt_half))
            hh = (h1 * cdf).astype(BF16)
            z = jnp.dot(hh, w2_ref[...], preferred_element_type=F32) + b_two
            live = (r0 + lax.broadcasted_iota(jnp.int32, (rows, 1), 0)) < count
            xin = fr_ref[0, pl.ds(r0, rows), :].astype(F32)
            bo_ref[0, pl.ds(r0, rows), :] = jnp.where(live, xin + gamma * z, 0.0).astype(BF16)
            dout = jnp.where(live, cot_ref[0, pl.ds(r0, rows), :].astype(F32), 0.0)
            g_gamma = g_gamma + jnp.sum(dout * z, axis=0, keepdims=True)
            dz = (gamma * dout).astype(BF16)
            g_b2 = g_b2 + jnp.sum(dz.astype(F32), axis=0, keepdims=True)
            gw2_s[...] += tdot(hh, dz)
            dhh = ntdot(dz, w2_ref[...])
            slope = cdf + h1 * (jnp.exp(-0.5 * (h1 * h1)) * inv_sqrt_2pi)
            dh1 = (dhh * slope).astype(BF16)
            g_b1 = g_b1 + jnp.sum(dh1.astype(F32), axis=0, keepdims=True)
            gw1_s[...] += tdot(a, dh1)
            da_s[pl.ds(r0, rows), :] = ntdot(dh1, w1_ref[...])
            return g_gamma, g_b2, g_b1

        nact = (count + rows - 1) // rows
        zero_d = jnp.zeros((1, width), F32)
        g_gamma, g_b2, g_b1 = lax.fori_loop(
            0, nact, chunk, (zero_d, zero_d, jnp.zeros((1, hidden), F32)))

        def dxm_block(b):
            r0 = b * rows
            base = PAD + r0 + HALF
            dxm = cw[0:1, :] * taps_of(dq, base)
            for k in range(1, TAPS):
                dxm = dxm + cw[k:k + 1, :] * taps_of(dq, base - k)
            live = (r0 + lax.broadcasted_iota(jnp.int32, (rows, 1), 0)) < count
            cot = cot_ref[0, r0:r0 + rows, :].astype(F32)
            ig_ref[0, r0:r0 + rows, :] = jnp.where(live, cot + dxm, 0.0)

        sums = [zero_d] * (3 + TAPS)
        for b in range(nblk):
            r0 = b * rows

            def _bwd_block(r0=r0):
                live = (r0 + lax.broadcasted_iota(jnp.int32, (rows, 1), 0)) < count
                da = jnp.where(live, da_s[r0:r0 + rows, :], 0.0)
                xhat = xhat_s[r0:r0 + rows, :]
                rstd = rstd_s[r0:r0 + rows, :]
                dn = da * ln_g
                m1 = jnp.sum(dn, axis=-1, keepdims=True) * inv_w
                m2 = jnp.sum(dn * xhat, axis=-1, keepdims=True) * inv_w
                dconv = jnp.where(live, rstd * (dn - m1 - xhat * m2), 0.0)
                for q in range(quads):
                    dq[pl.ds((PAD + r0) * quads + q, rows, stride=quads), :] = dconv[:, q * LANE:(q + 1) * LANE]
                part = [jnp.sum(dconv, axis=0, keepdims=True),
                        jnp.sum(da * xhat, axis=0, keepdims=True),
                        jnp.sum(da, axis=0, keepdims=True)]
                base = PAD + r0 - HALF
                for k in range(TAPS):
                    part.append(jnp.sum(dconv * taps_of(xq, base + k), axis=0, keepdims=True))
                return part

            active = r0 < count
            part = lax.cond(active, _bwd_block, lambda: [zero_d] * (3 + TAPS))

            @pl.when(jnp.logical_not(active))
            def _idle():
                dq[(PAD + r0) * quads:(PAD + r0 + rows) * quads, :] = jnp.zeros((rows * quads, LANE), F32)
                ig_ref[0, r0:r0 + rows, :] = jnp.zeros((rows, width), F32)

            sums = [s + p for s, p in zip(sums, part)]
            if b >= 1:
                @pl.when((b - 1) * rows < count)
                def _prev(b=b):
                    dxm_block(b - 1)

        @pl.when((nblk - 1) * rows < count)
        def _last():
            dxm_block(nblk - 1)

        gvec_ref[0:1, :] += sums[0]
        gvec_ref[1:2, :] += sums[1]
        gvec_ref[2:3, :] += sums[2]
        gvec_ref[3:4, :] += g_b2
        gvec_ref[4:5, :] += g_gamma
        for k in range(TAPS):
            gcw_ref[k:k + 1, :] += sums[3 + k]
        gb1_ref[0:1, :] += g_b1

        @pl.when(clip == pl.num_programs(0) - 1)
        def _flush():
            per1 = hidden // LANE
            per2 = width // LANE
            for j in range(per1):
                flat_s[pl.ds(j, width, stride=per1), :] = gw1_s[:, j * LANE:(j + 1) * LANE]
            at = width * hidden // LANE
            for j in range(per2):
                flat_s[pl.ds(at + j, hidden, stride=per2), :] = gw2_s[:, j * LANE:(j + 1) * LANE]
            at = 2 * at
            for q in range(per2):
                flat_s[pl.ds(at + q, TAPS, stride=per2), :] = gcw_ref[0:TAPS, q * LANE:(q + 1) * LANE]
            at = at + TAPS * per2
            for q in range(per2):
                flat_s[pl.ds(at + q, 5, stride=per2), :] = gvec_ref[0:5, q * LANE:(q + 1) * LANE]
            at = at + 5 * per2
            for j in range(per1):
                flat_s[at + j:at + j + 1, :] = gb1_ref[0:1, j * LANE:(j + 1) * LANE]
            at = at + per1
            flat_s[at:, :] = jnp.zeros((flat_rows - at, LANE), F32)
            out = pltpu.make_async_copy(flat_s, gflat_hbm, sems.at[0])
            out.start()
            out.wait()

    return kernel


def fused_block(frames, counts, cotangent, wrows, cw8, vec8, b1_8, flat_rows, rows=256):
    clips, length, width = frames.shape
    hidden = cw8.shape[1] * 3
    kernel = block_kernel(length, width, hidden, rows, flat_rows)
    clip_spec = pl.BlockSpec((1, length, width), lambda i, c: (i, 0, 0))
    fixed = lambda shape: pl.BlockSpec(shape, lambda i, c: (0, 0))
    grid_spec = pltpu.PrefetchScalarGridSpec(
        num_scalar_prefetch=1,
        grid=(clips,),
        in_specs=[clip_spec, clip_spec, pl.BlockSpec(memory_space=pl.ANY),
                  fixed((8, width)), fixed((8, width)), fixed((8, hidden))],
        out_specs=[clip_spec, clip_spec,
                   pl.BlockSpec(memory_space=pl.ANY),
                   fixed((8, width)), fixed((8, width)), fixed((8, hidden))],
        scratch_shapes=[
            pltpu.VMEM(((length + 2 * PAD) * (width // LANE), LANE), F32),
            pltpu.VMEM((length, width), F32),
            pltpu.VMEM((length, 1), F32),
            pltpu.VMEM((length, width), BF16),
            pltpu.VMEM((length, width), F32),
            pltpu.VMEM(((length + 2 * PAD) * (width // LANE), LANE), F32),
            pltpu.VMEM((width, hidden), F32),
            pltpu.VMEM((hidden, width), F32),
            pltpu.VMEM((flat_rows, LANE), F32),
            pltpu.VMEM((2 * width * hidden // LANE, LANE), BF16),
            pltpu.VMEM((width, hidden), BF16),
            pltpu.VMEM((hidden, width), BF16),
            pltpu.SemaphoreType.DMA((2,)),
        ],
    )
    flops = 12 * clips * length * width * hidden
    cost = pl.CostEstimate(flops=flops, transcendentals=2 * clips * length * hidden,
                           bytes_accessed=clips * length * width * 8 + 4 * width * hidden * 4)
    return pl.pallas_call(
        kernel,
        grid_spec=grid_spec,
        out_shape=[
            jax.ShapeDtypeStruct((clips, length, width), BF16),
            jax.ShapeDtypeStruct((clips, length, width), F32),
            jax.ShapeDtypeStruct((flat_rows, LANE), F32),
            jax.ShapeDtypeStruct((8, width), F32),
            jax.ShapeDtypeStruct((8, width), F32),
            jax.ShapeDtypeStruct((8, hidden), F32),
        ],
        compiler_params=pltpu.CompilerParams(
            dimension_semantics=("arbitrary",), vmem_limit_bytes=60 * 1024 * 1024),
        cost_estimate=cost,
    )(counts, frames, cotangent, wrows, cw8, vec8, b1_8)


def unpack(packed, width, hidden):
    shapes = [(width, hidden), (hidden, width), (TAPS, width), (width,), (width,), (width,), (width,), (width,), (hidden,)]
    pieces = []
    start_at = 0
    for shape in shapes:
        entries = 1
        for extent in shape:
            entries = entries * extent
        pieces.append(packed[start_at : start_at + entries].reshape(shape))
        start_at = start_at + entries
    return (tuple(pieces), start_at)


AXES = ("dp", "fsdp")
LANES = 128


def bit_order(mesh_sizes):
    dp_size, fsdp_size = mesh_sizes
    fsdp_bits = int(math.log2(fsdp_size))
    dp_bits = int(math.log2(dp_size))
    order = [0] + [fsdp_bits + b for b in range(dp_bits)] + list(range(1, fsdp_bits))
    return order, fsdp_bits + dp_bits


def swap_perm(devices, bit):
    return [(i, i ^ (1 << bit)) for i in range(devices)]


def split_orders(order):
    if len(order) < 3:
        return [order]
    other = [order[0], order[2], order[1]] + order[3:]
    return [order, other]


def tree_all_gather(shard, orders, nbits):
    me = lax.axis_index(AXES)
    devices = 1 << nbits
    rows = shard.shape[0]
    cuts = [rows * p // len(orders) for p in range(len(orders) + 1)]
    if rows >= 16 * len(orders):
        cuts = [c // 16 * 16 for c in cuts[:-1]] + [rows]
    held = [shard[cuts[p]:cuts[p + 1]].reshape([1] * nbits + [-1, LANES]) for p in range(len(orders))]
    for step in range(nbits):
        for p, order in enumerate(orders):
            bit = order[step]
            other = lax.ppermute(held[p], AXES, swap_perm(devices, bit))
            upper = ((me >> bit) & 1) == 1
            held[p] = jnp.concatenate(
                [jnp.where(upper, other, held[p]), jnp.where(upper, held[p], other)], axis=nbits - 1 - bit)
    parts = [h.reshape(devices, -1, LANES) for h in held]
    return jnp.concatenate(parts, axis=1).reshape(devices * rows, LANES)


def tree_reduce_scatter(full, orders, nbits):
    me = lax.axis_index(AXES)
    devices = 1 << nbits
    rows = full.shape[0] // devices
    cuts = [rows * p // len(orders) for p in range(len(orders) + 1)]
    if rows % 8 == 0:
        cuts = [c // 8 * 8 for c in cuts]
    shaped = full.reshape([2] * nbits + [rows, LANES])
    held = [shaped[..., cuts[p]:cuts[p + 1], :] for p in range(len(orders))]
    held_bits = [[nbits - 1 - a for a in range(nbits)] for _ in orders]
    for step in range(nbits):
        for p, order in enumerate(orders):
            bit = order[step]
            axis = held_bits[p].index(bit)
            mine = (me >> bit) & 1
            keep = lax.dynamic_index_in_dim(held[p], mine, axis=axis, keepdims=False)
            send = lax.dynamic_index_in_dim(held[p], 1 - mine, axis=axis, keepdims=False)
            held[p] = keep + lax.ppermute(send, AXES, swap_perm(devices, bit))
            held_bits[p].pop(axis)
    return jnp.concatenate(held, axis=0)


def tree_all_sum(value, order, nbits):
    devices = 1 << nbits
    for bit in reversed(order):
        value = value + lax.ppermute(value, AXES, swap_perm(devices, bit))
    return value


def body(frames, counts, cotangent, master, momentum, average, disc_grads, mesh_sizes=None):
    order, nbits = bit_order(mesh_sizes)
    devices = 1 << nbits
    clips, length, width = frames.shape
    hidden = 3 * width
    rows = clips * length
    local = master.shape[0]
    flat_size = local * devices
    total_frames = jnp.float32(rows * devices)
    rounded = master.astype(BF16).reshape(local // LANES, LANES)
    packed_rows = tree_all_gather(rounded, [o[::-1] for o in split_orders(order)], nbits)
    weight_rows = 2 * width * hidden // LANES
    small_rows = -(-(TAPS * width + 5 * width + hidden) // LANES)
    small = packed_rows[weight_rows:weight_rows + small_rows].reshape(-1)
    conv_w = small[: TAPS * width].reshape(TAPS, width)
    at = TAPS * width
    conv_b, ln_g, ln_b, b_two, gamma = [small[at + i * width: at + (i + 1) * width] for i in range(5)]
    at = at + 5 * width
    b_one = small[at: at + hidden]
    cw8 = jnp.zeros((8, width), F32).at[:TAPS].set(conv_w.astype(F32))
    vec8 = jnp.concatenate(
        [jnp.stack([conv_b, ln_g, ln_b, b_two, gamma]).astype(F32), jnp.zeros((3, width), F32)])
    b1_8 = jnp.zeros((8, hidden), F32).at[0].set(b_one.astype(F32))
    shard_rows = local // LANES
    padded_rows = -(-shard_rows // 8) * 8
    aligned = padded_rows != shard_rows and (padded_rows - shard_rows) * (devices - 1) <= padded_rows
    block = padded_rows if aligned else shard_rows
    block_out, input_grad, grad_full, _, _, _ = fused_block(
        frames, counts, cotangent, packed_rows, cw8, vec8, b1_8, devices * block)
    grad_block = tree_reduce_scatter(grad_full, split_orders(order), nbits)
    if aligned:
        me = lax.axis_index(AXES)
        prev = lax.ppermute(grad_block, AXES, [(i, (i + 1) % devices) for i in range(devices)])
        both = jnp.concatenate([prev, grad_block])
        grad_shard = lax.dynamic_slice_in_dim(both, block - (block - shard_rows) * me, shard_rows, axis=0)
    else:
        grad_shard = grad_block
    disc_rows = jnp.sum((disc_grads * disc_grads).reshape(-1, LANES), axis=0, keepdims=True)
    own_rows = jnp.sum(grad_block * grad_block, axis=0, keepdims=True)
    squares = jnp.broadcast_to(own_rows + disc_rows, (8, LANES))
    squares = tree_all_sum(squares, order, nbits)
    grad_norm = jnp.sqrt(jnp.sum(squares[0]))
    grad_shard = grad_shard.reshape(-1)
    clipped = grad_shard * jnp.minimum(1.0, 20.0 * jnp.sqrt(total_frames) / (grad_norm + 1e-06))
    new_momentum = 0.9 * momentum + clipped
    new_master = master - (clipped + 0.9 * new_momentum) / jnp.sqrt(total_frames)
    new_average = 0.99 * average + 0.01 * new_master
    return (
        block_out,
        input_grad,
        grad_norm,
        new_master,
        new_momentum,
        new_average,
        new_master.astype(BF16),
        new_average.astype(BF16),
    )


def solution(mesh):
    clip_spec = P(("dp", "fsdp"), None, None)
    flat_spec = P(("dp", "fsdp"))
    mesh_sizes = (mesh.shape["dp"], mesh.shape["fsdp"])
    return jax.shard_map(
        functools.partial(body, mesh_sizes=mesh_sizes),
        mesh=mesh,
        in_specs=(clip_spec, flat_spec, clip_spec, flat_spec, flat_spec, flat_spec, flat_spec),
        out_specs=(clip_spec, clip_spec, P(), flat_spec, flat_spec, flat_spec, flat_spec, flat_spec),
        check_vma=False,
    )
```

```python
import functools
import math

import jax
import jax.numpy as jnp
from jax import lax
from jax.experimental import pallas as pl
from jax.experimental.pallas import tpu as pltpu
from jax.sharding import PartitionSpec as P

F32 = jnp.float32
BF16 = jnp.bfloat16
TAPS = 7
HALF = TAPS // 2
PAD = 8
LANE = 128


def tdot(x, y):
    return lax.dot_general(x, y, (((0,), (0,)), ((), ())), preferred_element_type=F32)


def ntdot(x, y):
    return lax.dot_general(x, y, (((1,), (1,)), ((), ())), preferred_element_type=F32)


def block_kernel(length, width, hidden, rows, flat_rows, split):
    nblk = length // rows
    quads = width // LANE
    inv_w = 1.0 / width
    sqrt_half = math.sqrt(0.5)
    inv_sqrt_2pi = 1.0 / math.sqrt(2.0 * math.pi)

    def kernel(counts_ref, bit_ref, fr_ref, cot_ref, wrows_hbm, cw_ref, vec_ref, b1_ref, *refs):
        n_out = 2 if split else 1
        bo_ref, ig_ref = refs[0:2]
        g_refs = refs[2:2 + n_out]
        gcw_ref, gvec_ref, gb1_ref = refs[2 + n_out:5 + n_out]
        (xq, xhat_s, rstd_s, a_s, da_s, dq, gw1_s, gw2_s, flat_s, wb_s, w1_ref, w2_ref, sems) = refs[5 + n_out:]
        clip = pl.program_id(0)
        count = counts_ref[clip]

        @pl.when(clip == 0)
        def _weights():
            load = pltpu.make_async_copy(wrows_hbm.at[0:wb_s.shape[0], :], wb_s, sems.at[1])
            load.start()
            load.wait()
            wide = flat_s.at[0:wb_s.shape[0], :]
            wide[...] = wb_s[...].astype(F32)
            per1 = hidden // LANE
            per2 = width // LANE
            for j in range(per1):
                w1_ref[:, j * LANE:(j + 1) * LANE] = wide[pl.ds(j, width, stride=per1), :].astype(BF16)
            at = width * hidden // LANE
            for j in range(per2):
                w2_ref[:, j * LANE:(j + 1) * LANE] = wide[pl.ds(at + j, hidden, stride=per2), :].astype(BF16)

        @pl.when(clip == 0)
        def _init():
            gw1_s[...] = jnp.zeros_like(gw1_s)
            gw2_s[...] = jnp.zeros_like(gw2_s)
            gcw_ref[...] = jnp.zeros_like(gcw_ref)
            gvec_ref[...] = jnp.zeros_like(gvec_ref)
            gb1_ref[...] = jnp.zeros_like(gb1_ref)
            xq[0:PAD * quads, :] = jnp.zeros((PAD * quads, LANE), F32)
            xq[(PAD + length) * quads:, :] = jnp.zeros((PAD * quads, LANE), F32)
            dq[0:PAD * quads, :] = jnp.zeros((PAD * quads, LANE), F32)
            dq[(PAD + length) * quads:, :] = jnp.zeros((PAD * quads, LANE), F32)

        cw = cw_ref[...]
        conv_b = vec_ref[0:1, :]
        ln_g = vec_ref[1:2, :]
        ln_b = vec_ref[2:3, :]
        b_two = vec_ref[3:4, :]
        gamma = vec_ref[4:5, :]
        b_one = b1_ref[0:1, :]

        all_rows = lax.broadcasted_iota(jnp.int32, (length, 1), 0)
        xm_all = jnp.where(all_rows < count, fr_ref[0].astype(F32), 0.0)
        for q in range(quads):
            xq[pl.ds(PAD * quads + q, length, stride=quads), :] = xm_all[:, q * LANE:(q + 1) * LANE]

        def taps_of(buf, start):
            return jnp.concatenate(
                [buf[pl.ds(start * quads + q, rows, stride=quads), :] for q in range(quads)], axis=1)

        def fwd_block(b):
            r0 = pl.multiple_of(b * rows, rows)
            start = (PAD - HALF) * quads + r0 * quads
            conv = conv_b
            for k in range(TAPS):
                tap = jnp.concatenate(
                    [xq[pl.ds(start + k * quads + q, rows, stride=quads), :] for q in range(quads)], axis=1)
                conv = conv + cw[k:k + 1, :] * tap
            centre = jnp.sum(conv, axis=-1, keepdims=True) * inv_w
            shifted = conv - centre
            spread = jnp.sum(shifted * shifted, axis=-1, keepdims=True) * inv_w
            rstd = lax.rsqrt(spread + 1e-6)
            xhat = shifted * rstd
            xhat_s[pl.ds(r0, rows), :] = xhat
            rstd_s[pl.ds(r0, rows), :] = rstd
            a_s[pl.ds(r0, rows), :] = (xhat * ln_g + ln_b).astype(BF16)

        @pl.when(count > 0)
        def _first_block():
            fwd_block(0)

        bo_ref[...] = jnp.zeros_like(bo_ref)

        def chunk(c, carry):
            g_gamma, g_b2, g_b1 = carry
            r0 = pl.multiple_of(c * rows, rows)
            a = a_s[pl.ds(r0, rows), :]
            fwd_block(jnp.minimum(c + 1, nblk - 1))
            h1 = jnp.dot(a, w1_ref[...], preferred_element_type=F32) + b_one
            cdf = 0.5 * (1.0 + lax.erf(h1 * sqrt_half))
            hh = (h1 * cdf).astype(BF16)
            z = jnp.dot(hh, w2_ref[...], preferred_element_type=F32) + b_two
            live = (r0 + lax.broadcasted_iota(jnp.int32, (rows, 1), 0)) < count
            xin = fr_ref[0, pl.ds(r0, rows), :].astype(F32)
            bo_ref[0, pl.ds(r0, rows), :] = jnp.where(live, xin + gamma * z, 0.0).astype(BF16)
            dout = jnp.where(live, cot_ref[0, pl.ds(r0, rows), :].astype(F32), 0.0)
            g_gamma = g_gamma + jnp.sum(dout * z, axis=0, keepdims=True)
            dz = (gamma * dout).astype(BF16)
            g_b2 = g_b2 + jnp.sum(dz.astype(F32), axis=0, keepdims=True)
            gw2_s[...] += tdot(hh, dz)
            dhh = ntdot(dz, w2_ref[...])
            slope = cdf + h1 * (jnp.exp(-0.5 * (h1 * h1)) * inv_sqrt_2pi)
            dh1 = (dhh * slope).astype(BF16)
            g_b1 = g_b1 + jnp.sum(dh1.astype(F32), axis=0, keepdims=True)
            gw1_s[...] += tdot(a, dh1)
            da_s[pl.ds(r0, rows), :] = ntdot(dh1, w1_ref[...])
            return g_gamma, g_b2, g_b1

        nact = (count + rows - 1) // rows
        zero_d = jnp.zeros((1, width), F32)
        g_gamma, g_b2, g_b1 = lax.fori_loop(
            0, nact, chunk, (zero_d, zero_d, jnp.zeros((1, hidden), F32)))

        def dxm_block(b):
            r0 = b * rows
            base = PAD + r0 + HALF
            dxm = cw[0:1, :] * taps_of(dq, base)
            for k in range(1, TAPS):
                dxm = dxm + cw[k:k + 1, :] * taps_of(dq, base - k)
            live = (r0 + lax.broadcasted_iota(jnp.int32, (rows, 1), 0)) < count
            cot = cot_ref[0, r0:r0 + rows, :].astype(F32)
            ig_ref[0, r0:r0 + rows, :] = jnp.where(live, cot + dxm, 0.0)

        sums = [zero_d] * (3 + TAPS)
        for b in range(nblk):
            r0 = b * rows

            def _bwd_block(r0=r0):
                live = (r0 + lax.broadcasted_iota(jnp.int32, (rows, 1), 0)) < count
                da = jnp.where(live, da_s[r0:r0 + rows, :], 0.0)
                xhat = xhat_s[r0:r0 + rows, :]
                rstd = rstd_s[r0:r0 + rows, :]
                dn = da * ln_g
                m1 = jnp.sum(dn, axis=-1, keepdims=True) * inv_w
                m2 = jnp.sum(dn * xhat, axis=-1, keepdims=True) * inv_w
                dconv = jnp.where(live, rstd * (dn - m1 - xhat * m2), 0.0)
                for q in range(quads):
                    dq[pl.ds((PAD + r0) * quads + q, rows, stride=quads), :] = dconv[:, q * LANE:(q + 1) * LANE]
                part = [jnp.sum(dconv, axis=0, keepdims=True),
                        jnp.sum(da * xhat, axis=0, keepdims=True),
                        jnp.sum(da, axis=0, keepdims=True)]
                base = PAD + r0 - HALF
                for k in range(TAPS):
                    part.append(jnp.sum(dconv * taps_of(xq, base + k), axis=0, keepdims=True))
                return part

            active = r0 < count
            part = lax.cond(active, _bwd_block, lambda: [zero_d] * (3 + TAPS))

            @pl.when(jnp.logical_not(active))
            def _idle():
                dq[(PAD + r0) * quads:(PAD + r0 + rows) * quads, :] = jnp.zeros((rows * quads, LANE), F32)
                ig_ref[0, r0:r0 + rows, :] = jnp.zeros((rows, width), F32)

            sums = [s + p for s, p in zip(sums, part)]
            if b >= 1:
                @pl.when((b - 1) * rows < count)
                def _prev(b=b):
                    dxm_block(b - 1)

        @pl.when((nblk - 1) * rows < count)
        def _last():
            dxm_block(nblk - 1)

        gvec_ref[0:1, :] += sums[0]
        gvec_ref[1:2, :] += sums[1]
        gvec_ref[2:3, :] += sums[2]
        gvec_ref[3:4, :] += g_b2
        gvec_ref[4:5, :] += g_gamma
        for k in range(TAPS):
            gcw_ref[k:k + 1, :] += sums[3 + k]
        gb1_ref[0:1, :] += g_b1

        @pl.when(clip == pl.num_programs(0) - 1)
        def _flush():
            per1 = hidden // LANE
            per2 = width // LANE
            for j in range(per1):
                flat_s[pl.ds(j, width, stride=per1), :] = gw1_s[:, j * LANE:(j + 1) * LANE]
            at = width * hidden // LANE
            for j in range(per2):
                flat_s[pl.ds(at + j, hidden, stride=per2), :] = gw2_s[:, j * LANE:(j + 1) * LANE]
            at = 2 * at
            for q in range(per2):
                flat_s[pl.ds(at + q, TAPS, stride=per2), :] = gcw_ref[0:TAPS, q * LANE:(q + 1) * LANE]
            at = at + TAPS * per2
            for q in range(per2):
                flat_s[pl.ds(at + q, 5, stride=per2), :] = gvec_ref[0:5, q * LANE:(q + 1) * LANE]
            at = at + 5 * per2
            for j in range(per1):
                flat_s[at + j:at + j + 1, :] = gb1_ref[0:1, j * LANE:(j + 1) * LANE]
            at = at + per1
            flat_s[at:, :] = jnp.zeros((flat_rows - at, LANE), F32)
            if split:
                block, cuts = split
                mine = bit_ref[0]
                copies = []
                for s in range(flat_rows // block):
                    side = lax.rem(mine + s % 2, 2)
                    for p in range(len(cuts) - 1):
                        copies.append(pltpu.make_async_copy(
                            flat_s.at[pl.ds(s * block + cuts[p], cuts[p + 1] - cuts[p]), :],
                            g_refs[p].at[side, s // 2], sems.at[2 + len(copies)]))
                for cp in copies:
                    cp.start()
                for cp in copies:
                    cp.wait()
            else:
                out = pltpu.make_async_copy(flat_s, g_refs[0], sems.at[0])
                out.start()
                out.wait()

    return kernel


def fused_block(frames, counts, cotangent, wrows, cw8, vec8, b1_8, flat_rows, my_bit, split=None, rows=256):
    clips, length, width = frames.shape
    hidden = cw8.shape[1] * 3
    kernel = block_kernel(length, width, hidden, rows, flat_rows, split)
    if split:
        block, cuts = split
        half = flat_rows // block // 2
        grad_shapes = [(2, half, cuts[p + 1] - cuts[p], LANE) for p in range(len(cuts) - 1)]
        n_copies = 2 * half * (len(cuts) - 1)
    else:
        grad_shapes = [(flat_rows, LANE)]
        n_copies = 0
    clip_spec = pl.BlockSpec((1, length, width), lambda i, c, m: (i, 0, 0))
    fixed = lambda shape: pl.BlockSpec(shape, lambda i, c, m: (0, 0))
    grid_spec = pltpu.PrefetchScalarGridSpec(
        num_scalar_prefetch=2,
        grid=(clips,),
        in_specs=[clip_spec, clip_spec, pl.BlockSpec(memory_space=pl.ANY),
                  fixed((8, width)), fixed((8, width)), fixed((8, hidden))],
        out_specs=[clip_spec, clip_spec] + [pl.BlockSpec(memory_space=pl.ANY)] * len(grad_shapes)
                  + [fixed((8, width)), fixed((8, width)), fixed((8, hidden))],
        scratch_shapes=[
            pltpu.VMEM(((length + 2 * PAD) * (width // LANE), LANE), F32),
            pltpu.VMEM((length, width), F32),
            pltpu.VMEM((length, 1), F32),
            pltpu.VMEM((length, width), BF16),
            pltpu.VMEM((length, width), F32),
            pltpu.VMEM(((length + 2 * PAD) * (width // LANE), LANE), F32),
            pltpu.VMEM((width, hidden), F32),
            pltpu.VMEM((hidden, width), F32),
            pltpu.VMEM((flat_rows, LANE), F32),
            pltpu.VMEM((2 * width * hidden // LANE, LANE), BF16),
            pltpu.VMEM((width, hidden), BF16),
            pltpu.VMEM((hidden, width), BF16),
            pltpu.SemaphoreType.DMA((2 + n_copies,)),
        ],
    )
    flops = 12 * clips * length * width * hidden
    cost = pl.CostEstimate(flops=flops, transcendentals=2 * clips * length * hidden,
                           bytes_accessed=clips * length * width * 8 + 4 * width * hidden * 4)
    return pl.pallas_call(
        kernel,
        grid_spec=grid_spec,
        out_shape=[
            jax.ShapeDtypeStruct((clips, length, width), BF16),
            jax.ShapeDtypeStruct((clips, length, width), F32),
        ] + [jax.ShapeDtypeStruct(s, F32) for s in grad_shapes] + [
            jax.ShapeDtypeStruct((8, width), F32),
            jax.ShapeDtypeStruct((8, width), F32),
            jax.ShapeDtypeStruct((8, hidden), F32),
        ],
        compiler_params=pltpu.CompilerParams(
            dimension_semantics=("arbitrary",), vmem_limit_bytes=60 * 1024 * 1024),
        cost_estimate=cost,
    )(counts, my_bit, frames, cotangent, wrows, cw8, vec8, b1_8)


def unpack(packed, width, hidden):
    shapes = [(width, hidden), (hidden, width), (TAPS, width), (width,), (width,), (width,), (width,), (width,), (hidden,)]
    pieces = []
    start_at = 0
    for shape in shapes:
        entries = 1
        for extent in shape:
            entries = entries * extent
        pieces.append(packed[start_at : start_at + entries].reshape(shape))
        start_at = start_at + entries
    return (tuple(pieces), start_at)


AXES = ("dp", "fsdp")
LANES = 128


def bit_order(mesh_sizes):
    dp_size, fsdp_size = mesh_sizes
    fsdp_bits = int(math.log2(fsdp_size))
    dp_bits = int(math.log2(dp_size))
    order = [0] + [fsdp_bits + b for b in range(dp_bits)] + list(range(1, fsdp_bits))
    return order, fsdp_bits + dp_bits


def swap_perm(devices, bit):
    return [(i, i ^ (1 << bit)) for i in range(devices)]


def split_orders(order):
    if len(order) < 3:
        return [order]
    other = [order[0], order[2], order[1]] + order[3:]
    return [order, other]


def tree_all_gather(shard, orders, nbits):
    me = lax.axis_index(AXES)
    devices = 1 << nbits
    rows = shard.shape[0]
    cuts = [rows * p // len(orders) for p in range(len(orders) + 1)]
    if rows >= 16 * len(orders):
        cuts = [c // 16 * 16 for c in cuts[:-1]] + [rows]
    held = [shard[cuts[p]:cuts[p + 1]].reshape([1] * nbits + [-1, LANES]) for p in range(len(orders))]
    for step in range(nbits):
        for p, order in enumerate(orders):
            bit = order[step]
            other = lax.ppermute(held[p], AXES, swap_perm(devices, bit))
            upper = ((me >> bit) & 1) == 1
            held[p] = jnp.concatenate(
                [jnp.where(upper, other, held[p]), jnp.where(upper, held[p], other)], axis=nbits - 1 - bit)
    parts = [h.reshape(devices, -1, LANES) for h in held]
    return jnp.concatenate(parts, axis=1).reshape(devices * rows, LANES)


def row_cuts(rows, parts):
    cuts = [rows * p // parts for p in range(parts + 1)]
    if rows % 8 == 0:
        cuts = [c // 8 * 8 for c in cuts]
    return cuts


def halve_steps(held, orders, nbits, first_step):
    me = lax.axis_index(AXES)
    devices = 1 << nbits
    held_bits = [[b for b in range(nbits - 1, -1, -1) if b not in order[:first_step]] for order in orders]
    for step in range(first_step, nbits):
        for p, order in enumerate(orders):
            bit = order[step]
            axis = held_bits[p].index(bit)
            mine = (me >> bit) & 1
            keep = lax.dynamic_index_in_dim(held[p], mine, axis=axis, keepdims=False)
            send = lax.dynamic_index_in_dim(held[p], 1 - mine, axis=axis, keepdims=False)
            held[p] = keep + lax.ppermute(send, AXES, swap_perm(devices, bit))
            held_bits[p].pop(axis)
    return jnp.concatenate(held, axis=0)


def tree_reduce_scatter(full, orders, nbits):
    devices = 1 << nbits
    rows = full.shape[0] // devices
    cuts = row_cuts(rows, len(orders))
    shaped = full.reshape([2] * nbits + [rows, LANES])
    held = [shaped[..., cuts[p]:cuts[p + 1], :] for p in range(len(orders))]
    return halve_steps(held, orders, nbits, 0)


def tree_all_sum(value, order, nbits):
    devices = 1 << nbits
    for bit in reversed(order):
        value = value + lax.ppermute(value, AXES, swap_perm(devices, bit))
    return value


def body(frames, counts, cotangent, master, momentum, average, disc_grads, mesh_sizes=None):
    order, nbits = bit_order(mesh_sizes)
    devices = 1 << nbits
    clips, length, width = frames.shape
    hidden = 3 * width
    rows = clips * length
    local = master.shape[0]
    flat_size = local * devices
    total_frames = jnp.float32(rows * devices)
    rounded = master.astype(BF16).reshape(local // LANES, LANES)
    packed_rows = tree_all_gather(rounded, [o[::-1] for o in split_orders(order)], nbits)
    weight_rows = 2 * width * hidden // LANES
    small_rows = -(-(TAPS * width + 5 * width + hidden) // LANES)
    small = packed_rows[weight_rows:weight_rows + small_rows].reshape(-1)
    conv_w = small[: TAPS * width].reshape(TAPS, width)
    at = TAPS * width
    conv_b, ln_g, ln_b, b_two, gamma = [small[at + i * width: at + (i + 1) * width] for i in range(5)]
    at = at + 5 * width
    b_one = small[at: at + hidden]
    cw8 = jnp.zeros((8, width), F32).at[:TAPS].set(conv_w.astype(F32))
    vec8 = jnp.concatenate(
        [jnp.stack([conv_b, ln_g, ln_b, b_two, gamma]).astype(F32), jnp.zeros((3, width), F32)])
    b1_8 = jnp.zeros((8, hidden), F32).at[0].set(b_one.astype(F32))
    shard_rows = local // LANES
    padded_rows = -(-shard_rows // 8) * 8
    aligned = padded_rows != shard_rows and (padded_rows - shard_rows) * (devices - 1) <= padded_rows
    block = padded_rows if aligned else shard_rows
    orders = split_orders(order)
    my_bit = (lax.axis_index(AXES) & 1).astype(jnp.int32).reshape(1)
    if aligned and order[0] == 0 and all(o[0] == 0 for o in orders):
        cuts = row_cuts(block, len(orders))
        outs = fused_block(frames, counts, cotangent, packed_rows, cw8, vec8, b1_8, devices * block, my_bit,
                           split=(block, tuple(cuts)))
        block_out, input_grad = outs[0], outs[1]
        held = []
        for p in range(len(orders)):
            halves = outs[2 + p]
            got = lax.ppermute(halves[1], AXES, swap_perm(devices, 0))
            held.append((halves[0] + got).reshape([2] * (nbits - 1) + [cuts[p + 1] - cuts[p], LANES]))
        grad_block = halve_steps(held, orders, nbits, 1)
    else:
        block_out, input_grad, grad_full, _, _, _ = fused_block(
            frames, counts, cotangent, packed_rows, cw8, vec8, b1_8, devices * block, my_bit)
        grad_block = tree_reduce_scatter(grad_full, orders, nbits)
    if aligned:
        me = lax.axis_index(AXES)
        prev = lax.ppermute(grad_block, AXES, [(i, (i + 1) % devices) for i in range(devices)])
        both = jnp.concatenate([prev, grad_block])
        grad_shard = lax.dynamic_slice_in_dim(both, block - (block - shard_rows) * me, shard_rows, axis=0)
    else:
        grad_shard = grad_block
    disc_rows = jnp.sum((disc_grads * disc_grads).reshape(-1, LANES), axis=0, keepdims=True)
    own_rows = jnp.sum(grad_block * grad_block, axis=0, keepdims=True)
    squares = jnp.broadcast_to(own_rows + disc_rows, (8, LANES))
    squares = tree_all_sum(squares, order, nbits)
    grad_norm = jnp.sqrt(jnp.sum(squares[0]))
    grad_shard = grad_shard.reshape(-1)
    clipped = grad_shard * jnp.minimum(1.0, 20.0 * jnp.sqrt(total_frames) / (grad_norm + 1e-06))
    new_momentum = 0.9 * momentum + clipped
    new_master = master - (clipped + 0.9 * new_momentum) / jnp.sqrt(total_frames)
    new_average = 0.99 * average + 0.01 * new_master
    return (
        block_out,
        input_grad,
        grad_norm,
        new_master,
        new_momentum,
        new_average,
        new_master.astype(BF16),
        new_average.astype(BF16),
    )


def solution(mesh):
    clip_spec = P(("dp", "fsdp"), None, None)
    flat_spec = P(("dp", "fsdp"))
    mesh_sizes = (mesh.shape["dp"], mesh.shape["fsdp"])
    return jax.shard_map(
        functools.partial(body, mesh_sizes=mesh_sizes),
        mesh=mesh,
        in_specs=(clip_spec, flat_spec, clip_spec, flat_spec, flat_spec, flat_spec, flat_spec),
        out_specs=(clip_spec, clip_spec, P(), flat_spec, flat_spec, flat_spec, flat_spec, flat_spec),
        check_vma=False,
    )
```
